32 devices in a mesh: ox: 8 (over z, x), oy: 4 (over y, core).
Axes of the slice: x: 2, y: 2, z: 4, core: 2. Of those that a mesh axis runs over, the one named last changes fastest.
Arguments:
- atm_flux: bfloat16 [4, 40, 1024], P(None, 'oy', 'ox'), may hold values from -6 to 6
- remap_weights: bfloat16 [128, 12, 128, 128], P('ox', 'oy'), may hold values from -0.3125 to 0.3125
- tile_slots: int32 [128, 12], P('ox', 'oy'), may hold values from 0 to 23, as said below
- need_blocks: int32 [64, 12], P('ox', 'oy'), may hold values from -1 to 9, as said below
- send_blocks: int32 [64, 12], P('ox', 'oy'), may hold values from -1 to 9, as said below
- ocean_state: float32 [4, 16, 128, 512], P(None, None, 'ox', 'oy'), may hold values from -6 to 6
- land_mask: int32 [128, 512], P('ox', 'oy'), may hold values 0 or 1
- diffusivity: float32 [16], replicated, may hold values from 0.02 to 0.2
Outputs:
- ocean_final: float32 [4, 16, 128, 512], P(None, None, 'ox', 'oy')
- atmos_surface: float32 [40, 1024], P('oy', 'ox')
The draws below stay inside these ranges and needn't reach their ends.
Inputs may be any that keep to these rules, and one draw needn't show every extreme that they name: `tile_slots`: entry [x, j * 3 + k] is q * 3 + s: the s-th block that owner q sends the ocean device of row x and latitude group j, with s below the number of blocks that owner sends it. `need_blocks`: entry [i * 8 + q, j * 3 + s] is the local block of owner (q, j) that ocean device (i, j) takes in place s, or -1; the first 1 to 3 places hold distinct blocks and the rest -1; every ocean device takes 3 blocks from some owner, and some device takes 3 from every owner. `send_blocks`: entry [q * 8 + i, j * 3 + s] equals need_blocks[i * 8 + q, j * 3 + s].
All inputs are finite; a program needn't handle non-finite values. No bound on the sum of `land_mask` on one device may be relied on, other than what follows from the above.
Results may differ from the reference program's by a relative error of at most 0.0022.
Values may be sent and summed in bfloat16 or wider, within the bound.
No kernel may reach another device: no remote copies, remote signals or barrier semaphores. Data moves between devices by JAX's collectives and lax.ppermute only.
A program may use at most 64 MiB of HBM per device.

```python
import math
import jax
import jax.numpy as jnp
from jax import lax

CX = 16
CY = 128
LEV = 16
STEPS = 3
FLUX = 4
AB = 128
ABLK = 10
KB = 3
CAP = 3
NX = 128
NY = 512
N_OX = 8
N_OY = 4


def owner_tables(key):
    base = jax.random.fold_in(key, 11)
    keys = jax.random.split(base, 7)
    counts = jax.random.randint(keys[0], (N_OX, N_OX, N_OY), 1, CAP + 1)
    chosen = jax.random.randint(keys[1], (N_OX, 1, N_OY), 0, N_OX)
    owner_line = jnp.arange(N_OX, dtype=jnp.int32)[None, :, None]
    counts = jnp.where(owner_line == chosen, CAP, counts)
    full_recv = jax.random.randint(keys[2], (), 0, N_OX)
    full_group = jax.random.randint(keys[3], (), 0, N_OY)
    recv_line = jnp.arange(N_OX, dtype=jnp.int32)[:, None, None]
    group_line = jnp.arange(N_OY, dtype=jnp.int32)[None, None, :]
    counts = jnp.where((recv_line == full_recv) & (group_line == full_group), CAP, counts)
    scores = jax.random.randint(keys[4], (N_OX, N_OX, N_OY, ABLK), 0, 2 ** 20) * ABLK + jnp.arange(ABLK, dtype=jnp.int32)
    order = jnp.argsort(scores, axis=-1, stable=True).astype(jnp.int32)[..., :CAP]
    places = jnp.arange(CAP, dtype=jnp.int32)
    blocks = jnp.where(places < counts[..., None], order, -1).astype(jnp.int32)
    need = blocks.reshape(N_OX * N_OX, N_OY * CAP)
    send = jnp.transpose(blocks, (1, 0, 2, 3)).reshape(N_OX * N_OX, N_OY * CAP)
    owner_pick = jax.random.randint(keys[5], (N_OX, CX, N_OY, KB), 0, N_OX)
    recv_full = jnp.arange(N_OX, dtype=jnp.int32)[:, None, None, None]
    group_full = jnp.arange(N_OY, dtype=jnp.int32)[None, None, :, None]
    live = counts[recv_full, owner_pick, group_full]
    place_pick = jax.random.randint(keys[6], (N_OX, CX, N_OY, KB), 0, 2 ** 20) % live
    slots = owner_pick * CAP + place_pick
    row_line = jnp.arange(CX, dtype=jnp.int32)[None, :, None, None]
    ref_line = jnp.arange(KB, dtype=jnp.int32)[None, None, None, :]
    corner = (recv_full == full_recv) & (group_full == full_group) & (row_line == 0) & (ref_line == 0)
    slots = jnp.where(corner, N_OX * CAP - 1, slots).astype(jnp.int32)
    return (slots.reshape(N_OX * CX, N_OY * KB), need, send)


def draw_tile_slots(key, part):
    return owner_tables(key)[0]


def draw_need_blocks(key, part):
    return owner_tables(key)[1]


def draw_send_blocks(key, part):
    return owner_tables(key)[2]


def set_ends(result, stream_key, least, high):
    longest = result.shape.index(max(result.shape))
    spots = []
    for shift in (0, 1):
        where = [jax.random.randint(jax.random.fold_in(stream_key, axis), (), 0, length) for axis, length in enumerate(result.shape)]
        where[longest] = (where[longest] + shift) % result.shape[longest]
        spots.append(tuple(where))
    return result.at[spots[0]].set(least).at[spots[1]].set(high)


def steps_of(key, extent, cuts, least, top_value):
    level, own = 1.0, jax.random.fold_in(key, 6)
    for axis_at, parts in cuts:
        draws = jnp.exp(jax.random.uniform(jax.random.fold_in(own, axis_at), (parts,), jnp.float32, least / len(cuts), top_value / len(cuts)))
        level = level * jnp.repeat(draws, extent[axis_at] // parts).reshape([-1 if axis == axis_at else 1 for axis in range(len(extent))])
    return level


def gaussian(stream_key, shape, scale, bound, cuts=(), kind=jnp.bfloat16):
    factor_of = steps_of(stream_key, shape, cuts, -0.22, 0.18) if cuts else 1.0
    array = jax.random.normal(stream_key, shape, jnp.float32) * scale * factor_of
    return jnp.minimum(jnp.maximum(array, -bound), bound).astype(kind)


def setup_inputs(seed: int = 0) -> dict:
    streams_of = jax.random.split(jax.random.key(seed), 9)
    atm_flux = gaussian(streams_of[0], (FLUX, N_OY * ABLK, N_OX * AB), 1.0, 6.0, ((1, 4), (2, 8)))
    remap_weights = gaussian(streams_of[1], (NX, N_OY * KB, CY, AB), (KB * AB) ** -0.5, 0.3125, ((0, 8), (1, 4)))
    tile_slots = draw_tile_slots(jax.random.fold_in(streams_of[8], 71), 0)
    need_blocks = draw_need_blocks(jax.random.fold_in(streams_of[8], 71), 0)
    send_blocks = draw_send_blocks(jax.random.fold_in(streams_of[8], 71), 0)
    ocean_state = gaussian(streams_of[5], (4, LEV, NX, NY), 1.0, 6.0, ((2, 8), (3, 4)), jnp.float32)
    land_mask = set_ends((jax.random.randint(streams_of[6], (NX, NY), 0, 4) < 3).astype(jnp.int32), jax.random.fold_in(streams_of[6], 1), 0, 1)
    diffusivity = jnp.clip(jnp.exp(jax.random.uniform(streams_of[7], (LEV,), jnp.float32, math.log(0.02), math.log(0.2))), 0.02, 0.2)
    return dict(atm_flux=atm_flux, remap_weights=remap_weights, tile_slots=tile_slots, need_blocks=need_blocks, send_blocks=send_blocks, ocean_state=ocean_state, land_mask=land_mask, diffusivity=diffusivity)


advect_coef = 0.25
pressure_coef = 0.1
thermal_coef = 0.2
haline_coef = 0.8
coriolis_coef = 0.5
vertical_coef = 0.1
forcing_coef = 0.5


def advance(padded, center, diffusivity, coriolis, forcing, wetness):
    east = padded[:, :, 2:, 1:-1]
    west = padded[:, :, :-2, 1:-1]
    north = padded[:, :, 1:-1, 2:]
    south = padded[:, :, 1:-1, :-2]
    zonal = center[0]
    meridional = center[1]
    advection = -advect_coef * 0.5 * (zonal[None] * (east - west) + meridional[None] * (north - south))
    laplace = diffusivity[None, :, None, None] * (east + west + north + south - 4.0 * center)
    upper = jnp.concatenate([center[:, :1], center[:, :-1]], axis=1)
    lower = jnp.concatenate([center[:, 1:], center[:, -1:]], axis=1)
    mixing = vertical_coef * (upper + lower - 2.0 * center)
    density = haline_coef * padded[3] - thermal_coef * padded[2]
    pressure = jnp.cumsum(density, axis=0) - 0.5 * density
    grad_east = pressure[:, 2:, 1:-1] - pressure[:, :-2, 1:-1]
    grad_north = pressure[:, 1:-1, 2:] - pressure[:, 1:-1, :-2]
    zonal_push = coriolis * meridional - pressure_coef * 0.5 * grad_east
    merid_push = -coriolis * zonal - pressure_coef * 0.5 * grad_north
    tracer_zero = jnp.zeros((2,) + zonal.shape, jnp.float32)
    momentum = jnp.concatenate([zonal_push[None], merid_push[None], tracer_zero], axis=0)
    total = advection + laplace + mixing + momentum
    total = total.at[:, 0].add(forcing_coef * forcing)
    return center + wetness * total


def reference(atm_flux, remap_weights, tile_slots, need_blocks, send_blocks, ocean_state, land_mask, diffusivity):
    slots = tile_slots.reshape(N_OX, CX, N_OY, KB)
    owner_of = slots // CAP
    place_of = slots % CAP
    recv_idx = jnp.arange(N_OX, dtype=jnp.int32)[:, None, None, None]
    group_idx = jnp.arange(N_OY, dtype=jnp.int32)[None, None, :, None]
    needed = need_blocks.reshape(N_OX, N_OX, N_OY, CAP)
    in_block = needed[recv_idx, owner_of, group_idx, place_of]
    given = send_blocks.reshape(N_OX, N_OX, N_OY, CAP)
    back_block = given[owner_of, recv_idx, group_idx, place_of]
    atmos = atm_flux.reshape(FLUX, N_OY, ABLK, N_OX, AB)
    weights = remap_weights.reshape(N_OX, CX, N_OY, KB, CY, AB)
    group_row = jnp.arange(N_OY, dtype=jnp.int32)[None, :, None]

    def remap_in(index):
        picks = atmos[:, group_row, in_block[index], owner_of[index], :]
        block_w = weights[index].astype(jnp.float32)
        return jnp.einsum("fxjka,xjkra->fxjr", picks.astype(jnp.float32), block_w)

    forcing_all = lax.map(remap_in, jnp.arange(N_OX, dtype=jnp.int32))
    forcing = jnp.transpose(forcing_all, (1, 0, 2, 3, 4)).reshape(FLUX, NX, NY)

    latitude = jnp.arange(NY, dtype=jnp.int32).astype(jnp.float32)
    coriolis = coriolis_coef * (2.0 * (latitude + 0.5) / NY - 1.0)
    wetness = land_mask.astype(jnp.float32)
    state = ocean_state
    for repeat in range(STEPS):
        padded = jnp.pad(state, ((0, 0), (0, 0), (1, 1), (1, 1)))
        state = advance(padded, state, diffusivity, coriolis, forcing, wetness)

    surface = state[2, 0].astype(jnp.bfloat16).reshape(N_OX, CX, N_OY, CY)

    def remap_out(index):
        block_w = weights[index].astype(jnp.float32)
        return jnp.einsum("xjkra,xjr->xjka", block_w, surface[index].astype(jnp.float32))

    pieces = lax.map(remap_out, jnp.arange(N_OX, dtype=jnp.int32))
    group_full = jnp.broadcast_to(group_idx, back_block.shape)
    accum = jnp.zeros((N_OY, ABLK, N_OX, AB), jnp.float32)
    accum = accum.at[group_full, back_block, owner_of].add(pieces)
    return state, accum.reshape(N_OY * ABLK, N_OX * AB)
```

```python
import jax
import jax.numpy as jnp
from jax import lax
from jax.sharding import PartitionSpec as P

STEPS = 3


advect_coef = 0.25
pressure_coef = 0.1
thermal_coef = 0.2
haline_coef = 0.8
coriolis_coef = 0.5
vertical_coef = 0.1
forcing_coef = 0.5


def with_halo(block, sides, width):
    for axis, dim in sides:
        count = lax.axis_size(axis)
        forward = [(i, i + 1) for i in range(count - 1)]
        backward = [(target, source) for source, target in forward]
        low = lax.ppermute(
            lax.slice_in_dim(block, block.shape[dim] - width, None, axis=dim), axis, forward
        )
        high = lax.ppermute(lax.slice_in_dim(block, 0, width, axis=dim), axis, backward)
        block = jnp.concatenate([low, block, high], axis=dim)
    return block


def advance(padded, center, diffusivity, coriolis, forcing, wetness):
    east = padded[:, :, 2:, 1:-1]
    west = padded[:, :, :-2, 1:-1]
    north = padded[:, :, 1:-1, 2:]
    south = padded[:, :, 1:-1, :-2]
    zonal = center[0]
    meridional = center[1]
    advection = (
        -advect_coef * 0.5 * (zonal[None] * (east - west) + meridional[None] * (north - south))
    )
    laplace = diffusivity[None, :, None, None] * (east + west + north + south - 4.0 * center)
    upper = jnp.concatenate([center[:, :1], center[:, :-1]], axis=1)
    lower = jnp.concatenate([center[:, 1:], center[:, -1:]], axis=1)
    mixing = vertical_coef * (upper + lower - 2.0 * center)
    density = haline_coef * padded[3] - thermal_coef * padded[2]
    pressure = jnp.cumsum(density, axis=0) - 0.5 * density
    grad_east = pressure[:, 2:, 1:-1] - pressure[:, :-2, 1:-1]
    grad_north = pressure[:, 1:-1, 2:] - pressure[:, 1:-1, :-2]
    zonal_push = coriolis * meridional - pressure_coef * 0.5 * grad_east
    merid_push = -coriolis * zonal - pressure_coef * 0.5 * grad_north
    tracer_zero = jnp.zeros((2,) + zonal.shape, jnp.float32)
    momentum = jnp.concatenate([zonal_push[None], merid_push[None], tracer_zero], axis=0)
    total = advection + laplace + mixing + momentum
    total = total.at[:, 0].add(forcing_coef * forcing)
    return center + wetness * total


def row_targets(tile_slots, need_blocks, capacity, owners):
    owner_of = tile_slots // capacity
    place_of = tile_slots % capacity
    return need_blocks[owner_of, place_of] * owners + owner_of


def lat_factor(first_cell, count, lat_total):
    latitude = (first_cell + jnp.arange(count, dtype=jnp.int32)).astype(jnp.float32)
    return coriolis_coef * (2.0 * (latitude + 0.5) / lat_total - 1.0)


def per_device(
    atm_flux,
    remap_weights,
    tile_slots,
    need_blocks,
    send_blocks,
    ocean_state,
    land_mask,
    diffusivity,
):
    blocks_here = atm_flux.shape[1]
    block_width = atm_flux.shape[2]
    owners = lax.axis_size("ox")
    capacity = send_blocks.shape[1]
    slots = owners * capacity
    given = jnp.clip(send_blocks, 0, blocks_here - 1)
    outgoing = jnp.transpose(atm_flux[:, given, :], (1, 2, 0, 3))
    incoming = lax.all_to_all(outgoing, "ox", 0, 0, tiled=True)
    incoming = incoming.reshape((slots,) + incoming.shape[2:])
    picks = incoming[tile_slots]
    forcing = jnp.einsum("tkfa,tkra->ftr", picks, remap_weights, preferred_element_type=jnp.float32)
    lat_cells = ocean_state.shape[3]
    lat_total = lat_cells * lax.axis_size("oy")
    lat_start = lax.axis_index("oy") * lat_cells
    wetness = land_mask.astype(jnp.float32)
    state = ocean_state
    coriolis = lat_factor(lat_start, lat_cells, lat_total)
    for repeat in range(STEPS):
        padded = with_halo(state, (("ox", 2), ("oy", 3)), 1)
        state = advance(padded, state, diffusivity, coriolis, forcing, wetness)
    surface = state[2, 0].astype(jnp.bfloat16)
    pieces = jnp.einsum("tkra,tr->tka", remap_weights, surface, preferred_element_type=jnp.float32)
    slot_line = jnp.arange(slots, dtype=jnp.int32)
    to_slot = (tile_slots[:, :, None] == slot_line[None, None, :]).astype(jnp.float32)
    per_slot = jnp.einsum("tks,tka->sa", to_slot, pieces, precision=lax.Precision.HIGHEST)
    per_slot = per_slot.reshape(owners, capacity, block_width)
    returned = lax.all_to_all(per_slot, "ox", 0, 0, tiled=True)
    block_line = jnp.arange(blocks_here, dtype=jnp.int32)
    to_block = (send_blocks[:, :, None] == block_line[None, None, :]).astype(jnp.float32)
    atmos_surface = jnp.einsum(
        "isb,isa->ba", to_block, returned, precision=lax.Precision.HIGHEST
    )
    return (state, atmos_surface)


def solution(mesh):
    return jax.shard_map(
        per_device,
        mesh=mesh,
        in_specs=(
            P(None, "oy", "ox"),
            P("ox", "oy", None, None),
            P("ox", "oy"),
            P("ox", "oy"),
            P("ox", "oy"),
            P(None, None, "ox", "oy"),
            P("ox", "oy"),
            P(),
        ),
        out_specs=(P(None, None, "ox", "oy"), P("oy", "ox")),
        check_vma=False,
    )
```

```python
import jax
import jax.numpy as jnp
from jax import lax
from jax.sharding import PartitionSpec as P

STEPS = 3


advect_coef = 0.25
pressure_coef = 0.1
thermal_coef = 0.2
haline_coef = 0.8
coriolis_coef = 0.5
vertical_coef = 0.1
forcing_coef = 0.5


def with_halo(block, sides, width):
    for axis, dim in sides:
        count = lax.axis_size(axis)
        forward = [(i, i + 1) for i in range(count - 1)]
        backward = [(target, source) for source, target in forward]
        low = lax.ppermute(
            lax.slice_in_dim(block, block.shape[dim] - width, None, axis=dim), axis, forward
        )
        high = lax.ppermute(lax.slice_in_dim(block, 0, width, axis=dim), axis, backward)
        block = jnp.concatenate([low, block, high], axis=dim)
    return block


def advance(padded, center, diffusivity, coriolis, forcing, wetness):
    east = padded[:, :, 2:, 1:-1]
    west = padded[:, :, :-2, 1:-1]
    north = padded[:, :, 1:-1, 2:]
    south = padded[:, :, 1:-1, :-2]
    zonal = center[0]
    meridional = center[1]
    advection = (
        -advect_coef * 0.5 * (zonal[None] * (east - west) + meridional[None] * (north - south))
    )
    laplace = diffusivity[None, :, None, None] * (east + west + north + south - 4.0 * center)
    upper = jnp.concatenate([center[:, :1], center[:, :-1]], axis=1)
    lower = jnp.concatenate([center[:, 1:], center[:, -1:]], axis=1)
    mixing = vertical_coef * (upper + lower - 2.0 * center)
    density = haline_coef * padded[3] - thermal_coef * padded[2]
    pressure = jnp.cumsum(density, axis=0) - 0.5 * density
    grad_east = pressure[:, 2:, 1:-1] - pressure[:, :-2, 1:-1]
    grad_north = pressure[:, 1:-1, 2:] - pressure[:, 1:-1, :-2]
    zonal_push = coriolis * meridional - pressure_coef * 0.5 * grad_east
    merid_push = -coriolis * zonal - pressure_coef * 0.5 * grad_north
    tracer_zero = jnp.zeros((2,) + zonal.shape, jnp.float32)
    momentum = jnp.concatenate([zonal_push[None], merid_push[None], tracer_zero], axis=0)
    total = advection + laplace + mixing + momentum
    total = total.at[:, 0].add(forcing_coef * forcing)
    return center + wetness * total


def row_targets(tile_slots, need_blocks, capacity, owners):
    owner_of = tile_slots // capacity
    place_of = tile_slots % capacity
    return need_blocks[owner_of, place_of] * owners + owner_of


def lat_factor(first_cell, count, lat_total):
    latitude = (first_cell + jnp.arange(count, dtype=jnp.int32)).astype(jnp.float32)
    return coriolis_coef * (2.0 * (latitude + 0.5) / lat_total - 1.0)


def per_device(
    atm_flux,
    remap_weights,
    tile_slots,
    need_blocks,
    send_blocks,
    ocean_state,
    land_mask,
    diffusivity,
):
    blocks_here = atm_flux.shape[1]
    block_width = atm_flux.shape[2]
    owners = lax.axis_size("ox")
    capacity = send_blocks.shape[1]
    slots = owners * capacity
    given = jnp.clip(send_blocks, 0, blocks_here - 1)
    outgoing = jnp.transpose(atm_flux[:, given, :], (1, 2, 0, 3))
    incoming = lax.all_to_all(outgoing, "ox", 0, 0, tiled=True)
    incoming = incoming.reshape((slots,) + incoming.shape[2:])
    picks = incoming[tile_slots]
    forcing = jnp.einsum("tkfa,tkra->ftr", picks, remap_weights, preferred_element_type=jnp.float32)
    fields, levels, rows, lat_cells = ocean_state.shape
    lat_total = lat_cells * lax.axis_size("oy")
    lat_start = lax.axis_index("oy") * lat_cells
    wetness = land_mask.astype(jnp.float32)
    packed = jnp.concatenate(
        [ocean_state.reshape(fields * levels, rows, lat_cells), forcing, wetness[None]], axis=0
    )
    packed = with_halo(packed, (("ox", 1), ("oy", 2)), STEPS)
    state = packed[: fields * levels].reshape(fields, levels, rows + 2 * STEPS, lat_cells + 2 * STEPS)
    forcing_wide = packed[fields * levels : fields * levels + fields]
    wetness_wide = packed[fields * levels + fields]
    coriolis_wide = lat_factor(lat_start - STEPS, lat_cells + 2 * STEPS, lat_total)
    for repeat in range(STEPS):
        lo = repeat + 1
        hi_x = rows + 2 * STEPS - lo
        hi_y = lat_cells + 2 * STEPS - lo
        state = advance(
            state,
            state[:, :, 1:-1, 1:-1],
            diffusivity,
            coriolis_wide[lo:hi_y],
            forcing_wide[:, lo:hi_x, lo:hi_y],
            wetness_wide[lo:hi_x, lo:hi_y],
        )
    surface = state[2, 0].astype(jnp.bfloat16)
    pieces = jnp.einsum("tkra,tr->tka", remap_weights, surface, preferred_element_type=jnp.float32)
    slot_line = jnp.arange(slots, dtype=jnp.int32)
    to_slot = (tile_slots[:, :, None] == slot_line[None, None, :]).astype(jnp.float32)
    per_slot = jnp.einsum("tks,tka->sa", to_slot, pieces, precision=lax.Precision.HIGHEST)
    per_slot = per_slot.reshape(owners, capacity, block_width)
    returned = lax.all_to_all(per_slot, "ox", 0, 0, tiled=True)
    block_line = jnp.arange(blocks_here, dtype=jnp.int32)
    to_block = (send_blocks[:, :, None] == block_line[None, None, :]).astype(jnp.float32)
    atmos_surface = jnp.einsum(
        "isb,isa->ba", to_block, returned, precision=lax.Precision.HIGHEST
    )
    return (state, atmos_surface)


def solution(mesh):
    return jax.shard_map(
        per_device,
        mesh=mesh,
        in_specs=(
            P(None, "oy", "ox"),
            P("ox", "oy", None, None),
            P("ox", "oy"),
            P("ox", "oy"),
            P("ox", "oy"),
            P(None, None, "ox", "oy"),
            P("ox", "oy"),
            P(),
        ),
        out_specs=(P(None, None, "ox", "oy"), P("oy", "ox")),
        check_vma=False,
    )
```

```python
import jax
import jax.numpy as jnp
from jax import lax
from jax.experimental import pallas as pl
from jax.experimental.pallas import tpu as pltpu
from jax.sharding import PartitionSpec as P

STEPS = 3


advect_coef = 0.25
pressure_coef = 0.1
thermal_coef = 0.2
haline_coef = 0.8
coriolis_coef = 0.5
vertical_coef = 0.1
forcing_coef = 0.5


def with_halo(block, sides, width):
    for axis, dim in sides:
        count = lax.axis_size(axis)
        forward = [(i, i + 1) for i in range(count - 1)]
        backward = [(target, source) for source, target in forward]
        low = lax.ppermute(
            lax.slice_in_dim(block, block.shape[dim] - width, None, axis=dim), axis, forward
        )
        high = lax.ppermute(lax.slice_in_dim(block, 0, width, axis=dim), axis, backward)
        block = jnp.concatenate([low, block, high], axis=dim)
    return block


def advance(padded, center, diffusivity, coriolis, forcing, wetness):
    east = padded[:, :, 2:, 1:-1]
    west = padded[:, :, :-2, 1:-1]
    north = padded[:, :, 1:-1, 2:]
    south = padded[:, :, 1:-1, :-2]
    zonal = center[0]
    meridional = center[1]
    advection = (
        -advect_coef * 0.5 * (zonal[None] * (east - west) + meridional[None] * (north - south))
    )
    laplace = diffusivity[None, :, None, None] * (east + west + north + south - 4.0 * center)
    upper = jnp.concatenate([center[:, :1], center[:, :-1]], axis=1)
    lower = jnp.concatenate([center[:, 1:], center[:, -1:]], axis=1)
    mixing = vertical_coef * (upper + lower - 2.0 * center)
    density = haline_coef * padded[3] - thermal_coef * padded[2]
    pressure = jnp.cumsum(density, axis=0) - 0.5 * density
    grad_east = pressure[:, 2:, 1:-1] - pressure[:, :-2, 1:-1]
    grad_north = pressure[:, 1:-1, 2:] - pressure[:, 1:-1, :-2]
    zonal_push = coriolis * meridional - pressure_coef * 0.5 * grad_east
    merid_push = -coriolis * zonal - pressure_coef * 0.5 * grad_north
    tracer_zero = jnp.zeros((2,) + zonal.shape, jnp.float32)
    momentum = jnp.concatenate([zonal_push[None], merid_push[None], tracer_zero], axis=0)
    total = advection + laplace + mixing + momentum
    total = total.at[:, 0].add(forcing_coef * forcing)
    return center + wetness * total


def stencil_kernel(diff_ref, cor_ref, src_ref, out_ref, first, second):
    fields, levels, rows, lanes = out_ref.shape
    channels = fields * levels
    tall, wide = src_ref.shape[1], src_ref.shape[2]

    def one_step(read, write):
        def level(l, cum):
            up = jnp.maximum(l - 1, 0)
            down = jnp.minimum(l + 1, levels - 1)
            here = [read(f * levels + l) for f in range(fields)]
            density = haline_coef * here[3] - thermal_coef * here[2]
            cum = cum + density
            pressure = cum - 0.5 * density
            zonal = here[0]
            meridional = here[1]
            top = jnp.where(l == 0, forcing_coef, 0.0)
            diff = diff_ref[l]
            coriolis = cor_ref[...]
            for f in range(fields):
                center = here[f]
                east = pltpu.roll(center, tall - 1, 0)
                west = pltpu.roll(center, 1, 0)
                north = pltpu.roll(center, wide - 1, 1)
                south = pltpu.roll(center, 1, 1)
                advection = -advect_coef * 0.5 * (zonal * (east - west) + meridional * (north - south))
                laplace = diff * (east + west + north + south - 4.0 * center)
                mixing = vertical_coef * (
                    read(f * levels + up) + read(f * levels + down) - 2.0 * center
                )
                total = advection + laplace + mixing
                if f == 0:
                    grad = pltpu.roll(pressure, tall - 1, 0) - pltpu.roll(pressure, 1, 0)
                    total = total + (coriolis * meridional - pressure_coef * 0.5 * grad)
                if f == 1:
                    grad = pltpu.roll(pressure, wide - 1, 1) - pltpu.roll(pressure, 1, 1)
                    total = total + (-coriolis * zonal - pressure_coef * 0.5 * grad)
                total = total + top * src_ref[channels + f]
                write(f, l, center + src_ref[channels + fields] * total)
            return cum

        lax.fori_loop(0, levels, level, jnp.zeros((tall, wide), jnp.float32))

    def read_src(ch):
        return src_ref[ch]

    def read_first(ch):
        return first[ch]

    def read_second(ch):
        return second[ch]

    def write_first(f, l, value):
        first[f * levels + l] = value

    def write_second(f, l, value):
        second[f * levels + l] = value

    def write_out(f, l, value):
        out_ref[f, l] = value[:rows, :lanes]

    writers = [write_first, write_second]
    for repeat in range(STEPS):
        write = write_out if repeat == STEPS - 1 else writers[repeat % 2]
        read = read_src if repeat == 0 else (read_first if repeat % 2 == 1 else read_second)
        one_step(read, write)


def cyclic_halo(block, axis, dim, width, total):
    count = lax.axis_size(axis)
    forward = [(i, i + 1) for i in range(count - 1)]
    backward = [(target, source) for source, target in forward]
    size = block.shape[dim]
    low = lax.ppermute(lax.slice_in_dim(block, size - width, None, axis=dim), axis, forward)
    high = lax.ppermute(lax.slice_in_dim(block, 0, width, axis=dim), axis, backward)
    gap_shape = list(block.shape)
    gap_shape[dim] = total - size - 2 * width
    gap = jnp.zeros(gap_shape, block.dtype)
    return jnp.concatenate([block, high, gap, low], axis=dim)


def run_steps(packed, coriolis, diffusivity, out_shape):
    fields, levels = out_shape[0], out_shape[1]
    channels = fields * levels
    tall, wide = packed.shape[1], packed.shape[2]
    return pl.pallas_call(
        stencil_kernel,
        out_shape=jax.ShapeDtypeStruct(out_shape, jnp.float32),
        in_specs=[
            pl.BlockSpec(memory_space=pltpu.SMEM),
            pl.BlockSpec(memory_space=pltpu.VMEM),
            pl.BlockSpec(memory_space=pltpu.VMEM),
        ],
        out_specs=pl.BlockSpec(memory_space=pltpu.VMEM),
        scratch_shapes=[
            pltpu.VMEM((channels, tall, wide), jnp.float32),
            pltpu.VMEM((channels, tall, wide), jnp.float32),
        ],
    )(diffusivity, coriolis, packed)


def row_targets(tile_slots, need_blocks, capacity, owners):
    owner_of = tile_slots // capacity
    place_of = tile_slots % capacity
    return need_blocks[owner_of, place_of] * owners + owner_of


def lat_factor(first_cell, count, lat_total):
    latitude = (first_cell + jnp.arange(count, dtype=jnp.int32)).astype(jnp.float32)
    return coriolis_coef * (2.0 * (latitude + 0.5) / lat_total - 1.0)


def per_device(
    atm_flux,
    remap_weights,
    tile_slots,
    need_blocks,
    send_blocks,
    ocean_state,
    land_mask,
    diffusivity,
):
    blocks_here = atm_flux.shape[1]
    block_width = atm_flux.shape[2]
    owners = lax.axis_size("ox")
    capacity = send_blocks.shape[1]
    slots = owners * capacity
    given = jnp.clip(send_blocks, 0, blocks_here - 1)
    outgoing = jnp.transpose(atm_flux[:, given, :], (1, 2, 0, 3))
    incoming = lax.all_to_all(outgoing, "ox", 0, 0, tiled=True)
    incoming = incoming.reshape((slots,) + incoming.shape[2:])
    picks = incoming[tile_slots]
    forcing = jnp.einsum("tkfa,tkra->ftr", picks, remap_weights, preferred_element_type=jnp.float32)
    fields, levels, rows, lat_cells = ocean_state.shape
    lat_total = lat_cells * lax.axis_size("oy")
    lat_start = lax.axis_index("oy") * lat_cells
    wetness = land_mask.astype(jnp.float32)
    packed = jnp.concatenate(
        [ocean_state.reshape(fields * levels, rows, lat_cells), forcing, wetness[None]], axis=0
    )
    tall = -(-(rows + 2 * STEPS) // 8) * 8
    wide = -(-(lat_cells + 2 * STEPS) // 128) * 128
    packed = cyclic_halo(packed, "ox", 1, STEPS, tall)
    packed = cyclic_halo(packed, "oy", 2, STEPS, wide)
    lane = jnp.arange(wide, dtype=jnp.int32)
    offset = jnp.where(lane < lat_cells + STEPS, lane, lane - wide)
    latitude = (lat_start + offset).astype(jnp.float32)
    coriolis_wide = (coriolis_coef * (2.0 * (latitude + 0.5) / lat_total - 1.0))[None, :]
    state = run_steps(packed, coriolis_wide, diffusivity, ocean_state.shape)
    surface = state[2, 0].astype(jnp.bfloat16)
    pieces = jnp.einsum("tkra,tr->tka", remap_weights, surface, preferred_element_type=jnp.float32)
    slot_line = jnp.arange(slots, dtype=jnp.int32)
    to_slot = (tile_slots[:, :, None] == slot_line[None, None, :]).astype(jnp.float32)
    per_slot = jnp.einsum("tks,tka->sa", to_slot, pieces, precision=lax.Precision.HIGHEST)
    per_slot = per_slot.reshape(owners, capacity, block_width)
    returned = lax.all_to_all(per_slot, "ox", 0, 0, tiled=True)
    block_line = jnp.arange(blocks_here, dtype=jnp.int32)
    to_block = (send_blocks[:, :, None] == block_line[None, None, :]).astype(jnp.float32)
    atmos_surface = jnp.einsum(
        "isb,isa->ba", to_block, returned, precision=lax.Precision.HIGHEST
    )
    return (state, atmos_surface)


def solution(mesh):
    return jax.shard_map(
        per_device,
        mesh=mesh,
        in_specs=(
            P(None, "oy", "ox"),
            P("ox", "oy", None, None),
            P("ox", "oy"),
            P("ox", "oy"),
            P("ox", "oy"),
            P(None, None, "ox", "oy"),
            P("ox", "oy"),
            P(),
        ),
        out_specs=(P(None, None, "ox", "oy"), P("oy", "ox")),
        check_vma=False,
    )
```

```python
import jax
import jax.numpy as jnp
from jax import lax
from jax.experimental import pallas as pl
from jax.experimental.pallas import tpu as pltpu
from jax.sharding import PartitionSpec as P

STEPS = 3


advect_coef = 0.25
pressure_coef = 0.1
thermal_coef = 0.2
haline_coef = 0.8
coriolis_coef = 0.5
vertical_coef = 0.1
forcing_coef = 0.5


def advance(padded, center, diffusivity, coriolis, forcing, wetness):
    east = padded[:, :, 2:, 1:-1]
    west = padded[:, :, :-2, 1:-1]
    north = padded[:, :, 1:-1, 2:]
    south = padded[:, :, 1:-1, :-2]
    zonal = center[0]
    meridional = center[1]
    advection = (
        -advect_coef * 0.5 * (zonal[None] * (east - west) + meridional[None] * (north - south))
    )
    laplace = diffusivity[None, :, None, None] * (east + west + north + south - 4.0 * center)
    upper = jnp.concatenate([center[:, :1], center[:, :-1]], axis=1)
    lower = jnp.concatenate([center[:, 1:], center[:, -1:]], axis=1)
    mixing = vertical_coef * (upper + lower - 2.0 * center)
    density = haline_coef * padded[3] - thermal_coef * padded[2]
    pressure = jnp.cumsum(density, axis=0) - 0.5 * density
    grad_east = pressure[:, 2:, 1:-1] - pressure[:, :-2, 1:-1]
    grad_north = pressure[:, 1:-1, 2:] - pressure[:, 1:-1, :-2]
    zonal_push = coriolis * meridional - pressure_coef * 0.5 * grad_east
    merid_push = -coriolis * zonal - pressure_coef * 0.5 * grad_north
    tracer_zero = jnp.zeros((2,) + zonal.shape, jnp.float32)
    momentum = jnp.concatenate([zonal_push[None], merid_push[None], tracer_zero], axis=0)
    total = advection + laplace + mixing + momentum
    total = total.at[:, 0].add(forcing_coef * forcing)
    return center + wetness * total


def stencil_kernel(diff_ref, cor_ref, state_ref, aux_ref, xt_ref, yt_ref, out_ref, first, second):
    fields, levels, rows, lanes = out_ref.shape
    channels = fields * levels
    tall = rows + xt_ref.shape[1]
    wide = lanes + yt_ref.shape[2]

    def widen(inner, ch):
        left = jnp.concatenate([inner, xt_ref[ch]], axis=0)
        return jnp.concatenate([left, yt_ref[ch]], axis=1)

    def aux(index):
        return widen(aux_ref[index], channels + index)

    def one_step(read, write):
        def level(l, cum):
            up = jnp.maximum(l - 1, 0)
            down = jnp.minimum(l + 1, levels - 1)
            here = [read(f * levels + l) for f in range(fields)]
            density = haline_coef * here[3] - thermal_coef * here[2]
            cum = cum + density
            pressure = cum - 0.5 * density
            zonal = here[0]
            meridional = here[1]
            top = jnp.where(l == 0, forcing_coef, 0.0)
            diff = diff_ref[l]
            coriolis = cor_ref[...]
            for f in range(fields):
                center = here[f]
                east = pltpu.roll(center, tall - 1, 0)
                west = pltpu.roll(center, 1, 0)
                north = pltpu.roll(center, wide - 1, 1)
                south = pltpu.roll(center, 1, 1)
                advection = -advect_coef * 0.5 * (zonal * (east - west) + meridional * (north - south))
                laplace = diff * (east + west + north + south - 4.0 * center)
                mixing = vertical_coef * (
                    read(f * levels + up) + read(f * levels + down) - 2.0 * center
                )
                total = advection + laplace + mixing
                if f == 0:
                    grad = pltpu.roll(pressure, tall - 1, 0) - pltpu.roll(pressure, 1, 0)
                    total = total + (coriolis * meridional - pressure_coef * 0.5 * grad)
                if f == 1:
                    grad = pltpu.roll(pressure, wide - 1, 1) - pltpu.roll(pressure, 1, 1)
                    total = total + (-coriolis * zonal - pressure_coef * 0.5 * grad)
                total = total + top * aux(f)
                write(f, l, center + aux(fields) * total)
            return cum

        lax.fori_loop(0, levels, level, jnp.zeros((tall, wide), jnp.float32))

    def read_src(ch):
        return widen(state_ref[ch], ch)

    def read_first(ch):
        return first[ch]

    def read_second(ch):
        return second[ch]

    def write_first(f, l, value):
        first[f * levels + l] = value

    def write_second(f, l, value):
        second[f * levels + l] = value

    def write_out(f, l, value):
        out_ref[f, l] = value[:rows, :lanes]

    writers = [write_first, write_second]
    for repeat in range(STEPS):
        write = write_out if repeat == STEPS - 1 else writers[repeat % 2]
        read = read_src if repeat == 0 else (read_first if repeat % 2 == 1 else read_second)
        one_step(read, write)


def run_steps(state, aux, x_tile, y_tile, coriolis, diffusivity, out_shape):
    channels = state.shape[0]
    tall = state.shape[1] + x_tile.shape[1]
    wide = state.shape[2] + y_tile.shape[2]
    vmem = pl.BlockSpec(memory_space=pltpu.VMEM)
    return pl.pallas_call(
        stencil_kernel,
        out_shape=jax.ShapeDtypeStruct(out_shape, jnp.float32),
        in_specs=[pl.BlockSpec(memory_space=pltpu.SMEM)] + [vmem] * 5,
        out_specs=vmem,
        scratch_shapes=[
            pltpu.VMEM((channels, tall, wide), jnp.float32),
            pltpu.VMEM((channels, tall, wide), jnp.float32),
        ],
    )(diffusivity, coriolis, state, aux, x_tile, y_tile)


def shifted(block, axis, dim, width):
    count = lax.axis_size(axis)
    forward = [(i, i + 1) for i in range(count - 1)]
    backward = [(target, source) for source, target in forward]
    size = block.shape[dim]
    low = lax.ppermute(lax.slice_in_dim(block, size - width, None, axis=dim), axis, forward)
    high = lax.ppermute(lax.slice_in_dim(block, 0, width, axis=dim), axis, backward)
    return low, high


def lat_factor(first_cell, count, lat_total):
    latitude = (first_cell + jnp.arange(count, dtype=jnp.int32)).astype(jnp.float32)
    return coriolis_coef * (2.0 * (latitude + 0.5) / lat_total - 1.0)


def per_device(
    atm_flux,
    remap_weights,
    tile_slots,
    need_blocks,
    send_blocks,
    ocean_state,
    land_mask,
    diffusivity,
):
    blocks_here = atm_flux.shape[1]
    block_width = atm_flux.shape[2]
    owners = lax.axis_size("ox")
    capacity = send_blocks.shape[1]
    slots = owners * capacity
    block_line = jnp.arange(blocks_here, dtype=jnp.int32)
    to_block = send_blocks[:, :, None] == block_line[None, None, :]
    outgoing = jnp.einsum(
        "isb,fba->isfa", to_block.astype(atm_flux.dtype), atm_flux, preferred_element_type=jnp.float32
    ).astype(atm_flux.dtype)
    incoming = lax.all_to_all(outgoing, "ox", 0, 0, tiled=True)
    incoming = incoming.reshape((slots,) + incoming.shape[2:])
    picks = incoming[tile_slots]
    forcing = jnp.einsum("tkfa,tkra->ftr", picks, remap_weights, preferred_element_type=jnp.float32)
    fields, levels, rows, lat_cells = ocean_state.shape
    lat_total = lat_cells * lax.axis_size("oy")
    lat_start = lax.axis_index("oy") * lat_cells
    wetness = land_mask.astype(jnp.float32)
    inner = ocean_state.reshape(fields * levels, rows, lat_cells)
    aux = jnp.concatenate([forcing, wetness[None]], axis=0)
    packed = jnp.concatenate([inner, aux], axis=0)
    tall = -(-(rows + 2 * STEPS) // 8) * 8
    wide = -(-(lat_cells + 2 * STEPS) // 128) * 128
    low, high = shifted(packed, "ox", 1, STEPS)
    gap = jnp.zeros((packed.shape[0], tall - rows - 2 * STEPS, lat_cells), jnp.float32)
    x_tile = jnp.concatenate([high, gap, low], axis=1)
    tall_block = jnp.concatenate([packed, x_tile], axis=1)
    south, north = shifted(tall_block, "oy", 2, STEPS)
    gap = jnp.zeros((packed.shape[0], tall, wide - lat_cells - 2 * STEPS), jnp.float32)
    y_tile = jnp.concatenate([north, gap, south], axis=2)
    lane = jnp.arange(wide, dtype=jnp.int32)
    offset = jnp.where(lane < lat_cells + STEPS, lane, lane - wide)
    latitude = (lat_start + offset).astype(jnp.float32)
    coriolis_wide = (coriolis_coef * (2.0 * (latitude + 0.5) / lat_total - 1.0))[None, :]
    state = run_steps(inner, aux, x_tile, y_tile, coriolis_wide, diffusivity, ocean_state.shape)
    surface = state[2, 0].astype(jnp.bfloat16)
    pieces = jnp.einsum("tkra,tr->tka", remap_weights, surface, preferred_element_type=jnp.float32)
    slot_line = jnp.arange(slots, dtype=jnp.int32)
    to_slot = (tile_slots[:, :, None] == slot_line[None, None, :]).astype(jnp.float32)
    per_slot = jnp.einsum("tks,tka->sa", to_slot, pieces, precision=lax.Precision.HIGHEST)
    per_slot = per_slot.reshape(owners, capacity, block_width)
    returned = lax.all_to_all(per_slot, "ox", 0, 0, tiled=True)
    atmos_surface = jnp.einsum(
        "isb,isa->ba", to_block.astype(jnp.float32), returned, precision=lax.Precision.HIGHEST
    )
    return (state, atmos_surface)


def solution(mesh):
    return jax.shard_map(
        per_device,
        mesh=mesh,
        in_specs=(
            P(None, "oy", "ox"),
            P("ox", "oy", None, None),
            P("ox", "oy"),
            P("ox", "oy"),
            P("ox", "oy"),
            P(None, None, "ox", "oy"),
            P("ox", "oy"),
            P(),
        ),
        out_specs=(P(None, None, "ox", "oy"), P("oy", "ox")),
        check_vma=False,
    )
```

```python
import jax
import jax.numpy as jnp
from jax import lax
from jax.experimental import pallas as pl
from jax.experimental.pallas import tpu as pltpu
from jax.sharding import PartitionSpec as P

STEPS = 3


advect_coef = 0.25
pressure_coef = 0.1
thermal_coef = 0.2
haline_coef = 0.8
coriolis_coef = 0.5
vertical_coef = 0.1
forcing_coef = 0.5


def widen(inner, x_tile, y_tile):
    left = jnp.concatenate([inner, x_tile], axis=0)
    return jnp.concatenate([left, y_tile], axis=1)


def one_step(levels, shape, diff_ref, cor_ref, read, wet, force, write, partial):
    fields = 4
    tall, wide = shape

    def level(l, cum):
        up = jnp.maximum(l - 1, 0)
        down = jnp.minimum(l + 1, levels - 1)
        here = [read(f, l) for f in range(fields)]
        density = haline_coef * here[3] - thermal_coef * here[2]
        cum = cum + density
        pressure = cum - 0.5 * density
        zonal = here[0]
        meridional = here[1]
        top = jnp.where(l == 0, forcing_coef, 0.0)
        diff = diff_ref[l]
        coriolis = cor_ref[...]
        for f in range(fields):
            center = here[f]
            east = pltpu.roll(center, tall - 1, 0)
            west = pltpu.roll(center, 1, 0)
            north = pltpu.roll(center, wide - 1, 1)
            south = pltpu.roll(center, 1, 1)
            advection = -advect_coef * 0.5 * (zonal * (east - west) + meridional * (north - south))
            laplace = diff * (east + west + north + south - 4.0 * center)
            mixing = vertical_coef * (read(f, up) + read(f, down) - 2.0 * center)
            total = advection + laplace + mixing
            if f == 0:
                grad = pltpu.roll(pressure, tall - 1, 0) - pltpu.roll(pressure, 1, 0)
                total = total + (coriolis * meridional - pressure_coef * 0.5 * grad)
            if f == 1:
                grad = pltpu.roll(pressure, wide - 1, 1) - pltpu.roll(pressure, 1, 1)
                total = total + (-coriolis * zonal - pressure_coef * 0.5 * grad)
            if partial:
                write(f, l, jnp.where(l == 0, total, center + wet() * total))
            else:
                total = total + top * force(f)
                write(f, l, center + wet() * total)
        return cum

    lax.fori_loop(0, levels, level, jnp.zeros((tall, wide), jnp.float32))


def first_kernel(diff_ref, cor_ref, state_ref, xt_ref, yt_ref, out_ref):
    channels = state_ref.shape[0] - 1
    levels = channels // 4

    def read(f, l):
        ch = f * levels + l
        return widen(state_ref[ch], xt_ref[ch], yt_ref[ch])

    def wet():
        return widen(state_ref[channels], xt_ref[channels], yt_ref[channels])

    def write(f, l, value):
        out_ref[f * levels + l] = value

    one_step(levels, out_ref.shape[1:], diff_ref, cor_ref, read, wet, None, write, True)


def rest_kernel(
    diff_ref, cor_ref, state_ref, xt_ref, yt_ref, part_ref, force_ref, fxt_ref, fyt_ref,
    out_ref, bottom, second,
):
    fields, levels, rows, lanes = out_ref.shape
    channels = fields * levels

    def wet():
        return widen(state_ref[channels], xt_ref[channels], yt_ref[channels])

    def force(f):
        return widen(force_ref[f], fxt_ref[f], fyt_ref[f])

    for f in range(fields):
        ch = f * levels
        center = widen(state_ref[ch], xt_ref[ch], yt_ref[ch])
        bottom[f] = center + wet() * (part_ref[ch] + forcing_coef * force(f))

    def read_part(f, l):
        return jnp.where(l == 0, bottom[f], part_ref[f * levels + l])

    def read_second(f, l):
        return second[f * levels + l]

    def write_second(f, l, value):
        second[f * levels + l] = value

    def write_out(f, l, value):
        out_ref[f, l] = value[:rows, :lanes]

    shape = second.shape[1:]
    one_step(levels, shape, diff_ref, cor_ref, read_part, wet, force, write_second, False)
    one_step(levels, shape, diff_ref, cor_ref, read_second, wet, force, write_out, False)


def first_step(state, x_tile, y_tile, coriolis, diffusivity):
    channels = state.shape[0] - 1
    tall = state.shape[1] + x_tile.shape[1]
    wide = state.shape[2] + y_tile.shape[2]
    vmem = pl.BlockSpec(memory_space=pltpu.VMEM)
    return pl.pallas_call(
        first_kernel,
        out_shape=jax.ShapeDtypeStruct((channels, tall, wide), jnp.float32),
        in_specs=[pl.BlockSpec(memory_space=pltpu.SMEM)] + [vmem] * 4,
        out_specs=vmem,
    )(diffusivity, coriolis, state, x_tile, y_tile)


def rest_steps(state, x_tile, y_tile, part, forcing, fx_tile, fy_tile, coriolis, diffusivity, out_shape):
    channels = part.shape[0]
    tall, wide = part.shape[1], part.shape[2]
    vmem = pl.BlockSpec(memory_space=pltpu.VMEM)
    return pl.pallas_call(
        rest_kernel,
        out_shape=jax.ShapeDtypeStruct(out_shape, jnp.float32),
        in_specs=[pl.BlockSpec(memory_space=pltpu.SMEM)] + [vmem] * 8,
        out_specs=vmem,
        scratch_shapes=[
            pltpu.VMEM((out_shape[0], tall, wide), jnp.float32),
            pltpu.VMEM((channels, tall, wide), jnp.float32),
        ],
    )(diffusivity, coriolis, state, x_tile, y_tile, part, forcing, fx_tile, fy_tile)


def shifted(block, axis, dim, width):
    count = lax.axis_size(axis)
    forward = [(i, i + 1) for i in range(count - 1)]
    backward = [(target, source) for source, target in forward]
    size = block.shape[dim]
    low = lax.ppermute(lax.slice_in_dim(block, size - width, None, axis=dim), axis, forward)
    high = lax.ppermute(lax.slice_in_dim(block, 0, width, axis=dim), axis, backward)
    return low, high


def x_halo(block, tall):
    rows = block.shape[1]
    low, high = shifted(block, "ox", 1, STEPS)
    gap = jnp.zeros((block.shape[0], tall - rows - 2 * STEPS, block.shape[2]), block.dtype)
    return jnp.concatenate([high, gap, low], axis=1)


def y_halo(tall_block, wide):
    lat_cells = tall_block.shape[2]
    south, north = shifted(tall_block, "oy", 2, STEPS)
    gap = jnp.zeros(
        (tall_block.shape[0], tall_block.shape[1], wide - lat_cells - 2 * STEPS), tall_block.dtype
    )
    return jnp.concatenate([north, gap, south], axis=2)


def lat_factor(first_cell, count, lat_total):
    latitude = (first_cell + jnp.arange(count, dtype=jnp.int32)).astype(jnp.float32)
    return coriolis_coef * (2.0 * (latitude + 0.5) / lat_total - 1.0)


def per_device(
    atm_flux,
    remap_weights,
    tile_slots,
    need_blocks,
    send_blocks,
    ocean_state,
    land_mask,
    diffusivity,
):
    blocks_here = atm_flux.shape[1]
    block_width = atm_flux.shape[2]
    owners = lax.axis_size("ox")
    capacity = send_blocks.shape[1]
    slots = owners * capacity
    block_line = jnp.arange(blocks_here, dtype=jnp.int32)
    to_block = send_blocks[:, :, None] == block_line[None, None, :]
    outgoing = jnp.einsum(
        "isb,fba->isfa", to_block.astype(atm_flux.dtype), atm_flux, preferred_element_type=jnp.float32
    ).astype(atm_flux.dtype)
    incoming = lax.all_to_all(outgoing, "ox", 0, 0, tiled=True)
    fields, levels, rows, lat_cells = ocean_state.shape
    lat_total = lat_cells * lax.axis_size("oy")
    lat_start = lax.axis_index("oy") * lat_cells
    wetness = land_mask.astype(jnp.float32)
    inner = ocean_state.reshape(fields * levels, rows, lat_cells)
    packed = jnp.concatenate([inner, wetness[None]], axis=0)
    tall = -(-(rows + 2 * STEPS) // 8) * 8
    wide = -(-(lat_cells + 2 * STEPS) // 128) * 128
    x_tile = x_halo(packed, tall)
    y_tile = y_halo(jnp.concatenate([packed, x_tile], axis=1), wide)
    lane = jnp.arange(wide, dtype=jnp.int32)
    offset = jnp.where(lane < lat_cells + STEPS, lane, lane - wide)
    latitude = (lat_start + offset).astype(jnp.float32)
    coriolis_wide = (coriolis_coef * (2.0 * (latitude + 0.5) / lat_total - 1.0))[None, :]
    part = first_step(packed, x_tile, y_tile, coriolis_wide, diffusivity)
    incoming, part = lax.optimization_barrier((incoming, part))
    incoming = incoming.reshape((slots,) + incoming.shape[2:])
    picks = incoming[tile_slots]
    forcing = jnp.einsum("tkfa,tkra->ftr", picks, remap_weights, preferred_element_type=jnp.float32)
    fx_tile = x_halo(forcing, tall)
    forcing_tall = jnp.concatenate([forcing, fx_tile], axis=1)
    fy_tile = y_halo(forcing_tall, wide)
    state = rest_steps(
        packed, x_tile, y_tile, part, forcing, fx_tile, fy_tile, coriolis_wide, diffusivity, ocean_state.shape
    )
    surface = state[2, 0].astype(jnp.bfloat16)
    pieces = jnp.einsum("tkra,tr->tka", remap_weights, surface, preferred_element_type=jnp.float32)
    slot_line = jnp.arange(slots, dtype=jnp.int32)
    to_slot = (tile_slots[:, :, None] == slot_line[None, None, :]).astype(jnp.float32)
    per_slot = jnp.einsum("tks,tka->sa", to_slot, pieces, precision=lax.Precision.HIGHEST)
    per_slot = per_slot.reshape(owners, capacity, block_width)
    returned = lax.all_to_all(per_slot, "ox", 0, 0, tiled=True)
    atmos_surface = jnp.einsum(
        "isb,isa->ba", to_block.astype(jnp.float32), returned, precision=lax.Precision.HIGHEST
    )
    return (state, atmos_surface)


def solution(mesh):
    return jax.shard_map(
        per_device,
        mesh=mesh,
        in_specs=(
            P(None, "oy", "ox"),
            P("ox", "oy", None, None),
            P("ox", "oy"),
            P("ox", "oy"),
            P("ox", "oy"),
            P(None, None, "ox", "oy"),
            P("ox", "oy"),
            P(),
        ),
        out_specs=(P(None, None, "ox", "oy"), P("oy", "ox")),
        check_vma=False,
    )
```

```python
import jax
import jax.numpy as jnp
from jax import lax
from jax.experimental import pallas as pl
from jax.experimental.pallas import tpu as pltpu
from jax.sharding import PartitionSpec as P

STEPS = 3


advect_coef = 0.25
pressure_coef = 0.1
thermal_coef = 0.2
haline_coef = 0.8
coriolis_coef = 0.5
vertical_coef = 0.1
forcing_coef = 0.5


def stencil_kernel(
    diff_ref, cor_ref, state_ref, aux_ref, high_ref, low_ref, north_ref, south_ref,
    out_ref, source, first, second, x_pad, y_pad,
):
    fields, levels, rows, lanes = out_ref.shape
    channels = fields * levels
    tall, wide = source.shape[1], source.shape[2]
    width = high_ref.shape[1]
    x_pad[...] = jnp.zeros(x_pad.shape, jnp.float32)
    y_pad[...] = jnp.zeros(y_pad.shape, jnp.float32)
    row_line = lax.broadcasted_iota(jnp.int32, (tall - rows, lanes), 0)
    lane_line = lax.broadcasted_iota(jnp.int32, (tall, wide - lanes), 1)

    def assemble(ch, inner):
        source[ch, :rows, :lanes] = inner
        x_pad[0, :width] = high_ref[ch]
        x_pad[1, :width] = low_ref[ch]
        east_west = jnp.where(
            row_line < width, x_pad[0], pltpu.roll(x_pad[1], tall - rows - width, 0)
        )
        source[ch, rows:, :lanes] = east_west
        y_pad[0, :, :width] = north_ref[ch]
        y_pad[1, :, :width] = south_ref[ch]
        north_south = jnp.where(
            lane_line < width, y_pad[0], pltpu.roll(y_pad[1], wide - lanes - width, 1)
        )
        source[ch, :, lanes:] = north_south

    def assemble_state(ch, carry):
        assemble(ch, state_ref[ch])
        return carry

    def assemble_aux(index, carry):
        assemble(channels + index, aux_ref[index])
        return carry

    lax.fori_loop(0, channels, assemble_state, 0)
    lax.fori_loop(0, aux_ref.shape[0], assemble_aux, 0)

    def aux(index):
        return source[channels + index]

    def one_step(read, write):
        def level(l, cum):
            up = jnp.maximum(l - 1, 0)
            down = jnp.minimum(l + 1, levels - 1)
            here = [read(f * levels + l) for f in range(fields)]
            density = haline_coef * here[3] - thermal_coef * here[2]
            cum = cum + density
            pressure = cum - 0.5 * density
            zonal = here[0]
            meridional = here[1]
            top = jnp.where(l == 0, forcing_coef, 0.0)
            diff = diff_ref[l]
            coriolis = cor_ref[...]
            for f in range(fields):
                center = here[f]
                east = pltpu.roll(center, tall - 1, 0)
                west = pltpu.roll(center, 1, 0)
                north = pltpu.roll(center, wide - 1, 1)
                south = pltpu.roll(center, 1, 1)
                advection = -advect_coef * 0.5 * (zonal * (east - west) + meridional * (north - south))
                laplace = diff * (east + west + north + south - 4.0 * center)
                mixing = vertical_coef * (
                    read(f * levels + up) + read(f * levels + down) - 2.0 * center
                )
                total = advection + laplace + mixing
                if f == 0:
                    grad = pltpu.roll(pressure, tall - 1, 0) - pltpu.roll(pressure, 1, 0)
                    total = total + (coriolis * meridional - pressure_coef * 0.5 * grad)
                if f == 1:
                    grad = pltpu.roll(pressure, wide - 1, 1) - pltpu.roll(pressure, 1, 1)
                    total = total + (-coriolis * zonal - pressure_coef * 0.5 * grad)
                total = total + top * aux(f)
                write(f, l, center + aux(fields) * total)
            return cum

        lax.fori_loop(0, levels, level, jnp.zeros((tall, wide), jnp.float32))

    def read_src(ch):
        return source[ch]

    def read_first(ch):
        return first[ch]

    def read_second(ch):
        return second[ch]

    def write_first(f, l, value):
        first[f * levels + l] = value

    def write_second(f, l, value):
        second[f * levels + l] = value

    def write_out(f, l, value):
        out_ref[f, l] = value[:rows, :lanes]

    writers = [write_first, write_second]
    for repeat in range(STEPS):
        write = write_out if repeat == STEPS - 1 else writers[repeat % 2]
        read = read_src if repeat == 0 else (read_first if repeat % 2 == 1 else read_second)
        one_step(read, write)


def run_steps(state, aux, high, low, north, south, coriolis, diffusivity, out_shape):
    channels = state.shape[0] + aux.shape[0]
    rows, lanes = state.shape[1], state.shape[2]
    width = high.shape[1]
    tall = -(-(rows + 2 * width) // 8) * 8
    wide = -(-(lanes + 2 * width) // 128) * 128
    vmem = pl.BlockSpec(memory_space=pltpu.VMEM)
    return pl.pallas_call(
        stencil_kernel,
        out_shape=jax.ShapeDtypeStruct(out_shape, jnp.float32),
        in_specs=[pl.BlockSpec(memory_space=pltpu.SMEM)] + [vmem] * 7,
        out_specs=vmem,
        scratch_shapes=[
            pltpu.VMEM((channels, tall, wide), jnp.float32),
            pltpu.VMEM((state.shape[0], tall, wide), jnp.float32),
            pltpu.VMEM((state.shape[0], tall, wide), jnp.float32),
            pltpu.VMEM((2, tall - rows, lanes), jnp.float32),
            pltpu.VMEM((2, tall, wide - lanes), jnp.float32),
        ],
    )(diffusivity, coriolis, state, aux, high, low, north, south)


def shifted(block, axis, dim, width):
    count = lax.axis_size(axis)
    forward = [(i, i + 1) for i in range(count - 1)]
    backward = [(target, source) for source, target in forward]
    size = block.shape[dim]
    low = lax.ppermute(lax.slice_in_dim(block, size - width, None, axis=dim), axis, forward)
    high = lax.ppermute(lax.slice_in_dim(block, 0, width, axis=dim), axis, backward)
    return low, high


def lat_factor(first_cell, count, lat_total):
    latitude = (first_cell + jnp.arange(count, dtype=jnp.int32)).astype(jnp.float32)
    return coriolis_coef * (2.0 * (latitude + 0.5) / lat_total - 1.0)


def per_device(
    atm_flux,
    remap_weights,
    tile_slots,
    need_blocks,
    send_blocks,
    ocean_state,
    land_mask,
    diffusivity,
):
    blocks_here = atm_flux.shape[1]
    block_width = atm_flux.shape[2]
    owners = lax.axis_size("ox")
    capacity = send_blocks.shape[1]
    slots = owners * capacity
    block_line = jnp.arange(blocks_here, dtype=jnp.int32)
    to_block = send_blocks[:, :, None] == block_line[None, None, :]
    outgoing = jnp.einsum(
        "isb,fba->isfa", to_block.astype(atm_flux.dtype), atm_flux, preferred_element_type=jnp.float32
    ).astype(atm_flux.dtype)
    incoming = lax.all_to_all(outgoing, "ox", 0, 0, tiled=True)
    incoming = incoming.reshape((slots,) + incoming.shape[2:])
    picks = incoming[tile_slots]
    forcing = jnp.einsum("tkfa,tkra->ftr", picks, remap_weights, preferred_element_type=jnp.float32)
    fields, levels, rows, lat_cells = ocean_state.shape
    lat_total = lat_cells * lax.axis_size("oy")
    lat_start = lax.axis_index("oy") * lat_cells
    wetness = land_mask.astype(jnp.float32)
    inner = ocean_state.reshape(fields * levels, rows, lat_cells)
    aux = jnp.concatenate([forcing, wetness[None]], axis=0)
    packed = jnp.concatenate([inner, aux], axis=0)
    tall = -(-(rows + 2 * STEPS) // 8) * 8
    wide = -(-(lat_cells + 2 * STEPS) // 128) * 128
    low, high = shifted(packed, "ox", 1, STEPS)
    gap = jnp.zeros((packed.shape[0], tall - rows - 2 * STEPS, STEPS), jnp.float32)
    south_edge = jnp.concatenate(
        [packed[:, :, -STEPS:], high[:, :, -STEPS:], gap, low[:, :, -STEPS:]], axis=1
    )
    north_edge = jnp.concatenate(
        [packed[:, :, :STEPS], high[:, :, :STEPS], gap, low[:, :, :STEPS]], axis=1
    )
    count = lax.axis_size("oy")
    forward = [(i, i + 1) for i in range(count - 1)]
    backward = [(target, source) for source, target in forward]
    south = lax.ppermute(south_edge, "oy", forward)
    north = lax.ppermute(north_edge, "oy", backward)
    lane = jnp.arange(wide, dtype=jnp.int32)
    offset = jnp.where(lane < lat_cells + STEPS, lane, lane - wide)
    latitude = (lat_start + offset).astype(jnp.float32)
    coriolis_wide = (coriolis_coef * (2.0 * (latitude + 0.5) / lat_total - 1.0))[None, :]
    state = run_steps(inner, aux, high, low, north, south, coriolis_wide, diffusivity, ocean_state.shape)
    surface = state[2, 0].astype(jnp.bfloat16)
    pieces = jnp.einsum("tkra,tr->tka", remap_weights, surface, preferred_element_type=jnp.float32)
    slot_line = jnp.arange(slots, dtype=jnp.int32)
    to_slot = (tile_slots[:, :, None] == slot_line[None, None, :]).astype(jnp.float32)
    per_slot = jnp.einsum("tks,tka->sa", to_slot, pieces, precision=lax.Precision.HIGHEST)
    per_slot = per_slot.reshape(owners, capacity, block_width)
    returned = lax.all_to_all(per_slot, "ox", 0, 0, tiled=True)
    atmos_surface = jnp.einsum(
        "isb,isa->ba", to_block.astype(jnp.float32), returned, precision=lax.Precision.HIGHEST
    )
    return (state, atmos_surface)


def solution(mesh):
    return jax.shard_map(
        per_device,
        mesh=mesh,
        in_specs=(
            P(None, "oy", "ox"),
            P("ox", "oy", None, None),
            P("ox", "oy"),
            P("ox", "oy"),
            P("ox", "oy"),
            P(None, None, "ox", "oy"),
            P("ox", "oy"),
            P(),
        ),
        out_specs=(P(None, None, "ox", "oy"), P("oy", "ox")),
        check_vma=False,
    )
```

```python
import jax
import jax.numpy as jnp
from jax import lax
from jax.experimental import pallas as pl
from jax.experimental.pallas import tpu as pltpu
from jax.sharding import PartitionSpec as P

STEPS = 3


advect_coef = 0.25
pressure_coef = 0.1
thermal_coef = 0.2
haline_coef = 0.8
coriolis_coef = 0.5
vertical_coef = 0.1
forcing_coef = 0.5


def stencil_kernel(
    diff_ref, cor_ref, state_ref, aux_ref, high_ref, low_ref, north_ref, south_ref,
    out_ref, source, first, second,
):
    fields, levels, rows, lanes = out_ref.shape
    channels = fields * levels
    tall, wide = source.shape[1], source.shape[2]
    width = high_ref.shape[1]

    def assemble(ch, inner):
        source[ch, :rows, :lanes] = inner
        source[ch, rows:, :] = jnp.zeros((tall - rows, wide), jnp.float32)
        source[ch, :rows, lanes:] = jnp.zeros((rows, wide - lanes), jnp.float32)
        source[ch, rows : rows + width, :lanes] = high_ref[ch]
        source[ch, tall - width :, :lanes] = low_ref[ch]
        source[ch, :, lanes : lanes + width] = north_ref[ch]
        source[ch, :, wide - width :] = south_ref[ch]

    def assemble_state(ch, carry):
        assemble(ch, state_ref[ch])
        return carry

    def assemble_aux(index, carry):
        assemble(channels + index, aux_ref[index])
        return carry

    lax.fori_loop(0, channels, assemble_state, 0, unroll=4)
    lax.fori_loop(0, aux_ref.shape[0], assemble_aux, 0, unroll=True)

    def aux(index):
        return source[channels + index]

    def one_step(read, write):
        def level(l, cum):
            up = jnp.maximum(l - 1, 0)
            down = jnp.minimum(l + 1, levels - 1)
            here = [read(f * levels + l) for f in range(fields)]
            density = haline_coef * here[3] - thermal_coef * here[2]
            cum = cum + density
            pressure = cum - 0.5 * density
            zonal = here[0]
            meridional = here[1]
            top = jnp.where(l == 0, forcing_coef, 0.0)
            diff = diff_ref[l]
            coriolis = cor_ref[...]
            for f in range(fields):
                center = here[f]
                east = pltpu.roll(center, tall - 1, 0)
                west = pltpu.roll(center, 1, 0)
                north = pltpu.roll(center, wide - 1, 1)
                south = pltpu.roll(center, 1, 1)
                advection = -advect_coef * 0.5 * (zonal * (east - west) + meridional * (north - south))
                laplace = diff * (east + west + north + south - 4.0 * center)
                mixing = vertical_coef * (
                    read(f * levels + up) + read(f * levels + down) - 2.0 * center
                )
                total = advection + laplace + mixing
                if f == 0:
                    grad = pltpu.roll(pressure, tall - 1, 0) - pltpu.roll(pressure, 1, 0)
                    total = total + (coriolis * meridional - pressure_coef * 0.5 * grad)
                if f == 1:
                    grad = pltpu.roll(pressure, wide - 1, 1) - pltpu.roll(pressure, 1, 1)
                    total = total + (-coriolis * zonal - pressure_coef * 0.5 * grad)
                total = total + top * aux(f)
                write(f, l, center + aux(fields) * total)
            return cum

        lax.fori_loop(0, levels, level, jnp.zeros((tall, wide), jnp.float32))

    def read_src(ch):
        return source[ch]

    def read_first(ch):
        return first[ch]

    def read_second(ch):
        return second[ch]

    def write_first(f, l, value):
        first[f * levels + l] = value

    def write_second(f, l, value):
        second[f * levels + l] = value

    def write_out(f, l, value):
        out_ref[f, l] = value[:rows, :lanes]

    writers = [write_first, write_second]
    for repeat in range(STEPS):
        write = write_out if repeat == STEPS - 1 else writers[repeat % 2]
        read = read_src if repeat == 0 else (read_first if repeat % 2 == 1 else read_second)
        one_step(read, write)


def run_steps(state, aux, high, low, north, south, coriolis, diffusivity, out_shape):
    channels = state.shape[0] + aux.shape[0]
    rows, lanes = state.shape[1], state.shape[2]
    width = high.shape[1]
    tall = -(-(rows + 2 * width) // 8) * 8
    wide = -(-(lanes + 2 * width) // 128) * 128
    vmem = pl.BlockSpec(memory_space=pltpu.VMEM)
    return pl.pallas_call(
        stencil_kernel,
        out_shape=jax.ShapeDtypeStruct(out_shape, jnp.float32),
        in_specs=[pl.BlockSpec(memory_space=pltpu.SMEM)] + [vmem] * 7,
        out_specs=vmem,
        scratch_shapes=[
            pltpu.VMEM((channels, tall, wide), jnp.float32),
            pltpu.VMEM((state.shape[0], tall, wide), jnp.float32),
            pltpu.VMEM((state.shape[0], tall, wide), jnp.float32),
        ],
    )(diffusivity, coriolis, state, aux, high, low, north, south)


def shifted(block, axis, dim, width):
    count = lax.axis_size(axis)
    forward = [(i, i + 1) for i in range(count - 1)]
    backward = [(target, source) for source, target in forward]
    size = block.shape[dim]
    low = lax.ppermute(lax.slice_in_dim(block, size - width, None, axis=dim), axis, forward)
    high = lax.ppermute(lax.slice_in_dim(block, 0, width, axis=dim), axis, backward)
    return low, high


def lat_factor(first_cell, count, lat_total):
    latitude = (first_cell + jnp.arange(count, dtype=jnp.int32)).astype(jnp.float32)
    return coriolis_coef * (2.0 * (latitude + 0.5) / lat_total - 1.0)


def per_device(
    atm_flux,
    remap_weights,
    tile_slots,
    need_blocks,
    send_blocks,
    ocean_state,
    land_mask,
    diffusivity,
):
    blocks_here = atm_flux.shape[1]
    block_width = atm_flux.shape[2]
    owners = lax.axis_size("ox")
    capacity = send_blocks.shape[1]
    slots = owners * capacity
    block_line = jnp.arange(blocks_here, dtype=jnp.int32)
    to_block = send_blocks[:, :, None] == block_line[None, None, :]
    outgoing = jnp.einsum(
        "isb,fba->isfa", to_block.astype(atm_flux.dtype), atm_flux, preferred_element_type=jnp.float32
    ).astype(atm_flux.dtype)
    incoming = lax.all_to_all(outgoing, "ox", 0, 0, tiled=True)
    incoming = incoming.reshape((slots,) + incoming.shape[2:])
    picks = incoming[tile_slots]
    forcing = jnp.einsum("tkfa,tkra->ftr", picks, remap_weights, preferred_element_type=jnp.float32)
    fields, levels, rows, lat_cells = ocean_state.shape
    lat_total = lat_cells * lax.axis_size("oy")
    lat_start = lax.axis_index("oy") * lat_cells
    wetness = land_mask.astype(jnp.float32)
    inner = ocean_state.reshape(fields * levels, rows, lat_cells)
    aux = jnp.concatenate([forcing, wetness[None]], axis=0)
    packed = jnp.concatenate([inner, aux], axis=0)
    tall = -(-(rows + 2 * STEPS) // 8) * 8
    wide = -(-(lat_cells + 2 * STEPS) // 128) * 128
    low, high = shifted(packed, "ox", 1, STEPS)
    gap = jnp.zeros((packed.shape[0], tall - rows - 2 * STEPS, STEPS), jnp.float32)
    south_edge = jnp.concatenate(
        [packed[:, :, -STEPS:], high[:, :, -STEPS:], gap, low[:, :, -STEPS:]], axis=1
    )
    north_edge = jnp.concatenate(
        [packed[:, :, :STEPS], high[:, :, :STEPS], gap, low[:, :, :STEPS]], axis=1
    )
    count = lax.axis_size("oy")
    forward = [(i, i + 1) for i in range(count - 1)]
    backward = [(target, source) for source, target in forward]
    south = lax.ppermute(south_edge, "oy", forward)
    north = lax.ppermute(north_edge, "oy", backward)
    lane = jnp.arange(wide, dtype=jnp.int32)
    offset = jnp.where(lane < lat_cells + STEPS, lane, lane - wide)
    latitude = (lat_start + offset).astype(jnp.float32)
    coriolis_wide = (coriolis_coef * (2.0 * (latitude + 0.5) / lat_total - 1.0))[None, :]
    state = run_steps(inner, aux, high, low, north, south, coriolis_wide, diffusivity, ocean_state.shape)
    surface = state[2, 0].astype(jnp.bfloat16)
    pieces = jnp.einsum("tkra,tr->tka", remap_weights, surface, preferred_element_type=jnp.float32)
    slot_line = jnp.arange(slots, dtype=jnp.int32)
    to_slot = (tile_slots[:, :, None] == slot_line[None, None, :]).astype(jnp.float32)
    per_slot = jnp.einsum("tks,tka->sa", to_slot, pieces, precision=lax.Precision.HIGHEST)
    per_slot = per_slot.reshape(owners, capacity, block_width)
    returned = lax.all_to_all(per_slot, "ox", 0, 0, tiled=True)
    atmos_surface = jnp.einsum(
        "isb,isa->ba", to_block.astype(jnp.float32), returned, precision=lax.Precision.HIGHEST
    )
    return (state, atmos_surface)


def solution(mesh):
    return jax.shard_map(
        per_device,
        mesh=mesh,
        in_specs=(
            P(None, "oy", "ox"),
            P("ox", "oy", None, None),
            P("ox", "oy"),
            P("ox", "oy"),
            P("ox", "oy"),
            P(None, None, "ox", "oy"),
            P("ox", "oy"),
            P(),
        ),
        out_specs=(P(None, None, "ox", "oy"), P("oy", "ox")),
        check_vma=False,
    )
```

```python
import jax
import jax.numpy as jnp
from jax import lax
from jax.experimental import pallas as pl
from jax.experimental.pallas import tpu as pltpu
from jax.sharding import PartitionSpec as P

STEPS = 3


advect_coef = 0.25
pressure_coef = 0.1
thermal_coef = 0.2
haline_coef = 0.8
coriolis_coef = 0.5
vertical_coef = 0.1
forcing_coef = 0.5


def stencil_kernel(
    diff_ref, cor_ref, state_ref, aux_ref, high_ref, low_ref, north_ref, south_ref,
    out_ref, source, first, second,
):
    fields, levels, rows, lanes = out_ref.shape
    channels = fields * levels
    tall, wide = source.shape[1], source.shape[2]
    width = high_ref.shape[1]

    def assemble(ch, inner):
        source[ch, :rows, :lanes] = inner
        source[ch, rows:, :] = jnp.zeros((tall - rows, wide), jnp.float32)
        source[ch, :rows, lanes:] = jnp.zeros((rows, wide - lanes), jnp.float32)
        source[ch, rows : rows + width, :lanes] = high_ref[ch]
        source[ch, tall - width :, :lanes] = low_ref[ch]
        source[ch, :, lanes : lanes + width] = north_ref[ch]
        source[ch, :, wide - width :] = south_ref[ch]

    def assemble_state(ch, carry):
        assemble(ch, state_ref[ch])
        return carry

    def assemble_aux(index, carry):
        assemble(channels + index, aux_ref[index])
        return carry

    lax.fori_loop(0, channels, assemble_state, 0, unroll=4)
    lax.fori_loop(0, aux_ref.shape[0], assemble_aux, 0, unroll=True)

    def aux(index):
        return source[channels + index]

    def one_step(read, write, last):
        def crop(value):
            return value[:rows, :lanes] if last else value

        def level(l, cum):
            up = jnp.maximum(l - 1, 0)
            down = jnp.minimum(l + 1, levels - 1)
            here = [read(f * levels + l) for f in range(fields)]
            density = haline_coef * here[3] - thermal_coef * here[2]
            cum = cum + density
            pressure = cum - 0.5 * density
            zonal = crop(here[0])
            meridional = crop(here[1])
            top = jnp.where(l == 0, forcing_coef, 0.0)
            diff = diff_ref[l]
            coriolis = crop(jnp.broadcast_to(cor_ref[...], (tall, wide)))
            for f in range(fields):
                whole = here[f]
                center = crop(whole)
                east = crop(pltpu.roll(whole, tall - 1, 0))
                west = crop(pltpu.roll(whole, 1, 0))
                north = crop(pltpu.roll(whole, wide - 1, 1))
                south = crop(pltpu.roll(whole, 1, 1))
                advection = -advect_coef * 0.5 * (zonal * (east - west) + meridional * (north - south))
                laplace = diff * (east + west + north + south - 4.0 * center)
                mixing = vertical_coef * (
                    crop(read(f * levels + up)) + crop(read(f * levels + down)) - 2.0 * center
                )
                total = advection + laplace + mixing
                if f == 0:
                    grad = crop(pltpu.roll(pressure, tall - 1, 0)) - crop(pltpu.roll(pressure, 1, 0))
                    total = total + (coriolis * meridional - pressure_coef * 0.5 * grad)
                if f == 1:
                    grad = crop(pltpu.roll(pressure, wide - 1, 1)) - crop(pltpu.roll(pressure, 1, 1))
                    total = total + (-coriolis * zonal - pressure_coef * 0.5 * grad)
                total = total + top * crop(aux(f))
                write(f, l, center + crop(aux(fields)) * total)
            return cum

        lax.fori_loop(0, levels, level, jnp.zeros((tall, wide), jnp.float32))

    def read_src(ch):
        return source[ch]

    def read_first(ch):
        return first[ch]

    def read_second(ch):
        return second[ch]

    def write_first(f, l, value):
        first[f * levels + l] = value

    def write_second(f, l, value):
        second[f * levels + l] = value

    def write_out(f, l, value):
        out_ref[f, l] = value

    writers = [write_first, write_second]
    for repeat in range(STEPS):
        write = write_out if repeat == STEPS - 1 else writers[repeat % 2]
        read = read_src if repeat == 0 else (read_first if repeat % 2 == 1 else read_second)
        one_step(read, write, repeat == STEPS - 1)


def run_steps(state, aux, high, low, north, south, coriolis, diffusivity, out_shape):
    channels = state.shape[0] + aux.shape[0]
    rows, lanes = state.shape[1], state.shape[2]
    width = high.shape[1]
    tall = -(-(rows + 2 * width) // 8) * 8
    wide = -(-(lanes + 2 * width) // 128) * 128
    vmem = pl.BlockSpec(memory_space=pltpu.VMEM)
    return pl.pallas_call(
        stencil_kernel,
        out_shape=jax.ShapeDtypeStruct(out_shape, jnp.float32),
        in_specs=[pl.BlockSpec(memory_space=pltpu.SMEM)] + [vmem] * 7,
        out_specs=vmem,
        scratch_shapes=[
            pltpu.VMEM((channels, tall, wide), jnp.float32),
            pltpu.VMEM((state.shape[0], tall, wide), jnp.float32),
            pltpu.VMEM((state.shape[0], tall, wide), jnp.float32),
        ],
    )(diffusivity, coriolis, state, aux, high, low, north, south)


def shifted(block, axis, dim, width):
    count = lax.axis_size(axis)
    forward = [(i, i + 1) for i in range(count - 1)]
    backward = [(target, source) for source, target in forward]
    size = block.shape[dim]
    low = lax.ppermute(lax.slice_in_dim(block, size - width, None, axis=dim), axis, forward)
    high = lax.ppermute(lax.slice_in_dim(block, 0, width, axis=dim), axis, backward)
    return low, high


def lat_factor(first_cell, count, lat_total):
    latitude = (first_cell + jnp.arange(count, dtype=jnp.int32)).astype(jnp.float32)
    return coriolis_coef * (2.0 * (latitude + 0.5) / lat_total - 1.0)


def per_device(
    atm_flux,
    remap_weights,
    tile_slots,
    need_blocks,
    send_blocks,
    ocean_state,
    land_mask,
    diffusivity,
):
    blocks_here = atm_flux.shape[1]
    block_width = atm_flux.shape[2]
    owners = lax.axis_size("ox")
    capacity = send_blocks.shape[1]
    slots = owners * capacity
    block_line = jnp.arange(blocks_here, dtype=jnp.int32)
    to_block = send_blocks[:, :, None] == block_line[None, None, :]
    outgoing = jnp.einsum(
        "isb,fba->isfa", to_block.astype(atm_flux.dtype), atm_flux, preferred_element_type=jnp.float32
    ).astype(atm_flux.dtype)
    incoming = lax.all_to_all(outgoing, "ox", 0, 0, tiled=True)
    incoming = incoming.reshape((slots,) + incoming.shape[2:])
    picks = incoming[tile_slots]
    forcing = jnp.einsum("tkfa,tkra->ftr", picks, remap_weights, preferred_element_type=jnp.float32)
    fields, levels, rows, lat_cells = ocean_state.shape
    lat_total = lat_cells * lax.axis_size("oy")
    lat_start = lax.axis_index("oy") * lat_cells
    wetness = land_mask.astype(jnp.float32)
    inner = ocean_state.reshape(fields * levels, rows, lat_cells)
    aux = jnp.concatenate([forcing, wetness[None]], axis=0)
    packed = jnp.concatenate([inner, aux], axis=0)
    tall = -(-(rows + 2 * STEPS) // 8) * 8
    wide = -(-(lat_cells + 2 * STEPS) // 128) * 128
    low, high = shifted(packed, "ox", 1, STEPS)
    gap = jnp.zeros((packed.shape[0], tall - rows - 2 * STEPS, STEPS), jnp.float32)
    south_edge = jnp.concatenate(
        [packed[:, :, -STEPS:], high[:, :, -STEPS:], gap, low[:, :, -STEPS:]], axis=1
    )
    north_edge = jnp.concatenate(
        [packed[:, :, :STEPS], high[:, :, :STEPS], gap, low[:, :, :STEPS]], axis=1
    )
    count = lax.axis_size("oy")
    forward = [(i, i + 1) for i in range(count - 1)]
    backward = [(target, source) for source, target in forward]
    south = lax.ppermute(south_edge, "oy", forward)
    north = lax.ppermute(north_edge, "oy", backward)
    lane = jnp.arange(wide, dtype=jnp.int32)
    offset = jnp.where(lane < lat_cells + STEPS, lane, lane - wide)
    latitude = (lat_start + offset).astype(jnp.float32)
    coriolis_wide = (coriolis_coef * (2.0 * (latitude + 0.5) / lat_total - 1.0))[None, :]
    state = run_steps(inner, aux, high, low, north, south, coriolis_wide, diffusivity, ocean_state.shape)
    surface = state[2, 0].astype(jnp.bfloat16)
    pieces = jnp.einsum("tkra,tr->tka", remap_weights, surface, preferred_element_type=jnp.float32)
    slot_line = jnp.arange(slots, dtype=jnp.int32)
    to_slot = (tile_slots[:, :, None] == slot_line[None, None, :]).astype(jnp.float32)
    per_slot = jnp.einsum("tks,tka->sa", to_slot, pieces, precision=lax.Precision.HIGHEST)
    per_slot = per_slot.reshape(owners, capacity, block_width)
    returned = lax.all_to_all(per_slot, "ox", 0, 0, tiled=True)
    atmos_surface = jnp.einsum(
        "isb,isa->ba", to_block.astype(jnp.float32), returned, precision=lax.Precision.HIGHEST
    )
    return (state, atmos_surface)


def solution(mesh):
    return jax.shard_map(
        per_device,
        mesh=mesh,
        in_specs=(
            P(None, "oy", "ox"),
            P("ox", "oy", None, None),
            P("ox", "oy"),
            P("ox", "oy"),
            P("ox", "oy"),
            P(None, None, "ox", "oy"),
            P("ox", "oy"),
            P(),
        ),
        out_specs=(P(None, None, "ox", "oy"), P("oy", "ox")),
        check_vma=False,
    )
```

```python
import jax
import jax.numpy as jnp
from jax import lax
from jax.experimental import pallas as pl
from jax.experimental.pallas import tpu as pltpu
from jax.sharding import PartitionSpec as P

STEPS = 3


advect_coef = 0.25
pressure_coef = 0.1
thermal_coef = 0.2
haline_coef = 0.8
coriolis_coef = 0.5
vertical_coef = 0.1
forcing_coef = 0.5


def stencil_kernel(
    diff_ref, cor_ref, state_ref, aux_ref, high_ref, low_ref, north_ref, south_ref,
    out_ref, source, first, second,
):
    fields, levels, rows, lanes = out_ref.shape
    channels = fields * levels
    tall, wide = source.shape[1], source.shape[2]
    width = high_ref.shape[1]

    def assemble(ch, inner):
        source[ch, :rows, :lanes] = inner
        source[ch, rows:, :] = jnp.zeros((tall - rows, wide), jnp.float32)
        source[ch, :rows, lanes:] = jnp.zeros((rows, wide - lanes), jnp.float32)
        source[ch, rows : rows + width, :lanes] = high_ref[ch]
        source[ch, tall - width :, :lanes] = low_ref[ch]
        source[ch, :, lanes : lanes + width] = north_ref[ch]
        source[ch, :, wide - width :] = south_ref[ch]

    def assemble_state(ch, carry):
        assemble(ch, state_ref[ch])
        return carry

    def assemble_aux(index, carry):
        assemble(channels + index, aux_ref[index])
        return carry

    lax.fori_loop(0, channels, assemble_state, 0, unroll=4)
    lax.fori_loop(0, aux_ref.shape[0], assemble_aux, 0, unroll=True)

    def aux(index):
        return source[channels + index]

    def one_step(read, write, last):
        def crop(value):
            return value[:rows, :lanes] if last else value

        def level(l, cum):
            up = jnp.maximum(l - 1, 0)
            down = jnp.minimum(l + 1, levels - 1)
            here = [read(f * levels + l) for f in range(fields)]
            density = haline_coef * here[3] - thermal_coef * here[2]
            cum = cum + density
            pressure = cum - 0.5 * density
            zonal = crop(here[0])
            meridional = crop(here[1])
            top = jnp.where(l == 0, forcing_coef, 0.0)
            diff = diff_ref[l]
            coriolis = crop(jnp.broadcast_to(cor_ref[...], (tall, wide)))
            for f in range(fields):
                whole = here[f]
                center = crop(whole)
                east = crop(pltpu.roll(whole, tall - 1, 0))
                west = crop(pltpu.roll(whole, 1, 0))
                north = crop(pltpu.roll(whole, wide - 1, 1))
                south = crop(pltpu.roll(whole, 1, 1))
                advection = -advect_coef * 0.5 * (zonal * (east - west) + meridional * (north - south))
                laplace = diff * (east + west + north + south - 4.0 * center)
                mixing = vertical_coef * (
                    crop(read(f * levels + up)) + crop(read(f * levels + down)) - 2.0 * center
                )
                total = advection + laplace + mixing
                if f == 0:
                    grad = crop(pltpu.roll(pressure, tall - 1, 0)) - crop(pltpu.roll(pressure, 1, 0))
                    total = total + (coriolis * meridional - pressure_coef * 0.5 * grad)
                if f == 1:
                    grad = crop(pltpu.roll(pressure, wide - 1, 1)) - crop(pltpu.roll(pressure, 1, 1))
                    total = total + (-coriolis * zonal - pressure_coef * 0.5 * grad)
                total = total + top * crop(aux(f))
                write(f, l, center + crop(aux(fields)) * total)
            return cum

        lax.fori_loop(0, levels, level, jnp.zeros((tall, wide), jnp.float32), unroll=2)

    def read_src(ch):
        return source[ch]

    def read_first(ch):
        return first[ch]

    def read_second(ch):
        return second[ch]

    def write_first(f, l, value):
        first[f * levels + l] = value

    def write_second(f, l, value):
        second[f * levels + l] = value

    def write_out(f, l, value):
        out_ref[f, l] = value

    writers = [write_first, write_second]
    for repeat in range(STEPS):
        write = write_out if repeat == STEPS - 1 else writers[repeat % 2]
        read = read_src if repeat == 0 else (read_first if repeat % 2 == 1 else read_second)
        one_step(read, write, repeat == STEPS - 1)


def run_steps(state, aux, high, low, north, south, coriolis, diffusivity, out_shape):
    channels = state.shape[0] + aux.shape[0]
    rows, lanes = state.shape[1], state.shape[2]
    width = high.shape[1]
    tall = -(-(rows + 2 * width) // 8) * 8
    wide = -(-(lanes + 2 * width) // 128) * 128
    vmem = pl.BlockSpec(memory_space=pltpu.VMEM)
    return pl.pallas_call(
        stencil_kernel,
        out_shape=jax.ShapeDtypeStruct(out_shape, jnp.float32),
        in_specs=[pl.BlockSpec(memory_space=pltpu.SMEM)] + [vmem] * 7,
        out_specs=vmem,
        scratch_shapes=[
            pltpu.VMEM((channels, tall, wide), jnp.float32),
            pltpu.VMEM((state.shape[0], tall, wide), jnp.float32),
            pltpu.VMEM((state.shape[0], tall, wide), jnp.float32),
        ],
    )(diffusivity, coriolis, state, aux, high, low, north, south)


def shifted(block, axis, dim, width):
    count = lax.axis_size(axis)
    forward = [(i, i + 1) for i in range(count - 1)]
    backward = [(target, source) for source, target in forward]
    size = block.shape[dim]
    low = lax.ppermute(lax.slice_in_dim(block, size - width, None, axis=dim), axis, forward)
    high = lax.ppermute(lax.slice_in_dim(block, 0, width, axis=dim), axis, backward)
    return low, high


def lat_factor(first_cell, count, lat_total):
    latitude = (first_cell + jnp.arange(count, dtype=jnp.int32)).astype(jnp.float32)
    return coriolis_coef * (2.0 * (latitude + 0.5) / lat_total - 1.0)


def per_device(
    atm_flux,
    remap_weights,
    tile_slots,
    need_blocks,
    send_blocks,
    ocean_state,
    land_mask,
    diffusivity,
):
    blocks_here = atm_flux.shape[1]
    block_width = atm_flux.shape[2]
    owners = lax.axis_size("ox")
    capacity = send_blocks.shape[1]
    slots = owners * capacity
    block_line = jnp.arange(blocks_here, dtype=jnp.int32)
    to_block = send_blocks[:, :, None] == block_line[None, None, :]
    outgoing = jnp.einsum(
        "isb,fba->isfa", to_block.astype(atm_flux.dtype), atm_flux, preferred_element_type=jnp.float32
    ).astype(atm_flux.dtype)
    incoming = lax.all_to_all(outgoing, "ox", 0, 0, tiled=True)
    incoming = incoming.reshape((slots,) + incoming.shape[2:])
    picks = incoming[tile_slots]
    forcing = jnp.einsum("tkfa,tkra->ftr", picks, remap_weights, preferred_element_type=jnp.float32)
    fields, levels, rows, lat_cells = ocean_state.shape
    lat_total = lat_cells * lax.axis_size("oy")
    lat_start = lax.axis_index("oy") * lat_cells
    wetness = land_mask.astype(jnp.float32)
    inner = ocean_state.reshape(fields * levels, rows, lat_cells)
    aux = jnp.concatenate([forcing, wetness[None]], axis=0)
    packed = jnp.concatenate([inner, aux], axis=0)
    tall = -(-(rows + 2 * STEPS) // 8) * 8
    wide = -(-(lat_cells + 2 * STEPS) // 128) * 128
    low, high = shifted(packed, "ox", 1, STEPS)
    gap = jnp.zeros((packed.shape[0], tall - rows - 2 * STEPS, STEPS), jnp.float32)
    south_edge = jnp.concatenate(
        [packed[:, :, -STEPS:], high[:, :, -STEPS:], gap, low[:, :, -STEPS:]], axis=1
    )
    north_edge = jnp.concatenate(
        [packed[:, :, :STEPS], high[:, :, :STEPS], gap, low[:, :, :STEPS]], axis=1
    )
    count = lax.axis_size("oy")
    forward = [(i, i + 1) for i in range(count - 1)]
    backward = [(target, source) for source, target in forward]
    south = lax.ppermute(south_edge, "oy", forward)
    north = lax.ppermute(north_edge, "oy", backward)
    lane = jnp.arange(wide, dtype=jnp.int32)
    offset = jnp.where(lane < lat_cells + STEPS, lane, lane - wide)
    latitude = (lat_start + offset).astype(jnp.float32)
    coriolis_wide = (coriolis_coef * (2.0 * (latitude + 0.5) / lat_total - 1.0))[None, :]
    state = run_steps(inner, aux, high, low, north, south, coriolis_wide, diffusivity, ocean_state.shape)
    surface = state[2, 0].astype(jnp.bfloat16)
    pieces = jnp.einsum("tkra,tr->tka", remap_weights, surface, preferred_element_type=jnp.float32)
    slot_line = jnp.arange(slots, dtype=jnp.int32)
    to_slot = (tile_slots[:, :, None] == slot_line[None, None, :]).astype(jnp.float32)
    per_slot = jnp.einsum("tks,tka->sa", to_slot, pieces, precision=lax.Precision.HIGHEST)
    per_slot = per_slot.reshape(owners, capacity, block_width)
    returned = lax.all_to_all(per_slot, "ox", 0, 0, tiled=True)
    atmos_surface = jnp.einsum(
        "isb,isa->ba", to_block.astype(jnp.float32), returned, precision=lax.Precision.HIGHEST
    )
    return (state, atmos_surface)


def solution(mesh):
    return jax.shard_map(
        per_device,
        mesh=mesh,
        in_specs=(
            P(None, "oy", "ox"),
            P("ox", "oy", None, None),
            P("ox", "oy"),
            P("ox", "oy"),
            P("ox", "oy"),
            P(None, None, "ox", "oy"),
            P("ox", "oy"),
            P(),
        ),
        out_specs=(P(None, None, "ox", "oy"), P("oy", "ox")),
        check_vma=False,
    )
```

```python
import jax
import jax.numpy as jnp
from jax import lax
from jax.experimental import pallas as pl
from jax.experimental.pallas import tpu as pltpu
from jax.sharding import PartitionSpec as P

STEPS = 3


advect_coef = 0.25
pressure_coef = 0.1
thermal_coef = 0.2
haline_coef = 0.8
coriolis_coef = 0.5
vertical_coef = 0.1
forcing_coef = 0.5


def stencil_kernel(
    diff_ref, cor_ref, state_ref, aux_ref, high_ref, low_ref, north_ref, south_ref,
    out_ref, source, first, second,
):
    fields, levels, rows, lanes = out_ref.shape
    channels = fields * levels
    tall, wide = source.shape[1], source.shape[2]
    width = high_ref.shape[1]

    def assemble(ch, inner):
        source[ch, :rows, :lanes] = inner
        source[ch, rows:, :] = jnp.zeros((tall - rows, wide), jnp.float32)
        source[ch, :rows, lanes:] = jnp.zeros((rows, wide - lanes), jnp.float32)
        source[ch, rows : rows + width, :lanes] = high_ref[ch]
        source[ch, tall - width :, :lanes] = low_ref[ch]
        source[ch, :, lanes : lanes + width] = north_ref[ch]
        source[ch, :, wide - width :] = south_ref[ch]

    def assemble_state(ch, carry):
        assemble(ch, state_ref[ch])
        return carry

    def assemble_aux(index, carry):
        assemble(channels + index, aux_ref[index])
        return carry

    lax.fori_loop(0, channels, assemble_state, 0, unroll=4)
    lax.fori_loop(0, aux_ref.shape[0], assemble_aux, 0, unroll=True)

    def aux(index):
        return source[channels + index]

    def one_step(read, write, last):
        def crop(value):
            return value[:rows, :lanes] if last else value

        def level(l, cum):
            up = jnp.maximum(l - 1, 0)
            down = jnp.minimum(l + 1, levels - 1)
            here = [read(f * levels + l) for f in range(fields)]
            density = haline_coef * here[3] - thermal_coef * here[2]
            cum = cum + density
            pressure = cum - 0.5 * density
            zonal = crop(here[0])
            meridional = crop(here[1])
            top = jnp.where(l == 0, forcing_coef, 0.0)
            diff = diff_ref[l]
            coriolis = crop(jnp.broadcast_to(cor_ref[...], (tall, wide)))
            for f in range(fields):
                whole = here[f]
                center = crop(whole)
                east = crop(pltpu.roll(whole, tall - 1, 0))
                west = crop(pltpu.roll(whole, 1, 0))
                north = crop(pltpu.roll(whole, wide - 1, 1))
                south = crop(pltpu.roll(whole, 1, 1))
                advection = -advect_coef * 0.5 * (zonal * (east - west) + meridional * (north - south))
                laplace = diff * (east + west + north + south - 4.0 * center)
                mixing = vertical_coef * (
                    crop(read(f * levels + up)) + crop(read(f * levels + down)) - 2.0 * center
                )
                total = advection + laplace + mixing
                if f == 0:
                    grad = crop(pltpu.roll(pressure, tall - 1, 0)) - crop(pltpu.roll(pressure, 1, 0))
                    total = total + (coriolis * meridional - pressure_coef * 0.5 * grad)
                if f == 1:
                    grad = crop(pltpu.roll(pressure, wide - 1, 1)) - crop(pltpu.roll(pressure, 1, 1))
                    total = total + (-coriolis * zonal - pressure_coef * 0.5 * grad)
                total = total + top * crop(aux(f))
                write(f, l, center + crop(aux(fields)) * total)
            return cum

        lax.fori_loop(0, levels, level, jnp.zeros((tall, wide), jnp.float32), unroll=4)

    def read_src(ch):
        return source[ch]

    def read_first(ch):
        return first[ch]

    def read_second(ch):
        return second[ch]

    def write_first(f, l, value):
        first[f * levels + l] = value

    def write_second(f, l, value):
        second[f * levels + l] = value

    def write_out(f, l, value):
        out_ref[f, l] = value

    writers = [write_first, write_second]
    for repeat in range(STEPS):
        write = write_out if repeat == STEPS - 1 else writers[repeat % 2]
        read = read_src if repeat == 0 else (read_first if repeat % 2 == 1 else read_second)
        one_step(read, write, repeat == STEPS - 1)


def run_steps(state, aux, high, low, north, south, coriolis, diffusivity, out_shape):
    channels = state.shape[0] + aux.shape[0]
    rows, lanes = state.shape[1], state.shape[2]
    width = high.shape[1]
    tall = -(-(rows + 2 * width) // 8) * 8
    wide = -(-(lanes + 2 * width) // 128) * 128
    vmem = pl.BlockSpec(memory_space=pltpu.VMEM)
    return pl.pallas_call(
        stencil_kernel,
        out_shape=jax.ShapeDtypeStruct(out_shape, jnp.float32),
        in_specs=[pl.BlockSpec(memory_space=pltpu.SMEM)] + [vmem] * 7,
        out_specs=vmem,
        scratch_shapes=[
            pltpu.VMEM((channels, tall, wide), jnp.float32),
            pltpu.VMEM((state.shape[0], tall, wide), jnp.float32),
            pltpu.VMEM((state.shape[0], tall, wide), jnp.float32),
        ],
    )(diffusivity, coriolis, state, aux, high, low, north, south)


def shifted(block, axis, dim, width):
    count = lax.axis_size(axis)
    forward = [(i, i + 1) for i in range(count - 1)]
    backward = [(target, source) for source, target in forward]
    size = block.shape[dim]
    low = lax.ppermute(lax.slice_in_dim(block, size - width, None, axis=dim), axis, forward)
    high = lax.ppermute(lax.slice_in_dim(block, 0, width, axis=dim), axis, backward)
    return low, high


def lat_factor(first_cell, count, lat_total):
    latitude = (first_cell + jnp.arange(count, dtype=jnp.int32)).astype(jnp.float32)
    return coriolis_coef * (2.0 * (latitude + 0.5) / lat_total - 1.0)


def per_device(
    atm_flux,
    remap_weights,
    tile_slots,
    need_blocks,
    send_blocks,
    ocean_state,
    land_mask,
    diffusivity,
):
    blocks_here = atm_flux.shape[1]
    block_width = atm_flux.shape[2]
    owners = lax.axis_size("ox")
    capacity = send_blocks.shape[1]
    slots = owners * capacity
    block_line = jnp.arange(blocks_here, dtype=jnp.int32)
    to_block = send_blocks[:, :, None] == block_line[None, None, :]
    outgoing = jnp.einsum(
        "isb,fba->isfa", to_block.astype(atm_flux.dtype), atm_flux, preferred_element_type=jnp.float32
    ).astype(atm_flux.dtype)
    incoming = lax.all_to_all(outgoing, "ox", 0, 0, tiled=True)
    incoming = incoming.reshape((slots,) + incoming.shape[2:])
    picks = incoming[tile_slots]
    forcing = jnp.einsum("tkfa,tkra->ftr", picks, remap_weights, preferred_element_type=jnp.float32)
    fields, levels, rows, lat_cells = ocean_state.shape
    lat_total = lat_cells * lax.axis_size("oy")
    lat_start = lax.axis_index("oy") * lat_cells
    wetness = land_mask.astype(jnp.float32)
    inner = ocean_state.reshape(fields * levels, rows, lat_cells)
    aux = jnp.concatenate([forcing, wetness[None]], axis=0)
    packed = jnp.concatenate([inner, aux], axis=0)
    tall = -(-(rows + 2 * STEPS) // 8) * 8
    wide = -(-(lat_cells + 2 * STEPS) // 128) * 128
    low, high = shifted(packed, "ox", 1, STEPS)
    gap = jnp.zeros((packed.shape[0], tall - rows - 2 * STEPS, STEPS), jnp.float32)
    south_edge = jnp.concatenate(
        [packed[:, :, -STEPS:], high[:, :, -STEPS:], gap, low[:, :, -STEPS:]], axis=1
    )
    north_edge = jnp.concatenate(
        [packed[:, :, :STEPS], high[:, :, :STEPS], gap, low[:, :, :STEPS]], axis=1
    )
    count = lax.axis_size("oy")
    forward = [(i, i + 1) for i in range(count - 1)]
    backward = [(target, source) for source, target in forward]
    south = lax.ppermute(south_edge, "oy", forward)
    north = lax.ppermute(north_edge, "oy", backward)
    lane = jnp.arange(wide, dtype=jnp.int32)
    offset = jnp.where(lane < lat_cells + STEPS, lane, lane - wide)
    latitude = (lat_start + offset).astype(jnp.float32)
    coriolis_wide = (coriolis_coef * (2.0 * (latitude + 0.5) / lat_total - 1.0))[None, :]
    state = run_steps(inner, aux, high, low, north, south, coriolis_wide, diffusivity, ocean_state.shape)
    surface = state[2, 0].astype(jnp.bfloat16)
    pieces = jnp.einsum("tkra,tr->tka", remap_weights, surface, preferred_element_type=jnp.float32)
    slot_line = jnp.arange(slots, dtype=jnp.int32)
    to_slot = (tile_slots[:, :, None] == slot_line[None, None, :]).astype(jnp.float32)
    per_slot = jnp.einsum("tks,tka->sa", to_slot, pieces, precision=lax.Precision.HIGHEST)
    per_slot = per_slot.reshape(owners, capacity, block_width)
    returned = lax.all_to_all(per_slot, "ox", 0, 0, tiled=True)
    atmos_surface = jnp.einsum(
        "isb,isa->ba", to_block.astype(jnp.float32), returned, precision=lax.Precision.HIGHEST
    )
    return (state, atmos_surface)


def solution(mesh):
    return jax.shard_map(
        per_device,
        mesh=mesh,
        in_specs=(
            P(None, "oy", "ox"),
            P("ox", "oy", None, None),
            P("ox", "oy"),
            P("ox", "oy"),
            P("ox", "oy"),
            P(None, None, "ox", "oy"),
            P("ox", "oy"),
            P(),
        ),
        out_specs=(P(None, None, "ox", "oy"), P("oy", "ox")),
        check_vma=False,
    )
```

```python
import jax
import jax.numpy as jnp
from jax import lax
from jax.experimental import pallas as pl
from jax.experimental.pallas import tpu as pltpu
from jax.sharding import PartitionSpec as P

STEPS = 3


advect_coef = 0.25
pressure_coef = 0.1
thermal_coef = 0.2
haline_coef = 0.8
coriolis_coef = 0.5
vertical_coef = 0.1
forcing_coef = 0.5


def stencil_kernel(
    diff_ref, cor_ref, state_ref, aux_ref, high_ref, low_ref, north_ref, south_ref,
    out_ref, source, first, second,
):
    fields, levels, rows, lanes = out_ref.shape
    channels = fields * levels
    tall, wide = source.shape[1], source.shape[2]
    width = high_ref.shape[1]

    def assemble(ch, inner):
        source[ch, :rows, :lanes] = inner
        source[ch, rows:, :] = jnp.zeros((tall - rows, wide), jnp.float32)
        source[ch, :rows, lanes:] = jnp.zeros((rows, wide - lanes), jnp.float32)
        source[ch, rows : rows + width, :lanes] = high_ref[ch]
        source[ch, tall - width :, :lanes] = low_ref[ch]
        source[ch, :, lanes : lanes + width] = north_ref[ch]
        source[ch, :, wide - width :] = south_ref[ch]

    def assemble_state(ch, carry):
        assemble(ch, state_ref[ch])
        return carry

    def assemble_aux(index, carry):
        assemble(channels + index, aux_ref[index])
        return carry

    lax.fori_loop(0, channels, assemble_state, 0, unroll=4)
    lax.fori_loop(0, aux_ref.shape[0], assemble_aux, 0, unroll=True)

    def aux(index):
        return source[channels + index]

    def one_step(read, write, last):
        def crop(value):
            return value[:rows, :lanes] if last else value

        def level(l, cum):
            up = jnp.maximum(l - 1, 0)
            down = jnp.minimum(l + 1, levels - 1)
            here = [read(f * levels + l) for f in range(fields)]
            density = haline_coef * here[3] - thermal_coef * here[2]
            cum = cum + density
            pressure = cum - 0.5 * density
            zonal = crop(here[0])
            meridional = crop(here[1])
            top = jnp.where(l == 0, forcing_coef, 0.0)
            diff = diff_ref[l]
            coriolis = crop(jnp.broadcast_to(cor_ref[...], (tall, wide)))
            for f in range(fields):
                whole = here[f]
                center = crop(whole)
                east = crop(pltpu.roll(whole, tall - 1, 0))
                west = crop(pltpu.roll(whole, 1, 0))
                north = crop(pltpu.roll(whole, wide - 1, 1))
                south = crop(pltpu.roll(whole, 1, 1))
                advection = -advect_coef * 0.5 * (zonal * (east - west) + meridional * (north - south))
                laplace = diff * (east + west + north + south - 4.0 * center)
                mixing = vertical_coef * (
                    crop(read(f * levels + up)) + crop(read(f * levels + down)) - 2.0 * center
                )
                total = advection + laplace + mixing
                if f == 0:
                    grad = crop(pltpu.roll(pressure, tall - 1, 0)) - crop(pltpu.roll(pressure, 1, 0))
                    total = total + (coriolis * meridional - pressure_coef * 0.5 * grad)
                if f == 1:
                    grad = crop(pltpu.roll(pressure, wide - 1, 1)) - crop(pltpu.roll(pressure, 1, 1))
                    total = total + (-coriolis * zonal - pressure_coef * 0.5 * grad)
                total = total + top * crop(aux(f))
                write(f, l, center + crop(aux(fields)) * total)
            return cum

        lax.fori_loop(0, levels, level, jnp.zeros((tall, wide), jnp.float32), unroll=True)

    def read_src(ch):
        return source[ch]

    def read_first(ch):
        return first[ch]

    def read_second(ch):
        return second[ch]

    def write_first(f, l, value):
        first[f * levels + l] = value

    def write_second(f, l, value):
        second[f * levels + l] = value

    def write_out(f, l, value):
        out_ref[f, l] = value

    writers = [write_first, write_second]
    for repeat in range(STEPS):
        write = write_out if repeat == STEPS - 1 else writers[repeat % 2]
        read = read_src if repeat == 0 else (read_first if repeat % 2 == 1 else read_second)
        one_step(read, write, repeat == STEPS - 1)


def run_steps(state, aux, high, low, north, south, coriolis, diffusivity, out_shape):
    channels = state.shape[0] + aux.shape[0]
    rows, lanes = state.shape[1], state.shape[2]
    width = high.shape[1]
    tall = -(-(rows + 2 * width) // 8) * 8
    wide = -(-(lanes + 2 * width) // 128) * 128
    vmem = pl.BlockSpec(memory_space=pltpu.VMEM)
    return pl.pallas_call(
        stencil_kernel,
        out_shape=jax.ShapeDtypeStruct(out_shape, jnp.float32),
        in_specs=[pl.BlockSpec(memory_space=pltpu.SMEM)] + [vmem] * 7,
        out_specs=vmem,
        scratch_shapes=[
            pltpu.VMEM((channels, tall, wide), jnp.float32),
            pltpu.VMEM((state.shape[0], tall, wide), jnp.float32),
            pltpu.VMEM((state.shape[0], tall, wide), jnp.float32),
        ],
    )(diffusivity, coriolis, state, aux, high, low, north, south)


def shifted(block, axis, dim, width):
    count = lax.axis_size(axis)
    forward = [(i, i + 1) for i in range(count - 1)]
    backward = [(target, source) for source, target in forward]
    size = block.shape[dim]
    low = lax.ppermute(lax.slice_in_dim(block, size - width, None, axis=dim), axis, forward)
    high = lax.ppermute(lax.slice_in_dim(block, 0, width, axis=dim), axis, backward)
    return low, high


def lat_factor(first_cell, count, lat_total):
    latitude = (first_cell + jnp.arange(count, dtype=jnp.int32)).astype(jnp.float32)
    return coriolis_coef * (2.0 * (latitude + 0.5) / lat_total - 1.0)


def per_device(
    atm_flux,
    remap_weights,
    tile_slots,
    need_blocks,
    send_blocks,
    ocean_state,
    land_mask,
    diffusivity,
):
    blocks_here = atm_flux.shape[1]
    block_width = atm_flux.shape[2]
    owners = lax.axis_size("ox")
    capacity = send_blocks.shape[1]
    slots = owners * capacity
    block_line = jnp.arange(blocks_here, dtype=jnp.int32)
    to_block = send_blocks[:, :, None] == block_line[None, None, :]
    outgoing = jnp.broadcast_to(atm_flux[None], (owners,) + atm_flux.shape)
    incoming = lax.all_to_all(outgoing, "ox", 0, 0, tiled=True)
    owner_of = tile_slots // capacity
    block_of = need_blocks.reshape(-1)[tile_slots]
    picks = incoming[owner_of, :, block_of, :]
    forcing = jnp.einsum("tkfa,tkra->ftr", picks, remap_weights, preferred_element_type=jnp.float32)
    fields, levels, rows, lat_cells = ocean_state.shape
    lat_total = lat_cells * lax.axis_size("oy")
    lat_start = lax.axis_index("oy") * lat_cells
    wetness = land_mask.astype(jnp.float32)
    inner = ocean_state.reshape(fields * levels, rows, lat_cells)
    aux = jnp.concatenate([forcing, wetness[None]], axis=0)
    packed = jnp.concatenate([inner, aux], axis=0)
    tall = -(-(rows + 2 * STEPS) // 8) * 8
    wide = -(-(lat_cells + 2 * STEPS) // 128) * 128
    low, high = shifted(packed, "ox", 1, STEPS)
    gap = jnp.zeros((packed.shape[0], tall - rows - 2 * STEPS, STEPS), jnp.float32)
    south_edge = jnp.concatenate(
        [packed[:, :, -STEPS:], high[:, :, -STEPS:], gap, low[:, :, -STEPS:]], axis=1
    )
    north_edge = jnp.concatenate(
        [packed[:, :, :STEPS], high[:, :, :STEPS], gap, low[:, :, :STEPS]], axis=1
    )
    count = lax.axis_size("oy")
    forward = [(i, i + 1) for i in range(count - 1)]
    backward = [(target, source) for source, target in forward]
    south = lax.ppermute(south_edge, "oy", forward)
    north = lax.ppermute(north_edge, "oy", backward)
    lane = jnp.arange(wide, dtype=jnp.int32)
    offset = jnp.where(lane < lat_cells + STEPS, lane, lane - wide)
    latitude = (lat_start + offset).astype(jnp.float32)
    coriolis_wide = (coriolis_coef * (2.0 * (latitude + 0.5) / lat_total - 1.0))[None, :]
    state = run_steps(inner, aux, high, low, north, south, coriolis_wide, diffusivity, ocean_state.shape)
    surface = state[2, 0].astype(jnp.bfloat16)
    pieces = jnp.einsum("tkra,tr->tka", remap_weights, surface, preferred_element_type=jnp.float32)
    slot_line = jnp.arange(slots, dtype=jnp.int32)
    to_slot = (tile_slots[:, :, None] == slot_line[None, None, :]).astype(jnp.float32)
    per_slot = jnp.einsum("tks,tka->sa", to_slot, pieces, precision=lax.Precision.HIGHEST)
    per_slot = per_slot.reshape(owners, capacity, block_width)
    returned = lax.all_to_all(per_slot, "ox", 0, 0, tiled=True)
    atmos_surface = jnp.einsum(
        "isb,isa->ba", to_block.astype(jnp.float32), returned, precision=lax.Precision.HIGHEST
    )
    return (state, atmos_surface)


def solution(mesh):
    return jax.shard_map(
        per_device,
        mesh=mesh,
        in_specs=(
            P(None, "oy", "ox"),
            P("ox", "oy", None, None),
            P("ox", "oy"),
            P("ox", "oy"),
            P("ox", "oy"),
            P(None, None, "ox", "oy"),
            P("ox", "oy"),
            P(),
        ),
        out_specs=(P(None, None, "ox", "oy"), P("oy", "ox")),
        check_vma=False,
    )
```

```python
import jax
import jax.numpy as jnp
from jax import lax
from jax.experimental import pallas as pl
from jax.experimental.pallas import tpu as pltpu
from jax.sharding import PartitionSpec as P

STEPS = 3


advect_coef = 0.25
pressure_coef = 0.1
thermal_coef = 0.2
haline_coef = 0.8
coriolis_coef = 0.5
vertical_coef = 0.1
forcing_coef = 0.5


def stencil_kernel(
    diff_ref, cor_ref, state_ref, aux_ref, high_ref, low_ref, north_ref, south_ref,
    out_ref, source, first, second,
):
    fields, levels, rows, lanes = out_ref.shape
    channels = fields * levels
    tall, wide = source.shape[1], source.shape[2]
    width = high_ref.shape[1]

    north_rows = [north_ref[s] for s in range(width)]
    south_rows = [south_ref[s] for s in range(width)]
    spread = north_ref.shape[2]
    far = wide - lanes - width

    def assemble(ch, inner):
        source[ch, :rows, :lanes] = inner
        source[ch, rows:, :] = jnp.zeros((tall - rows, wide), jnp.float32)
        source[ch, :rows, lanes:] = jnp.zeros((rows, wide - lanes), jnp.float32)
        source[ch, rows : rows + width, :lanes] = high_ref[ch]
        source[ch, tall - width :, :lanes] = low_ref[ch]
        for s in range(width):
            moved = pltpu.roll(north_rows[s], (s - ch + spread) % spread, 1)
            source[ch, :, lanes + s : lanes + s + 1] = moved[:, s : s + 1]
            moved = pltpu.roll(south_rows[s], (far + s - ch + spread) % spread, 1)
            source[ch, :, lanes + far + s : lanes + far + s + 1] = moved[:, far + s : far + s + 1]

    def assemble_state(ch, carry):
        assemble(ch, state_ref[ch])
        return carry

    def assemble_aux(index, carry):
        assemble(channels + index, aux_ref[index])
        return carry

    lax.fori_loop(0, channels, assemble_state, 0, unroll=4)
    lax.fori_loop(0, aux_ref.shape[0], assemble_aux, 0, unroll=True)

    def aux(index):
        return source[channels + index]

    def one_step(read, write, last):
        def crop(value):
            return value[:rows, :lanes] if last else value

        def level(l, cum):
            up = jnp.maximum(l - 1, 0)
            down = jnp.minimum(l + 1, levels - 1)
            here = [read(f * levels + l) for f in range(fields)]
            density = haline_coef * here[3] - thermal_coef * here[2]
            cum = cum + density
            pressure = cum - 0.5 * density
            zonal = crop(here[0])
            meridional = crop(here[1])
            top = jnp.where(l == 0, forcing_coef, 0.0)
            diff = diff_ref[l]
            coriolis = crop(jnp.broadcast_to(cor_ref[...], (tall, wide)))
            for f in range(fields):
                whole = here[f]
                center = crop(whole)
                east = crop(pltpu.roll(whole, tall - 1, 0))
                west = crop(pltpu.roll(whole, 1, 0))
                north = crop(pltpu.roll(whole, wide - 1, 1))
                south = crop(pltpu.roll(whole, 1, 1))
                advection = -advect_coef * 0.5 * (zonal * (east - west) + meridional * (north - south))
                laplace = diff * (east + west + north + south - 4.0 * center)
                mixing = vertical_coef * (
                    crop(read(f * levels + up)) + crop(read(f * levels + down)) - 2.0 * center
                )
                total = advection + laplace + mixing
                if f == 0:
                    grad = crop(pltpu.roll(pressure, tall - 1, 0)) - crop(pltpu.roll(pressure, 1, 0))
                    total = total + (coriolis * meridional - pressure_coef * 0.5 * grad)
                if f == 1:
                    grad = crop(pltpu.roll(pressure, wide - 1, 1)) - crop(pltpu.roll(pressure, 1, 1))
                    total = total + (-coriolis * zonal - pressure_coef * 0.5 * grad)
                total = total + top * crop(aux(f))
                write(f, l, center + crop(aux(fields)) * total)
            return cum

        lax.fori_loop(0, levels, level, jnp.zeros((tall, wide), jnp.float32), unroll=True)

    def read_src(ch):
        return source[ch]

    def read_first(ch):
        return first[ch]

    def read_second(ch):
        return second[ch]

    def write_first(f, l, value):
        first[f * levels + l] = value

    def write_second(f, l, value):
        second[f * levels + l] = value

    def write_out(f, l, value):
        out_ref[f, l] = value

    writers = [write_first, write_second]
    for repeat in range(STEPS):
        write = write_out if repeat == STEPS - 1 else writers[repeat % 2]
        read = read_src if repeat == 0 else (read_first if repeat % 2 == 1 else read_second)
        one_step(read, write, repeat == STEPS - 1)


def run_steps(state, aux, high, low, north, south, coriolis, diffusivity, out_shape):
    channels = state.shape[0] + aux.shape[0]
    rows, lanes = state.shape[1], state.shape[2]
    width = high.shape[1]
    tall = -(-(rows + 2 * width) // 8) * 8
    wide = -(-(lanes + 2 * width) // 128) * 128
    vmem = pl.BlockSpec(memory_space=pltpu.VMEM)
    return pl.pallas_call(
        stencil_kernel,
        out_shape=jax.ShapeDtypeStruct(out_shape, jnp.float32),
        in_specs=[pl.BlockSpec(memory_space=pltpu.SMEM)] + [vmem] * 7,
        out_specs=vmem,
        scratch_shapes=[
            pltpu.VMEM((channels, tall, wide), jnp.float32),
            pltpu.VMEM((state.shape[0], tall, wide), jnp.float32),
            pltpu.VMEM((state.shape[0], tall, wide), jnp.float32),
        ],
    )(diffusivity, coriolis, state, aux, high, low, north, south)


def shifted(block, axis, dim, width):
    count = lax.axis_size(axis)
    forward = [(i, i + 1) for i in range(count - 1)]
    backward = [(target, source) for source, target in forward]
    size = block.shape[dim]
    low = lax.ppermute(lax.slice_in_dim(block, size - width, None, axis=dim), axis, forward)
    high = lax.ppermute(lax.slice_in_dim(block, 0, width, axis=dim), axis, backward)
    return low, high


def lat_factor(first_cell, count, lat_total):
    latitude = (first_cell + jnp.arange(count, dtype=jnp.int32)).astype(jnp.float32)
    return coriolis_coef * (2.0 * (latitude + 0.5) / lat_total - 1.0)


def per_device(
    atm_flux,
    remap_weights,
    tile_slots,
    need_blocks,
    send_blocks,
    ocean_state,
    land_mask,
    diffusivity,
):
    blocks_here = atm_flux.shape[1]
    block_width = atm_flux.shape[2]
    owners = lax.axis_size("ox")
    capacity = send_blocks.shape[1]
    slots = owners * capacity
    block_line = jnp.arange(blocks_here, dtype=jnp.int32)
    to_block = send_blocks[:, :, None] == block_line[None, None, :]
    outgoing = jnp.broadcast_to(atm_flux[None], (owners,) + atm_flux.shape)
    incoming = lax.all_to_all(outgoing, "ox", 0, 0, tiled=True)
    owner_of = tile_slots // capacity
    block_of = need_blocks.reshape(-1)[tile_slots]
    picks = incoming[owner_of, :, block_of, :]
    forcing = jnp.einsum("tkfa,tkra->ftr", picks, remap_weights, preferred_element_type=jnp.float32)
    fields, levels, rows, lat_cells = ocean_state.shape
    lat_total = lat_cells * lax.axis_size("oy")
    lat_start = lax.axis_index("oy") * lat_cells
    wetness = land_mask.astype(jnp.float32)
    inner = ocean_state.reshape(fields * levels, rows, lat_cells)
    aux = jnp.concatenate([forcing, wetness[None]], axis=0)
    packed = jnp.concatenate([inner, aux], axis=0)
    tall = -(-(rows + 2 * STEPS) // 8) * 8
    wide = -(-(lat_cells + 2 * STEPS) // 128) * 128
    low, high = shifted(packed, "ox", 1, STEPS)
    gap = jnp.zeros((packed.shape[0], tall - rows - 2 * STEPS, STEPS), jnp.float32)
    south_edge = jnp.concatenate(
        [packed[:, :, -STEPS:], high[:, :, -STEPS:], gap, low[:, :, -STEPS:]], axis=1
    )
    north_edge = jnp.concatenate(
        [packed[:, :, :STEPS], high[:, :, :STEPS], gap, low[:, :, :STEPS]], axis=1
    )
    count = lax.axis_size("oy")
    forward = [(i, i + 1) for i in range(count - 1)]
    backward = [(target, source) for source, target in forward]
    spread = -(-packed.shape[0] // 128) * 128
    lane_pad = ((0, 0), (0, 0), (0, spread - packed.shape[0]))
    south_edge = jnp.pad(jnp.transpose(south_edge, (2, 1, 0)), lane_pad)
    north_edge = jnp.pad(jnp.transpose(north_edge, (2, 1, 0)), lane_pad)
    south = lax.ppermute(south_edge, "oy", forward)
    north = lax.ppermute(north_edge, "oy", backward)
    lane = jnp.arange(wide, dtype=jnp.int32)
    offset = jnp.where(lane < lat_cells + STEPS, lane, lane - wide)
    latitude = (lat_start + offset).astype(jnp.float32)
    coriolis_wide = (coriolis_coef * (2.0 * (latitude + 0.5) / lat_total - 1.0))[None, :]
    state = run_steps(inner, aux, high, low, north, south, coriolis_wide, diffusivity, ocean_state.shape)
    surface = state[2, 0].astype(jnp.bfloat16)
    pieces = jnp.einsum("tkra,tr->tka", remap_weights, surface, preferred_element_type=jnp.float32)
    slot_line = jnp.arange(slots, dtype=jnp.int32)
    to_slot = (tile_slots[:, :, None] == slot_line[None, None, :]).astype(jnp.float32)
    per_slot = jnp.einsum("tks,tka->sa", to_slot, pieces, precision=lax.Precision.HIGHEST)
    per_slot = per_slot.reshape(owners, capacity, block_width)
    returned = lax.all_to_all(per_slot, "ox", 0, 0, tiled=True)
    atmos_surface = jnp.einsum(
        "isb,isa->ba", to_block.astype(jnp.float32), returned, precision=lax.Precision.HIGHEST
    )
    return (state, atmos_surface)


def solution(mesh):
    return jax.shard_map(
        per_device,
        mesh=mesh,
        in_specs=(
            P(None, "oy", "ox"),
            P("ox", "oy", None, None),
            P("ox", "oy"),
            P("ox", "oy"),
            P("ox", "oy"),
            P(None, None, "ox", "oy"),
            P("ox", "oy"),
            P(),
        ),
        out_specs=(P(None, None, "ox", "oy"), P("oy", "ox")),
        check_vma=False,
    )
```

```python
import functools

import jax
import jax.numpy as jnp
from jax import lax
from jax.experimental import pallas as pl
from jax.experimental.pallas import tpu as pltpu
from jax.sharding import PartitionSpec as P

STEPS = 3


advect_coef = 0.25
pressure_coef = 0.1
thermal_coef = 0.2
haline_coef = 0.8
coriolis_coef = 0.5
vertical_coef = 0.1
forcing_coef = 0.5


def stencil_kernel(
    diff_ref, cor_ref, state_ref, aux_ref, high_ref, low_ref, north_ref, south_ref,
    out_ref, source, first, second, surface_only,
):
    fields = 4
    channels, rows, lanes = state_ref.shape
    levels = channels // fields
    tall, wide = source.shape[1], source.shape[2]
    width = high_ref.shape[1]

    def assemble(ch, inner):
        source[ch, :rows, :lanes] = inner
        source[ch, rows:, :] = jnp.zeros((tall - rows, wide), jnp.float32)
        source[ch, :rows, lanes:] = jnp.zeros((rows, wide - lanes), jnp.float32)
        source[ch, rows : rows + width, :lanes] = high_ref[ch]
        source[ch, tall - width :, :lanes] = low_ref[ch]
        source[ch, :, lanes : lanes + width] = north_ref[ch]
        source[ch, :, wide - width :] = south_ref[ch]

    def assemble_state(ch, carry):
        assemble(ch, state_ref[ch])
        return carry

    def assemble_aux(index, carry):
        assemble(channels + index, aux_ref[index])
        return carry

    if surface_only:
        for f in range(fields):
            for l in range(min(levels, STEPS + 1)):
                assemble(f * levels + l, state_ref[f * levels + l])
    else:
        lax.fori_loop(0, channels, assemble_state, 0, unroll=4)
    lax.fori_loop(0, aux_ref.shape[0], assemble_aux, 0, unroll=True)

    def aux(index):
        return source[channels + index]

    def one_step(read, write, last, count):
        def crop(value):
            return value[:rows, :lanes] if last else value

        def level(l, cum):
            up = jnp.maximum(l - 1, 0)
            down = jnp.minimum(l + 1, levels - 1)
            here = [read(f * levels + l) for f in range(fields)]
            density = haline_coef * here[3] - thermal_coef * here[2]
            cum = cum + density
            pressure = cum - 0.5 * density
            zonal = crop(here[0])
            meridional = crop(here[1])
            top = jnp.where(l == 0, forcing_coef, 0.0)
            diff = diff_ref[l]
            coriolis = crop(jnp.broadcast_to(cor_ref[...], (tall, wide)))
            for f in range(fields):
                whole = here[f]
                center = crop(whole)
                east = crop(pltpu.roll(whole, tall - 1, 0))
                west = crop(pltpu.roll(whole, 1, 0))
                north = crop(pltpu.roll(whole, wide - 1, 1))
                south = crop(pltpu.roll(whole, 1, 1))
                advection = -advect_coef * 0.5 * (zonal * (east - west) + meridional * (north - south))
                laplace = diff * (east + west + north + south - 4.0 * center)
                mixing = vertical_coef * (
                    crop(read(f * levels + up)) + crop(read(f * levels + down)) - 2.0 * center
                )
                total = advection + laplace + mixing
                if f == 0:
                    grad = crop(pltpu.roll(pressure, tall - 1, 0)) - crop(pltpu.roll(pressure, 1, 0))
                    total = total + (coriolis * meridional - pressure_coef * 0.5 * grad)
                if f == 1:
                    grad = crop(pltpu.roll(pressure, wide - 1, 1)) - crop(pltpu.roll(pressure, 1, 1))
                    total = total + (-coriolis * zonal - pressure_coef * 0.5 * grad)
                total = total + top * crop(aux(f))
                write(f, l, center + crop(aux(fields)) * total)
            return cum

        lax.fori_loop(0, count, level, jnp.zeros((tall, wide), jnp.float32), unroll=True)

    def read_src(ch):
        return source[ch]

    def read_first(ch):
        return first[ch]

    def read_second(ch):
        return second[ch]

    def write_first(f, l, value):
        first[f * levels + l] = value

    def write_second(f, l, value):
        second[f * levels + l] = value

    def write_out(f, l, value):
        if not surface_only:
            out_ref[f, l] = value
        elif f == 2:
            out_ref[...] = value

    writers = [write_first, write_second]
    for repeat in range(STEPS):
        write = write_out if repeat == STEPS - 1 else writers[repeat % 2]
        read = read_src if repeat == 0 else (read_first if repeat % 2 == 1 else read_second)
        count = min(levels, STEPS - repeat) if surface_only else levels
        one_step(read, write, repeat == STEPS - 1, count)


def run_steps(state, aux, high, low, north, south, coriolis, diffusivity, out_shape):
    channels = state.shape[0] + aux.shape[0]
    rows, lanes = state.shape[1], state.shape[2]
    width = high.shape[1]
    tall = -(-(rows + 2 * width) // 8) * 8
    wide = -(-(lanes + 2 * width) // 128) * 128
    vmem = pl.BlockSpec(memory_space=pltpu.VMEM)
    operands = (diffusivity, coriolis, state, aux, high, low, north, south)

    def call(surface_only, shape):
        return pl.pallas_call(
            functools.partial(stencil_kernel, surface_only=surface_only),
            out_shape=jax.ShapeDtypeStruct(shape, jnp.float32),
            in_specs=[pl.BlockSpec(memory_space=pltpu.SMEM)] + [vmem] * 7,
            out_specs=vmem,
            scratch_shapes=[
                pltpu.VMEM((channels, tall, wide), jnp.float32),
                pltpu.VMEM((state.shape[0], tall, wide), jnp.float32),
                pltpu.VMEM((state.shape[0], tall, wide), jnp.float32),
            ],
        )(*operands)

    return call(True, (rows, lanes)), call(False, out_shape)


def shifted(block, axis, dim, width):
    count = lax.axis_size(axis)
    forward = [(i, i + 1) for i in range(count - 1)]
    backward = [(target, source) for source, target in forward]
    size = block.shape[dim]
    low = lax.ppermute(lax.slice_in_dim(block, size - width, None, axis=dim), axis, forward)
    high = lax.ppermute(lax.slice_in_dim(block, 0, width, axis=dim), axis, backward)
    return low, high


def lat_factor(first_cell, count, lat_total):
    latitude = (first_cell + jnp.arange(count, dtype=jnp.int32)).astype(jnp.float32)
    return coriolis_coef * (2.0 * (latitude + 0.5) / lat_total - 1.0)


def per_device(
    atm_flux,
    remap_weights,
    tile_slots,
    need_blocks,
    send_blocks,
    ocean_state,
    land_mask,
    diffusivity,
):
    blocks_here = atm_flux.shape[1]
    block_width = atm_flux.shape[2]
    owners = lax.axis_size("ox")
    capacity = send_blocks.shape[1]
    slots = owners * capacity
    block_line = jnp.arange(blocks_here, dtype=jnp.int32)
    to_block = send_blocks[:, :, None] == block_line[None, None, :]
    outgoing = jnp.broadcast_to(atm_flux[None], (owners,) + atm_flux.shape)
    incoming = lax.all_to_all(outgoing, "ox", 0, 0, tiled=True)
    owner_of = tile_slots // capacity
    block_of = need_blocks.reshape(-1)[tile_slots]
    picks = incoming[owner_of, :, block_of, :]
    forcing = jnp.einsum("tkfa,tkra->ftr", picks, remap_weights, preferred_element_type=jnp.float32)
    fields, levels, rows, lat_cells = ocean_state.shape
    lat_total = lat_cells * lax.axis_size("oy")
    lat_start = lax.axis_index("oy") * lat_cells
    wetness = land_mask.astype(jnp.float32)
    inner = ocean_state.reshape(fields * levels, rows, lat_cells)
    aux = jnp.concatenate([forcing, wetness[None]], axis=0)
    packed = jnp.concatenate([inner, aux], axis=0)
    tall = -(-(rows + 2 * STEPS) // 8) * 8
    wide = -(-(lat_cells + 2 * STEPS) // 128) * 128
    low, high = shifted(packed, "ox", 1, STEPS)
    gap = jnp.zeros((packed.shape[0], tall - rows - 2 * STEPS, STEPS), jnp.float32)
    south_edge = jnp.concatenate(
        [packed[:, :, -STEPS:], high[:, :, -STEPS:], gap, low[:, :, -STEPS:]], axis=1
    )
    north_edge = jnp.concatenate(
        [packed[:, :, :STEPS], high[:, :, :STEPS], gap, low[:, :, :STEPS]], axis=1
    )
    count = lax.axis_size("oy")
    forward = [(i, i + 1) for i in range(count - 1)]
    backward = [(target, source) for source, target in forward]
    south = lax.ppermute(south_edge, "oy", forward)
    north = lax.ppermute(north_edge, "oy", backward)
    lane = jnp.arange(wide, dtype=jnp.int32)
    offset = jnp.where(lane < lat_cells + STEPS, lane, lane - wide)
    latitude = (lat_start + offset).astype(jnp.float32)
    coriolis_wide = (coriolis_coef * (2.0 * (latitude + 0.5) / lat_total - 1.0))[None, :]
    top, state = run_steps(inner, aux, high, low, north, south, coriolis_wide, diffusivity, ocean_state.shape)
    surface = top.astype(jnp.bfloat16)
    pieces = jnp.einsum("tkra,tr->tka", remap_weights, surface, preferred_element_type=jnp.float32)
    slot_line = jnp.arange(slots, dtype=jnp.int32)
    to_slot = (tile_slots[:, :, None] == slot_line[None, None, :]).astype(jnp.float32)
    per_slot = jnp.einsum("tks,tka->sa", to_slot, pieces, precision=lax.Precision.HIGHEST)
    per_slot = per_slot.reshape(owners, capacity, block_width)
    returned = lax.all_to_all(per_slot, "ox", 0, 0, tiled=True)
    atmos_surface = jnp.einsum(
        "isb,isa->ba", to_block.astype(jnp.float32), returned, precision=lax.Precision.HIGHEST
    )
    return (state, atmos_surface)


def solution(mesh):
    return jax.shard_map(
        per_device,
        mesh=mesh,
        in_specs=(
            P(None, "oy", "ox"),
            P("ox", "oy", None, None),
            P("ox", "oy"),
            P("ox", "oy"),
            P("ox", "oy"),
            P(None, None, "ox", "oy"),
            P("ox", "oy"),
            P(),
        ),
        out_specs=(P(None, None, "ox", "oy"), P("oy", "ox")),
        check_vma=False,
    )
```

```python
import functools

import jax
import jax.numpy as jnp
from jax import lax
from jax.experimental import pallas as pl
from jax.experimental.pallas import tpu as pltpu
from jax.sharding import PartitionSpec as P

STEPS = 3


advect_coef = 0.25
pressure_coef = 0.1
thermal_coef = 0.2
haline_coef = 0.8
coriolis_coef = 0.5
vertical_coef = 0.1
forcing_coef = 0.5


def stencil_kernel(
    diff_ref, cor_ref, state_ref, aux_ref, high_ref, low_ref, north_ref, south_ref,
    out_ref, source, first, second, surface_only,
):
    fields = 4
    channels, rows, lanes = state_ref.shape
    levels = channels // fields
    tall, wide = source.shape[1], source.shape[2]
    width = high_ref.shape[1]

    north_rows = [north_ref[s] for s in range(width)]
    south_rows = [south_ref[s] for s in range(width)]

    def assemble(ch, inner):
        source[ch, :rows, :lanes] = inner
        source[ch, rows:, :] = jnp.zeros((tall - rows, wide), jnp.float32)
        source[ch, :rows, lanes:] = jnp.zeros((rows, wide - lanes), jnp.float32)
        source[ch, rows : rows + width, :lanes] = high_ref[ch]
        source[ch, tall - width :, :lanes] = low_ref[ch]
        for s in range(width):
            source[ch, :, lanes + s : lanes + s + 1] = north_rows[s][:, ch : ch + 1]
            far = wide - width + s
            source[ch, :, far : far + 1] = south_rows[s][:, ch : ch + 1]

    if surface_only:
        for f in range(fields):
            for l in range(min(levels, STEPS + 1)):
                assemble(f * levels + l, state_ref[f * levels + l])
    else:
        for ch in range(channels):
            assemble(ch, state_ref[ch])
    for index in range(aux_ref.shape[0]):
        assemble(channels + index, aux_ref[index])

    def aux(index):
        return source[channels + index]

    def one_step(read, write, last, count):
        def crop(value):
            return value[:rows, :lanes] if last else value

        def level(l, cum):
            up = jnp.maximum(l - 1, 0)
            down = jnp.minimum(l + 1, levels - 1)
            here = [read(f * levels + l) for f in range(fields)]
            density = haline_coef * here[3] - thermal_coef * here[2]
            cum = cum + density
            pressure = cum - 0.5 * density
            zonal = crop(here[0])
            meridional = crop(here[1])
            top = jnp.where(l == 0, forcing_coef, 0.0)
            diff = diff_ref[l]
            coriolis = crop(jnp.broadcast_to(cor_ref[...], (tall, wide)))
            for f in range(fields):
                whole = here[f]
                center = crop(whole)
                east = crop(pltpu.roll(whole, tall - 1, 0))
                west = crop(pltpu.roll(whole, 1, 0))
                north = crop(pltpu.roll(whole, wide - 1, 1))
                south = crop(pltpu.roll(whole, 1, 1))
                advection = -advect_coef * 0.5 * (zonal * (east - west) + meridional * (north - south))
                laplace = diff * (east + west + north + south - 4.0 * center)
                mixing = vertical_coef * (
                    crop(read(f * levels + up)) + crop(read(f * levels + down)) - 2.0 * center
                )
                total = advection + laplace + mixing
                if f == 0:
                    grad = crop(pltpu.roll(pressure, tall - 1, 0)) - crop(pltpu.roll(pressure, 1, 0))
                    total = total + (coriolis * meridional - pressure_coef * 0.5 * grad)
                if f == 1:
                    grad = crop(pltpu.roll(pressure, wide - 1, 1)) - crop(pltpu.roll(pressure, 1, 1))
                    total = total + (-coriolis * zonal - pressure_coef * 0.5 * grad)
                total = total + top * crop(aux(f))
                write(f, l, center + crop(aux(fields)) * total)
            return cum

        lax.fori_loop(0, count, level, jnp.zeros((tall, wide), jnp.float32), unroll=True)

    def read_src(ch):
        return source[ch]

    def read_first(ch):
        return first[ch]

    def read_second(ch):
        return second[ch]

    def write_first(f, l, value):
        first[f * levels + l] = value

    def write_second(f, l, value):
        second[f * levels + l] = value

    def write_out(f, l, value):
        if not surface_only:
            out_ref[f, l] = value
        elif f == 2:
            out_ref[...] = value

    writers = [write_first, write_second]
    for repeat in range(STEPS):
        write = write_out if repeat == STEPS - 1 else writers[repeat % 2]
        read = read_src if repeat == 0 else (read_first if repeat % 2 == 1 else read_second)
        count = min(levels, STEPS - repeat) if surface_only else levels
        one_step(read, write, repeat == STEPS - 1, count)


def run_steps(state, aux, high, low, north, south, coriolis, diffusivity, out_shape):
    channels = state.shape[0] + aux.shape[0]
    rows, lanes = state.shape[1], state.shape[2]
    width = high.shape[1]
    tall = -(-(rows + 2 * width) // 8) * 8
    wide = -(-(lanes + 2 * width) // 128) * 128
    vmem = pl.BlockSpec(memory_space=pltpu.VMEM)
    operands = (diffusivity, coriolis, state, aux, high, low, north, south)

    def call(surface_only, shape):
        return pl.pallas_call(
            functools.partial(stencil_kernel, surface_only=surface_only),
            out_shape=jax.ShapeDtypeStruct(shape, jnp.float32),
            in_specs=[pl.BlockSpec(memory_space=pltpu.SMEM)] + [vmem] * 7,
            out_specs=vmem,
            scratch_shapes=[
                pltpu.VMEM((channels, tall, wide), jnp.float32),
                pltpu.VMEM((state.shape[0], tall, wide), jnp.float32),
                pltpu.VMEM((state.shape[0], tall, wide), jnp.float32),
            ],
        )(*operands)

    return call(True, (rows, lanes)), call(False, out_shape)


def shifted(block, axis, dim, width):
    count = lax.axis_size(axis)
    forward = [(i, i + 1) for i in range(count - 1)]
    backward = [(target, source) for source, target in forward]
    size = block.shape[dim]
    low = lax.ppermute(lax.slice_in_dim(block, size - width, None, axis=dim), axis, forward)
    high = lax.ppermute(lax.slice_in_dim(block, 0, width, axis=dim), axis, backward)
    return low, high


def lat_factor(first_cell, count, lat_total):
    latitude = (first_cell + jnp.arange(count, dtype=jnp.int32)).astype(jnp.float32)
    return coriolis_coef * (2.0 * (latitude + 0.5) / lat_total - 1.0)


def per_device(
    atm_flux,
    remap_weights,
    tile_slots,
    need_blocks,
    send_blocks,
    ocean_state,
    land_mask,
    diffusivity,
):
    blocks_here = atm_flux.shape[1]
    block_width = atm_flux.shape[2]
    owners = lax.axis_size("ox")
    capacity = send_blocks.shape[1]
    slots = owners * capacity
    block_line = jnp.arange(blocks_here, dtype=jnp.int32)
    to_block = send_blocks[:, :, None] == block_line[None, None, :]
    outgoing = jnp.broadcast_to(atm_flux[None], (owners,) + atm_flux.shape)
    incoming = lax.all_to_all(outgoing, "ox", 0, 0, tiled=True)
    owner_of = tile_slots // capacity
    block_of = need_blocks.reshape(-1)[tile_slots]
    picks = incoming[owner_of, :, block_of, :]
    forcing = jnp.einsum("tkfa,tkra->ftr", picks, remap_weights, preferred_element_type=jnp.float32)
    fields, levels, rows, lat_cells = ocean_state.shape
    lat_total = lat_cells * lax.axis_size("oy")
    lat_start = lax.axis_index("oy") * lat_cells
    wetness = land_mask.astype(jnp.float32)
    inner = ocean_state.reshape(fields * levels, rows, lat_cells)
    aux = jnp.concatenate([forcing, wetness[None]], axis=0)
    packed = jnp.concatenate([inner, aux], axis=0)
    tall = -(-(rows + 2 * STEPS) // 8) * 8
    wide = -(-(lat_cells + 2 * STEPS) // 128) * 128
    low, high = shifted(packed, "ox", 1, STEPS)
    gap = jnp.zeros((packed.shape[0], tall - rows - 2 * STEPS, STEPS), jnp.float32)
    south_edge = jnp.concatenate(
        [packed[:, :, -STEPS:], high[:, :, -STEPS:], gap, low[:, :, -STEPS:]], axis=1
    )
    north_edge = jnp.concatenate(
        [packed[:, :, :STEPS], high[:, :, :STEPS], gap, low[:, :, :STEPS]], axis=1
    )
    count = lax.axis_size("oy")
    forward = [(i, i + 1) for i in range(count - 1)]
    backward = [(target, source) for source, target in forward]
    south = jnp.transpose(lax.ppermute(south_edge, "oy", forward), (2, 1, 0))
    north = jnp.transpose(lax.ppermute(north_edge, "oy", backward), (2, 1, 0))
    lane = jnp.arange(wide, dtype=jnp.int32)
    offset = jnp.where(lane < lat_cells + STEPS, lane, lane - wide)
    latitude = (lat_start + offset).astype(jnp.float32)
    coriolis_wide = (coriolis_coef * (2.0 * (latitude + 0.5) / lat_total - 1.0))[None, :]
    top, state = run_steps(inner, aux, high, low, north, south, coriolis_wide, diffusivity, ocean_state.shape)
    surface = top.astype(jnp.bfloat16)
    pieces = jnp.einsum("tkra,tr->tka", remap_weights, surface, preferred_element_type=jnp.float32)
    slot_line = jnp.arange(slots, dtype=jnp.int32)
    to_slot = (tile_slots[:, :, None] == slot_line[None, None, :]).astype(jnp.float32)
    per_slot = jnp.einsum("tks,tka->sa", to_slot, pieces, precision=lax.Precision.HIGHEST)
    per_slot = per_slot.reshape(owners, capacity, block_width)
    returned = lax.all_to_all(per_slot, "ox", 0, 0, tiled=True)
    atmos_surface = jnp.einsum(
        "isb,isa->ba", to_block.astype(jnp.float32), returned, precision=lax.Precision.HIGHEST
    )
    return (state, atmos_surface)


def solution(mesh):
    return jax.shard_map(
        per_device,
        mesh=mesh,
        in_specs=(
            P(None, "oy", "ox"),
            P("ox", "oy", None, None),
            P("ox", "oy"),
            P("ox", "oy"),
            P("ox", "oy"),
            P(None, None, "ox", "oy"),
            P("ox", "oy"),
            P(),
        ),
        out_specs=(P(None, None, "ox", "oy"), P("oy", "ox")),
        check_vma=False,
    )
```

```python
import functools

import jax
import jax.numpy as jnp
from jax import lax
from jax.experimental import pallas as pl
from jax.experimental.layout import Layout, with_layout_constraint
from jax.experimental.pallas import tpu as pltpu
from jax.sharding import PartitionSpec as P

STEPS = 3


advect_coef = 0.25
pressure_coef = 0.1
thermal_coef = 0.2
haline_coef = 0.8
coriolis_coef = 0.5
vertical_coef = 0.1
forcing_coef = 0.5


def stencil_kernel(
    diff_ref, cor_ref, state_ref, aux_ref, high_ref, low_ref, north_ref, south_ref,
    out_ref, source, first, second, surface_only,
):
    fields = 4
    channels, rows, lanes = state_ref.shape
    levels = channels // fields
    tall, wide = source.shape[1], source.shape[2]
    width = high_ref.shape[1]

    north_rows = [north_ref[s] for s in range(width)]
    south_rows = [south_ref[s] for s in range(width)]

    def assemble(ch, inner):
        source[ch, :rows, :lanes] = inner
        source[ch, rows:, :] = jnp.zeros((tall - rows, wide), jnp.float32)
        source[ch, :rows, lanes:] = jnp.zeros((rows, wide - lanes), jnp.float32)
        source[ch, rows : rows + width, :lanes] = high_ref[ch]
        source[ch, tall - width :, :lanes] = low_ref[ch]
        for s in range(width):
            source[ch, :, lanes + s : lanes + s + 1] = north_rows[s][:, ch : ch + 1]
            far = wide - width + s
            source[ch, :, far : far + 1] = south_rows[s][:, ch : ch + 1]

    if surface_only:
        for f in range(fields):
            for l in range(min(levels, STEPS + 1)):
                assemble(f * levels + l, state_ref[f * levels + l])
    else:
        for ch in range(channels):
            assemble(ch, state_ref[ch])
    for index in range(aux_ref.shape[0]):
        assemble(channels + index, aux_ref[index])

    def aux(index):
        return source[channels + index]

    def one_step(read, write, last, count):
        def crop(value):
            return value[:rows, :lanes] if last else value

        def level(l, cum):
            up = jnp.maximum(l - 1, 0)
            down = jnp.minimum(l + 1, levels - 1)
            here = [read(f * levels + l) for f in range(fields)]
            density = haline_coef * here[3] - thermal_coef * here[2]
            cum = cum + density
            pressure = cum - 0.5 * density
            zonal = crop(here[0])
            meridional = crop(here[1])
            top = jnp.where(l == 0, forcing_coef, 0.0)
            diff = diff_ref[l]
            coriolis = crop(jnp.broadcast_to(cor_ref[...], (tall, wide)))
            for f in range(fields):
                whole = here[f]
                center = crop(whole)
                east = crop(pltpu.roll(whole, tall - 1, 0))
                west = crop(pltpu.roll(whole, 1, 0))
                north = crop(pltpu.roll(whole, wide - 1, 1))
                south = crop(pltpu.roll(whole, 1, 1))
                advection = -advect_coef * 0.5 * (zonal * (east - west) + meridional * (north - south))
                laplace = diff * (east + west + north + south - 4.0 * center)
                mixing = vertical_coef * (
                    crop(read(f * levels + up)) + crop(read(f * levels + down)) - 2.0 * center
                )
                total = advection + laplace + mixing
                if f == 0:
                    grad = crop(pltpu.roll(pressure, tall - 1, 0)) - crop(pltpu.roll(pressure, 1, 0))
                    total = total + (coriolis * meridional - pressure_coef * 0.5 * grad)
                if f == 1:
                    grad = crop(pltpu.roll(pressure, wide - 1, 1)) - crop(pltpu.roll(pressure, 1, 1))
                    total = total + (-coriolis * zonal - pressure_coef * 0.5 * grad)
                total = total + top * crop(aux(f))
                write(f, l, center + crop(aux(fields)) * total)
            return cum

        lax.fori_loop(0, count, level, jnp.zeros((tall, wide), jnp.float32), unroll=True)

    def read_src(ch):
        return source[ch]

    def read_first(ch):
        return first[ch]

    def read_second(ch):
        return second[ch]

    def write_first(f, l, value):
        first[f * levels + l] = value

    def write_second(f, l, value):
        second[f * levels + l] = value

    def write_out(f, l, value):
        if not surface_only:
            out_ref[f, l] = value
        elif f == 2:
            out_ref[...] = value

    writers = [write_first, write_second]
    for repeat in range(STEPS):
        write = write_out if repeat == STEPS - 1 else writers[repeat % 2]
        read = read_src if repeat == 0 else (read_first if repeat % 2 == 1 else read_second)
        count = min(levels, STEPS - repeat) if surface_only else levels
        one_step(read, write, repeat == STEPS - 1, count)


def run_steps(state, aux, high, low, north, south, coriolis, diffusivity, out_shape):
    channels = state.shape[0] + aux.shape[0]
    rows, lanes = state.shape[1], state.shape[2]
    width = high.shape[1]
    tall = -(-(rows + 2 * width) // 8) * 8
    wide = -(-(lanes + 2 * width) // 128) * 128
    vmem = pl.BlockSpec(memory_space=pltpu.VMEM)
    operands = (diffusivity, coriolis, state, aux, high, low, north, south)

    def call(surface_only, shape):
        return pl.pallas_call(
            functools.partial(stencil_kernel, surface_only=surface_only),
            out_shape=jax.ShapeDtypeStruct(shape, jnp.float32),
            in_specs=[pl.BlockSpec(memory_space=pltpu.SMEM)] + [vmem] * 7,
            out_specs=vmem,
            scratch_shapes=[
                pltpu.VMEM((channels, tall, wide), jnp.float32),
                pltpu.VMEM((state.shape[0], tall, wide), jnp.float32),
                pltpu.VMEM((state.shape[0], tall, wide), jnp.float32),
            ],
        )(*operands)

    return call(True, (rows, lanes)), call(False, out_shape)


def shifted(block, axis, dim, width):
    count = lax.axis_size(axis)
    forward = [(i, i + 1) for i in range(count - 1)]
    backward = [(target, source) for source, target in forward]
    size = block.shape[dim]
    low = lax.ppermute(lax.slice_in_dim(block, size - width, None, axis=dim), axis, forward)
    high = lax.ppermute(lax.slice_in_dim(block, 0, width, axis=dim), axis, backward)
    return low, high


def lat_factor(first_cell, count, lat_total):
    latitude = (first_cell + jnp.arange(count, dtype=jnp.int32)).astype(jnp.float32)
    return coriolis_coef * (2.0 * (latitude + 0.5) / lat_total - 1.0)


def per_device(
    atm_flux,
    remap_weights,
    tile_slots,
    need_blocks,
    send_blocks,
    ocean_state,
    land_mask,
    diffusivity,
):
    blocks_here = atm_flux.shape[1]
    block_width = atm_flux.shape[2]
    owners = lax.axis_size("ox")
    capacity = send_blocks.shape[1]
    slots = owners * capacity
    block_line = jnp.arange(blocks_here, dtype=jnp.int32)
    to_block = send_blocks[:, :, None] == block_line[None, None, :]
    outgoing = jnp.broadcast_to(atm_flux[None], (owners,) + atm_flux.shape)
    incoming = lax.all_to_all(outgoing, "ox", 0, 0, tiled=True)
    owner_of = tile_slots // capacity
    block_of = need_blocks.reshape(-1)[tile_slots]
    picks = incoming[owner_of, :, block_of, :]
    forcing = jnp.einsum("tkfa,tkra->ftr", picks, remap_weights, preferred_element_type=jnp.float32)
    fields, levels, rows, lat_cells = ocean_state.shape
    lat_total = lat_cells * lax.axis_size("oy")
    lat_start = lax.axis_index("oy") * lat_cells
    wetness = land_mask.astype(jnp.float32)
    inner = ocean_state.reshape(fields * levels, rows, lat_cells)
    aux = jnp.concatenate([forcing, wetness[None]], axis=0)
    packed = jnp.concatenate([inner, aux], axis=0)
    packed = with_layout_constraint(packed, Layout((0, 1, 2)))
    tall = -(-(rows + 2 * STEPS) // 8) * 8
    wide = -(-(lat_cells + 2 * STEPS) // 128) * 128
    low, high = shifted(packed, "ox", 1, STEPS)
    low = with_layout_constraint(low, Layout((0, 1, 2)))
    high = with_layout_constraint(high, Layout((0, 1, 2)))
    gap = jnp.zeros((packed.shape[0], tall - rows - 2 * STEPS, STEPS), jnp.float32)
    south_edge = jnp.concatenate(
        [packed[:, :, -STEPS:], high[:, :, -STEPS:], gap, low[:, :, -STEPS:]], axis=1
    )
    north_edge = jnp.concatenate(
        [packed[:, :, :STEPS], high[:, :, :STEPS], gap, low[:, :, :STEPS]], axis=1
    )
    count = lax.axis_size("oy")
    forward = [(i, i + 1) for i in range(count - 1)]
    backward = [(target, source) for source, target in forward]
    south = jnp.transpose(lax.ppermute(south_edge, "oy", forward), (2, 1, 0))
    north = jnp.transpose(lax.ppermute(north_edge, "oy", backward), (2, 1, 0))
    lane = jnp.arange(wide, dtype=jnp.int32)
    offset = jnp.where(lane < lat_cells + STEPS, lane, lane - wide)
    latitude = (lat_start + offset).astype(jnp.float32)
    coriolis_wide = (coriolis_coef * (2.0 * (latitude + 0.5) / lat_total - 1.0))[None, :]
    top, state = run_steps(inner, aux, high, low, north, south, coriolis_wide, diffusivity, ocean_state.shape)
    surface = top.astype(jnp.bfloat16)
    pieces = jnp.einsum("tkra,tr->tka", remap_weights, surface, preferred_element_type=jnp.float32)
    slot_line = jnp.arange(slots, dtype=jnp.int32)
    to_slot = (tile_slots[:, :, None] == slot_line[None, None, :]).astype(jnp.float32)
    per_slot = jnp.einsum("tks,tka->sa", to_slot, pieces, precision=lax.Precision.HIGHEST)
    per_slot = per_slot.reshape(owners, capacity, block_width)
    returned = lax.all_to_all(per_slot, "ox", 0, 0, tiled=True)
    atmos_surface = jnp.einsum(
        "isb,isa->ba", to_block.astype(jnp.float32), returned, precision=lax.Precision.HIGHEST
    )
    return (state, atmos_surface)


def solution(mesh):
    return jax.shard_map(
        per_device,
        mesh=mesh,
        in_specs=(
            P(None, "oy", "ox"),
            P("ox", "oy", None, None),
            P("ox", "oy"),
            P("ox", "oy"),
            P("ox", "oy"),
            P(None, None, "ox", "oy"),
            P("ox", "oy"),
            P(),
        ),
        out_specs=(P(None, None, "ox", "oy"), P("oy", "ox")),
        check_vma=False,
    )
```

```python
import functools

import jax
import jax.numpy as jnp
from jax import lax
from jax.experimental import pallas as pl
from jax.experimental.layout import Layout, with_layout_constraint
from jax.experimental.pallas import tpu as pltpu
from jax.sharding import PartitionSpec as P

STEPS = 3


advect_coef = 0.25
pressure_coef = 0.1
thermal_coef = 0.2
haline_coef = 0.8
coriolis_coef = 0.5
vertical_coef = 0.1
forcing_coef = 0.5


def stencil_kernel(
    diff_ref, cor_ref, state_ref, aux_ref, high_ref, low_ref, north_ref, south_ref,
    out_ref, source, first, second, surface_only,
):
    fields = 4
    channels, rows, lanes = state_ref.shape
    levels = channels // fields
    tall, wide = source.shape[1], source.shape[2]
    width = high_ref.shape[1]

    north_rows = [north_ref[s] for s in range(width)]
    south_rows = [south_ref[s] for s in range(width)]

    def assemble(ch, inner):
        source[ch, :rows, :lanes] = inner
        source[ch, rows:, :] = jnp.zeros((tall - rows, wide), jnp.float32)
        source[ch, :rows, lanes:] = jnp.zeros((rows, wide - lanes), jnp.float32)
        source[ch, rows : rows + width, :lanes] = high_ref[ch]
        source[ch, tall - width :, :lanes] = low_ref[ch]
        for s in range(width):
            source[ch, :, lanes + s : lanes + s + 1] = north_rows[s][:, ch : ch + 1]
            far = wide - width + s
            source[ch, :, far : far + 1] = south_rows[s][:, ch : ch + 1]

    if surface_only:
        for f in range(fields):
            for l in range(min(levels, STEPS + 1)):
                assemble(f * levels + l, state_ref[f * levels + l])
    else:
        for ch in range(channels):
            assemble(ch, state_ref[ch])
    for index in range(aux_ref.shape[0]):
        assemble(channels + index, aux_ref[index])

    def aux(index):
        return source[channels + index]

    def one_step(read, write, last, count):
        def crop(value):
            return value[:rows, :lanes] if last else value

        def level(l, cum):
            up = jnp.maximum(l - 1, 0)
            down = jnp.minimum(l + 1, levels - 1)
            here = [read(f * levels + l) for f in range(fields)]
            density = haline_coef * here[3] - thermal_coef * here[2]
            cum = cum + density
            pressure = cum - 0.5 * density
            zonal = crop(here[0])
            meridional = crop(here[1])
            top = jnp.where(l == 0, forcing_coef, 0.0)
            diff = diff_ref[l]
            coriolis = crop(jnp.broadcast_to(cor_ref[...], (tall, wide)))
            for f in range(fields):
                whole = here[f]
                center = crop(whole)
                east = crop(pltpu.roll(whole, tall - 1, 0))
                west = crop(pltpu.roll(whole, 1, 0))
                north = crop(pltpu.roll(whole, wide - 1, 1))
                south = crop(pltpu.roll(whole, 1, 1))
                advection = -advect_coef * 0.5 * (zonal * (east - west) + meridional * (north - south))
                laplace = diff * (east + west + north + south - 4.0 * center)
                mixing = vertical_coef * (
                    crop(read(f * levels + up)) + crop(read(f * levels + down)) - 2.0 * center
                )
                total = advection + laplace + mixing
                if f == 0:
                    grad = crop(pltpu.roll(pressure, tall - 1, 0)) - crop(pltpu.roll(pressure, 1, 0))
                    total = total + (coriolis * meridional - pressure_coef * 0.5 * grad)
                if f == 1:
                    grad = crop(pltpu.roll(pressure, wide - 1, 1)) - crop(pltpu.roll(pressure, 1, 1))
                    total = total + (-coriolis * zonal - pressure_coef * 0.5 * grad)
                total = total + top * crop(aux(f))
                write(f, l, center + crop(aux(fields)) * total)
            return cum

        lax.fori_loop(0, count, level, jnp.zeros((tall, wide), jnp.float32), unroll=True)

    def read_src(ch):
        return source[ch]

    def read_first(ch):
        return first[ch]

    def read_second(ch):
        return second[ch]

    def write_first(f, l, value):
        first[f * levels + l] = value

    def write_second(f, l, value):
        second[f * levels + l] = value

    def write_out(f, l, value):
        if not surface_only:
            out_ref[f, l] = value
        elif f == 2:
            out_ref[...] = value.astype(out_ref.dtype)

    writers = [write_first, write_second]
    for repeat in range(STEPS):
        write = write_out if repeat == STEPS - 1 else writers[repeat % 2]
        read = read_src if repeat == 0 else (read_first if repeat % 2 == 1 else read_second)
        count = min(levels, STEPS - repeat) if surface_only else levels
        one_step(read, write, repeat == STEPS - 1, count)


def run_steps(state, aux, high, low, north, south, coriolis, diffusivity, out_shape):
    channels = state.shape[0] + aux.shape[0]
    rows, lanes = state.shape[1], state.shape[2]
    width = high.shape[1]
    tall = -(-(rows + 2 * width) // 8) * 8
    wide = -(-(lanes + 2 * width) // 128) * 128
    vmem = pl.BlockSpec(memory_space=pltpu.VMEM)
    operands = (diffusivity, coriolis, state, aux, high, low, north, south)

    def call(surface_only, shape, dtype):
        return pl.pallas_call(
            functools.partial(stencil_kernel, surface_only=surface_only),
            out_shape=jax.ShapeDtypeStruct(shape, dtype),
            in_specs=[pl.BlockSpec(memory_space=pltpu.SMEM)] + [vmem] * 7,
            out_specs=vmem,
            scratch_shapes=[
                pltpu.VMEM((channels, tall, wide), jnp.float32),
                pltpu.VMEM((state.shape[0], tall, wide), jnp.float32),
                pltpu.VMEM((state.shape[0], tall, wide), jnp.float32),
            ],
        )(*operands)

    return call(True, (rows, lanes), jnp.bfloat16), call(False, out_shape, jnp.float32)


def shifted(block, axis, dim, width):
    count = lax.axis_size(axis)
    forward = [(i, i + 1) for i in range(count - 1)]
    backward = [(target, source) for source, target in forward]
    size = block.shape[dim]
    low = lax.ppermute(lax.slice_in_dim(block, size - width, None, axis=dim), axis, forward)
    high = lax.ppermute(lax.slice_in_dim(block, 0, width, axis=dim), axis, backward)
    return low, high


def lat_factor(first_cell, count, lat_total):
    latitude = (first_cell + jnp.arange(count, dtype=jnp.int32)).astype(jnp.float32)
    return coriolis_coef * (2.0 * (latitude + 0.5) / lat_total - 1.0)


def per_device(
    atm_flux,
    remap_weights,
    tile_slots,
    need_blocks,
    send_blocks,
    ocean_state,
    land_mask,
    diffusivity,
):
    blocks_here = atm_flux.shape[1]
    block_width = atm_flux.shape[2]
    owners = lax.axis_size("ox")
    capacity = send_blocks.shape[1]
    slots = owners * capacity
    block_line = jnp.arange(blocks_here, dtype=jnp.int32)
    to_block = send_blocks[:, :, None] == block_line[None, None, :]
    outgoing = jnp.broadcast_to(atm_flux[None], (owners,) + atm_flux.shape)
    incoming = lax.all_to_all(outgoing, "ox", 0, 0, tiled=True)
    owner_of = tile_slots // capacity
    block_of = need_blocks.reshape(-1)[tile_slots]
    picks = incoming[owner_of, :, block_of, :]
    forcing = jnp.einsum("tkfa,tkra->ftr", picks, remap_weights, preferred_element_type=jnp.float32)
    fields, levels, rows, lat_cells = ocean_state.shape
    lat_total = lat_cells * lax.axis_size("oy")
    lat_start = lax.axis_index("oy") * lat_cells
    wetness = land_mask.astype(jnp.float32)
    inner = ocean_state.reshape(fields * levels, rows, lat_cells)
    aux = jnp.concatenate([forcing, wetness[None]], axis=0)
    packed = jnp.concatenate([inner, aux], axis=0)
    packed = with_layout_constraint(packed, Layout((0, 1, 2)))
    tall = -(-(rows + 2 * STEPS) // 8) * 8
    wide = -(-(lat_cells + 2 * STEPS) // 128) * 128
    low, high = shifted(packed, "ox", 1, STEPS)
    low = with_layout_constraint(low, Layout((0, 1, 2)))
    high = with_layout_constraint(high, Layout((0, 1, 2)))
    gap = jnp.zeros((packed.shape[0], tall - rows - 2 * STEPS, STEPS), jnp.float32)
    south_edge = jnp.concatenate(
        [packed[:, :, -STEPS:], high[:, :, -STEPS:], gap, low[:, :, -STEPS:]], axis=1
    )
    north_edge = jnp.concatenate(
        [packed[:, :, :STEPS], high[:, :, :STEPS], gap, low[:, :, :STEPS]], axis=1
    )
    count = lax.axis_size("oy")
    forward = [(i, i + 1) for i in range(count - 1)]
    backward = [(target, source) for source, target in forward]
    south = jnp.transpose(lax.ppermute(south_edge, "oy", forward), (2, 1, 0))
    north = jnp.transpose(lax.ppermute(north_edge, "oy", backward), (2, 1, 0))
    lane = jnp.arange(wide, dtype=jnp.int32)
    offset = jnp.where(lane < lat_cells + STEPS, lane, lane - wide)
    latitude = (lat_start + offset).astype(jnp.float32)
    coriolis_wide = (coriolis_coef * (2.0 * (latitude + 0.5) / lat_total - 1.0))[None, :]
    top, state = run_steps(inner, aux, high, low, north, south, coriolis_wide, diffusivity, ocean_state.shape)
    surface = top
    pieces = jnp.einsum("tkra,tr->tka", remap_weights, surface, preferred_element_type=jnp.float32)
    slot_line = jnp.arange(slots, dtype=jnp.int32)
    to_slot = (tile_slots[:, :, None] == slot_line[None, None, :]).astype(jnp.float32)
    per_slot = jnp.einsum("tks,tka->sa", to_slot, pieces, precision=lax.Precision.HIGHEST)
    per_slot = per_slot.reshape(owners, capacity, block_width)
    returned = lax.all_to_all(per_slot, "ox", 0, 0, tiled=True)
    atmos_surface = jnp.einsum(
        "isb,isa->ba", to_block.astype(jnp.float32), returned, precision=lax.Precision.HIGHEST
    )
    return (state, atmos_surface)


def solution(mesh):
    return jax.shard_map(
        per_device,
        mesh=mesh,
        in_specs=(
            P(None, "oy", "ox"),
            P("ox", "oy", None, None),
            P("ox", "oy"),
            P("ox", "oy"),
            P("ox", "oy"),
            P(None, None, "ox", "oy"),
            P("ox", "oy"),
            P(),
        ),
        out_specs=(P(None, None, "ox", "oy"), P("oy", "ox")),
        check_vma=False,
    )
```

```python
import functools

import jax
import jax.numpy as jnp
from jax import lax
from jax.experimental import pallas as pl
from jax.experimental.layout import Layout, with_layout_constraint
from jax.experimental.pallas import tpu as pltpu
from jax.sharding import PartitionSpec as P

STEPS = 3


advect_coef = 0.25
pressure_coef = 0.1
thermal_coef = 0.2
haline_coef = 0.8
coriolis_coef = 0.5
vertical_coef = 0.1
forcing_coef = 0.5


def stencil_kernel(
    diff_ref, cor_ref, state_ref, high_ref, low_ref, north_ref, south_ref,
    out_ref, source, first, second, surface_only, levels,
):
    fields = 4
    channels = fields * levels
    rows, lanes = state_ref.shape[1], state_ref.shape[2]
    tall, wide = source.shape[1], source.shape[2]
    width = high_ref.shape[1]

    north_rows = [north_ref[s] for s in range(width)]
    south_rows = [south_ref[s] for s in range(width)]

    def assemble(ch, inner):
        source[ch, :rows, :lanes] = inner
        source[ch, rows:, :] = jnp.zeros((tall - rows, wide), jnp.float32)
        source[ch, :rows, lanes:] = jnp.zeros((rows, wide - lanes), jnp.float32)
        source[ch, rows : rows + width, :lanes] = high_ref[ch]
        source[ch, tall - width :, :lanes] = low_ref[ch]
        for s in range(width):
            source[ch, :, lanes + s : lanes + s + 1] = north_rows[s][:, ch : ch + 1]
            far = wide - width + s
            source[ch, :, far : far + 1] = south_rows[s][:, ch : ch + 1]

    if surface_only:
        for f in range(fields):
            for l in range(min(levels, STEPS + 1)):
                assemble(f * levels + l, state_ref[f * levels + l])
    else:
        for ch in range(channels):
            assemble(ch, state_ref[ch])
    for index in range(channels, state_ref.shape[0]):
        assemble(index, state_ref[index])

    def aux(index):
        return source[channels + index]

    def one_step(read, write, last, count):
        def crop(value):
            return value[:rows, :lanes] if last else value

        def level(l, cum):
            up = jnp.maximum(l - 1, 0)
            down = jnp.minimum(l + 1, levels - 1)
            here = [read(f * levels + l) for f in range(fields)]
            density = haline_coef * here[3] - thermal_coef * here[2]
            cum = cum + density
            pressure = cum - 0.5 * density
            zonal = crop(here[0])
            meridional = crop(here[1])
            top = jnp.where(l == 0, forcing_coef, 0.0)
            diff = diff_ref[l]
            coriolis = crop(jnp.broadcast_to(cor_ref[...], (tall, wide)))
            for f in range(fields):
                whole = here[f]
                center = crop(whole)
                east = crop(pltpu.roll(whole, tall - 1, 0))
                west = crop(pltpu.roll(whole, 1, 0))
                north = crop(pltpu.roll(whole, wide - 1, 1))
                south = crop(pltpu.roll(whole, 1, 1))
                advection = -advect_coef * 0.5 * (zonal * (east - west) + meridional * (north - south))
                laplace = diff * (east + west + north + south - 4.0 * center)
                mixing = vertical_coef * (
                    crop(read(f * levels + up)) + crop(read(f * levels + down)) - 2.0 * center
                )
                total = advection + laplace + mixing
                if f == 0:
                    grad = crop(pltpu.roll(pressure, tall - 1, 0)) - crop(pltpu.roll(pressure, 1, 0))
                    total = total + (coriolis * meridional - pressure_coef * 0.5 * grad)
                if f == 1:
                    grad = crop(pltpu.roll(pressure, wide - 1, 1)) - crop(pltpu.roll(pressure, 1, 1))
                    total = total + (-coriolis * zonal - pressure_coef * 0.5 * grad)
                total = total + top * crop(aux(f))
                write(f, l, center + crop(aux(fields)) * total)
            return cum

        lax.fori_loop(0, count, level, jnp.zeros((tall, wide), jnp.float32), unroll=True)

    def read_src(ch):
        return source[ch]

    def read_first(ch):
        return first[ch]

    def read_second(ch):
        return second[ch]

    def write_first(f, l, value):
        first[f * levels + l] = value

    def write_second(f, l, value):
        second[f * levels + l] = value

    def write_out(f, l, value):
        if not surface_only:
            out_ref[f, l] = value
        elif f == 2:
            out_ref[...] = value.astype(out_ref.dtype)

    writers = [write_first, write_second]
    for repeat in range(STEPS):
        write = write_out if repeat == STEPS - 1 else writers[repeat % 2]
        read = read_src if repeat == 0 else (read_first if repeat % 2 == 1 else read_second)
        count = min(levels, STEPS - repeat) if surface_only else levels
        one_step(read, write, repeat == STEPS - 1, count)


def run_steps(state, high, low, north, south, coriolis, diffusivity, out_shape):
    channels = state.shape[0]
    fields, levels = out_shape[0], out_shape[1]
    rows, lanes = state.shape[1], state.shape[2]
    width = high.shape[1]
    tall = -(-(rows + 2 * width) // 8) * 8
    wide = -(-(lanes + 2 * width) // 128) * 128
    vmem = pl.BlockSpec(memory_space=pltpu.VMEM)
    operands = (diffusivity, coriolis, state, high, low, north, south)

    def call(surface_only, shape, dtype):
        return pl.pallas_call(
            functools.partial(stencil_kernel, surface_only=surface_only, levels=levels),
            out_shape=jax.ShapeDtypeStruct(shape, dtype),
            in_specs=[pl.BlockSpec(memory_space=pltpu.SMEM)] + [vmem] * 6,
            out_specs=vmem,
            scratch_shapes=[
                pltpu.VMEM((channels, tall, wide), jnp.float32),
                pltpu.VMEM((fields * levels, tall, wide), jnp.float32),
                pltpu.VMEM((fields * levels, tall, wide), jnp.float32),
            ],
        )(*operands)

    return call(True, (rows, lanes), jnp.bfloat16), call(False, out_shape, jnp.float32)


def shifted(block, axis, dim, width):
    count = lax.axis_size(axis)
    forward = [(i, i + 1) for i in range(count - 1)]
    backward = [(target, source) for source, target in forward]
    size = block.shape[dim]
    low = lax.ppermute(lax.slice_in_dim(block, size - width, None, axis=dim), axis, forward)
    high = lax.ppermute(lax.slice_in_dim(block, 0, width, axis=dim), axis, backward)
    return low, high


def lat_factor(first_cell, count, lat_total):
    latitude = (first_cell + jnp.arange(count, dtype=jnp.int32)).astype(jnp.float32)
    return coriolis_coef * (2.0 * (latitude + 0.5) / lat_total - 1.0)


def per_device(
    atm_flux,
    remap_weights,
    tile_slots,
    need_blocks,
    send_blocks,
    ocean_state,
    land_mask,
    diffusivity,
):
    blocks_here = atm_flux.shape[1]
    block_width = atm_flux.shape[2]
    owners = lax.axis_size("ox")
    capacity = send_blocks.shape[1]
    slots = owners * capacity
    block_line = jnp.arange(blocks_here, dtype=jnp.int32)
    to_block = send_blocks[:, :, None] == block_line[None, None, :]
    outgoing = jnp.broadcast_to(atm_flux[None], (owners,) + atm_flux.shape)
    incoming = lax.all_to_all(outgoing, "ox", 0, 0, tiled=True)
    owner_of = tile_slots // capacity
    block_of = need_blocks.reshape(-1)[tile_slots]
    picks = incoming[owner_of, :, block_of, :]
    forcing = jnp.einsum("tkfa,tkra->ftr", picks, remap_weights, preferred_element_type=jnp.float32)
    fields, levels, rows, lat_cells = ocean_state.shape
    lat_total = lat_cells * lax.axis_size("oy")
    lat_start = lax.axis_index("oy") * lat_cells
    wetness = land_mask.astype(jnp.float32)
    inner = ocean_state.reshape(fields * levels, rows, lat_cells)
    aux = jnp.concatenate([forcing, wetness[None]], axis=0)
    packed = jnp.concatenate([inner, aux], axis=0)
    packed = with_layout_constraint(packed, Layout((0, 1, 2)))
    tall = -(-(rows + 2 * STEPS) // 8) * 8
    wide = -(-(lat_cells + 2 * STEPS) // 128) * 128
    low, high = shifted(packed, "ox", 1, STEPS)
    low = with_layout_constraint(low, Layout((0, 1, 2)))
    high = with_layout_constraint(high, Layout((0, 1, 2)))
    gap = jnp.zeros((packed.shape[0], tall - rows - 2 * STEPS, STEPS), jnp.float32)
    south_edge = jnp.concatenate(
        [packed[:, :, -STEPS:], high[:, :, -STEPS:], gap, low[:, :, -STEPS:]], axis=1
    )
    north_edge = jnp.concatenate(
        [packed[:, :, :STEPS], high[:, :, :STEPS], gap, low[:, :, :STEPS]], axis=1
    )
    count = lax.axis_size("oy")
    forward = [(i, i + 1) for i in range(count - 1)]
    backward = [(target, source) for source, target in forward]
    south = jnp.transpose(lax.ppermute(south_edge, "oy", forward), (2, 1, 0))
    north = jnp.transpose(lax.ppermute(north_edge, "oy", backward), (2, 1, 0))
    lane = jnp.arange(wide, dtype=jnp.int32)
    offset = jnp.where(lane < lat_cells + STEPS, lane, lane - wide)
    latitude = (lat_start + offset).astype(jnp.float32)
    coriolis_wide = (coriolis_coef * (2.0 * (latitude + 0.5) / lat_total - 1.0))[None, :]
    top, state = run_steps(packed, high, low, north, south, coriolis_wide, diffusivity, ocean_state.shape)
    surface = top
    pieces = jnp.einsum("tkra,tr->tka", remap_weights, surface, preferred_element_type=jnp.float32)
    slot_line = jnp.arange(slots, dtype=jnp.int32)
    to_slot = (tile_slots[:, :, None] == slot_line[None, None, :]).astype(jnp.float32)
    per_slot = jnp.einsum("tks,tka->sa", to_slot, pieces, precision=lax.Precision.HIGHEST)
    per_slot = per_slot.reshape(owners, capacity, block_width)
    returned = lax.all_to_all(per_slot, "ox", 0, 0, tiled=True)
    atmos_surface = jnp.einsum(
        "isb,isa->ba", to_block.astype(jnp.float32), returned, precision=lax.Precision.HIGHEST
    )
    return (state, atmos_surface)


def solution(mesh):
    return jax.shard_map(
        per_device,
        mesh=mesh,
        in_specs=(
            P(None, "oy", "ox"),
            P("ox", "oy", None, None),
            P("ox", "oy"),
            P("ox", "oy"),
            P("ox", "oy"),
            P(None, None, "ox", "oy"),
            P("ox", "oy"),
            P(),
        ),
        out_specs=(P(None, None, "ox", "oy"), P("oy", "ox")),
        check_vma=False,
    )
```

```python
import functools

import jax
import jax.numpy as jnp
from jax import lax
from jax.experimental import pallas as pl
from jax.experimental.layout import Layout, with_layout_constraint
from jax.experimental.pallas import tpu as pltpu
from jax.sharding import PartitionSpec as P

STEPS = 3


advect_coef = 0.25
pressure_coef = 0.1
thermal_coef = 0.2
haline_coef = 0.8
coriolis_coef = 0.5
vertical_coef = 0.1
forcing_coef = 0.5


def stencil_kernel(
    diff_ref, cor_ref, state_ref, aux_ref, high_ref, low_ref, north_ref, south_ref,
    out_ref, source, first, second, surface_only,
):
    fields = 4
    channels, rows, lanes = state_ref.shape
    levels = channels // fields
    tall, wide = source.shape[1], source.shape[2]
    width = high_ref.shape[1]

    north_rows = [north_ref[s] for s in range(width)]
    south_rows = [south_ref[s] for s in range(width)]

    def assemble(ch, inner):
        source[ch, :rows, :lanes] = inner
        source[ch, rows:, :] = jnp.zeros((tall - rows, wide), jnp.float32)
        source[ch, :rows, lanes:] = jnp.zeros((rows, wide - lanes), jnp.float32)
        source[ch, rows : rows + width, :lanes] = high_ref[ch]
        source[ch, tall - width :, :lanes] = low_ref[ch]
        for s in range(width):
            source[ch, :, lanes + s : lanes + s + 1] = north_rows[s][:, ch : ch + 1]
            far = wide - width + s
            source[ch, :, far : far + 1] = south_rows[s][:, ch : ch + 1]

    if surface_only:
        for f in range(fields):
            for l in range(min(levels, STEPS + 1)):
                assemble(f * levels + l, state_ref[f * levels + l])
    else:
        for ch in range(channels):
            assemble(ch, state_ref[ch])
    for index in range(aux_ref.shape[0]):
        assemble(channels + index, aux_ref[index])

    def aux(index):
        return source[channels + index]

    def one_step(read, write, last, count):
        def crop(value):
            return value[:rows, :lanes] if last else value

        def level(l, cum):
            up = jnp.maximum(l - 1, 0)
            down = jnp.minimum(l + 1, levels - 1)
            here = [read(f * levels + l) for f in range(fields)]
            density = haline_coef * here[3] - thermal_coef * here[2]
            cum = cum + density
            pressure = cum - 0.5 * density
            zonal = crop(here[0])
            meridional = crop(here[1])
            top = jnp.where(l == 0, forcing_coef, 0.0)
            diff = diff_ref[l]
            coriolis = crop(jnp.broadcast_to(cor_ref[...], (tall, wide)))
            for f in range(fields):
                whole = here[f]
                center = crop(whole)
                east = crop(pltpu.roll(whole, tall - 1, 0))
                west = crop(pltpu.roll(whole, 1, 0))
                north = crop(pltpu.roll(whole, wide - 1, 1))
                south = crop(pltpu.roll(whole, 1, 1))
                advection = -advect_coef * 0.5 * (zonal * (east - west) + meridional * (north - south))
                laplace = diff * (east + west + north + south - 4.0 * center)
                mixing = vertical_coef * (
                    crop(read(f * levels + up)) + crop(read(f * levels + down)) - 2.0 * center
                )
                total = advection + laplace + mixing
                if f == 0:
                    grad = crop(pltpu.roll(pressure, tall - 1, 0)) - crop(pltpu.roll(pressure, 1, 0))
                    total = total + (coriolis * meridional - pressure_coef * 0.5 * grad)
                if f == 1:
                    grad = crop(pltpu.roll(pressure, wide - 1, 1)) - crop(pltpu.roll(pressure, 1, 1))
                    total = total + (-coriolis * zonal - pressure_coef * 0.5 * grad)
                total = total + top * crop(aux(f))
                write(f, l, center + crop(aux(fields)) * total)
            return cum

        lax.fori_loop(0, count, level, jnp.zeros((tall, wide), jnp.float32), unroll=True)

    def read_src(ch):
        return source[ch]

    def read_first(ch):
        return first[ch]

    def read_second(ch):
        return second[ch]

    def write_first(f, l, value):
        first[f * levels + l] = value

    def write_second(f, l, value):
        second[f * levels + l] = value

    def write_out(f, l, value):
        if not surface_only:
            out_ref[f, l] = value
        elif f == 2:
            out_ref[...] = value.astype(out_ref.dtype)

    writers = [write_first, write_second]
    for repeat in range(STEPS):
        write = write_out if repeat == STEPS - 1 else writers[repeat % 2]
        read = read_src if repeat == 0 else (read_first if repeat % 2 == 1 else read_second)
        count = min(levels, STEPS - repeat) if surface_only else levels
        one_step(read, write, repeat == STEPS - 1, count)


def run_steps(state, aux, high, low, north, south, coriolis, diffusivity, out_shape):
    channels = state.shape[0] + aux.shape[0]
    rows, lanes = state.shape[1], state.shape[2]
    width = high.shape[1]
    tall = -(-(rows + 2 * width) // 8) * 8
    wide = -(-(lanes + 2 * width) // 128) * 128
    vmem = pl.BlockSpec(memory_space=pltpu.VMEM)
    operands = (diffusivity, coriolis, state, aux, high, low, north, south)

    def call(surface_only, shape, dtype):
        return pl.pallas_call(
            functools.partial(stencil_kernel, surface_only=surface_only),
            out_shape=jax.ShapeDtypeStruct(shape, dtype),
            in_specs=[pl.BlockSpec(memory_space=pltpu.SMEM)] + [vmem] * 7,
            out_specs=vmem,
            scratch_shapes=[
                pltpu.VMEM((channels, tall, wide), jnp.float32),
                pltpu.VMEM((state.shape[0], tall, wide), jnp.float32),
                pltpu.VMEM((state.shape[0], tall, wide), jnp.float32),
            ],
        )(*operands)

    return call(True, (rows, lanes), jnp.bfloat16), call(False, out_shape, jnp.float32)


def shifted(block, axis, dim, width):
    count = lax.axis_size(axis)
    forward = [(i, i + 1) for i in range(count - 1)]
    backward = [(target, source) for source, target in forward]
    size = block.shape[dim]
    low = lax.ppermute(lax.slice_in_dim(block, size - width, None, axis=dim), axis, forward)
    high = lax.ppermute(lax.slice_in_dim(block, 0, width, axis=dim), axis, backward)
    return low, high


def lat_factor(first_cell, count, lat_total):
    latitude = (first_cell + jnp.arange(count, dtype=jnp.int32)).astype(jnp.float32)
    return coriolis_coef * (2.0 * (latitude + 0.5) / lat_total - 1.0)


def per_device(
    atm_flux,
    remap_weights,
    tile_slots,
    need_blocks,
    send_blocks,
    ocean_state,
    land_mask,
    diffusivity,
):
    blocks_here = atm_flux.shape[1]
    block_width = atm_flux.shape[2]
    owners = lax.axis_size("ox")
    capacity = send_blocks.shape[1]
    slots = owners * capacity
    block_line = jnp.arange(blocks_here, dtype=jnp.int32)
    to_block = send_blocks[:, :, None] == block_line[None, None, :]
    outgoing = jnp.broadcast_to(atm_flux[None], (owners,) + atm_flux.shape)
    incoming = lax.all_to_all(outgoing, "ox", 0, 0, tiled=True)
    owner_of = tile_slots // capacity
    block_of = need_blocks.reshape(-1)[tile_slots]
    picks = incoming[owner_of, :, block_of, :]
    forcing = jnp.einsum("tkfa,tkra->ftr", picks, remap_weights, preferred_element_type=jnp.float32)
    fields, levels, rows, lat_cells = ocean_state.shape
    lat_total = lat_cells * lax.axis_size("oy")
    lat_start = lax.axis_index("oy") * lat_cells
    wetness = land_mask.astype(jnp.float32)
    inner = ocean_state.reshape(fields * levels, rows, lat_cells)
    aux = jnp.concatenate([forcing, wetness[None]], axis=0)
    packed = jnp.concatenate([inner, aux], axis=0)
    packed = with_layout_constraint(packed, Layout((0, 1, 2)))
    tall = -(-(rows + 2 * STEPS) // 8) * 8
    wide = -(-(lat_cells + 2 * STEPS) // 128) * 128
    low, high = shifted(packed, "ox", 1, STEPS)
    low = with_layout_constraint(low, Layout((0, 1, 2)))
    high = with_layout_constraint(high, Layout((0, 1, 2)))
    gap = jnp.zeros((packed.shape[0], tall - rows - 2 * STEPS, STEPS), jnp.float32)
    south_edge = jnp.concatenate(
        [packed[:, :, -STEPS:], high[:, :, -STEPS:], gap, low[:, :, -STEPS:]], axis=1
    )
    north_edge = jnp.concatenate(
        [packed[:, :, :STEPS], high[:, :, :STEPS], gap, low[:, :, :STEPS]], axis=1
    )
    count = lax.axis_size("oy")
    forward = [(i, i + 1) for i in range(count - 1)]
    backward = [(target, source) for source, target in forward]
    south = jnp.transpose(lax.ppermute(south_edge, "oy", forward), (2, 1, 0))
    north = jnp.transpose(lax.ppermute(north_edge, "oy", backward), (2, 1, 0))
    lane = jnp.arange(wide, dtype=jnp.int32)
    offset = jnp.where(lane < lat_cells + STEPS, lane, lane - wide)
    latitude = (lat_start + offset).astype(jnp.float32)
    coriolis_wide = (coriolis_coef * (2.0 * (latitude + 0.5) / lat_total - 1.0))[None, :]
    top, state = run_steps(inner, aux, high, low, north, south, coriolis_wide, diffusivity, ocean_state.shape)
    surface = top
    pieces = jnp.einsum("tkra,tr->tka", remap_weights, surface, preferred_element_type=jnp.float32)
    room = -(-capacity // 8) * 8
    slot_of = (tile_slots // capacity) * room + tile_slots % capacity
    slot_line = jnp.arange(owners * room, dtype=jnp.int32)
    to_slot = (slot_of[:, :, None] == slot_line[None, None, :]).astype(jnp.float32)
    per_slot = jnp.einsum("tks,tka->sa", to_slot, pieces, precision=lax.Precision.HIGHEST)
    per_slot = per_slot.reshape(owners, room, block_width)
    returned = lax.all_to_all(per_slot, "ox", 0, 0, tiled=True)
    wide_send = jnp.pad(send_blocks, ((0, 0), (0, room - capacity)), constant_values=-1)
    to_room = wide_send[:, :, None] == block_line[None, None, :]
    atmos_surface = jnp.einsum(
        "isb,isa->ba", to_room.astype(jnp.float32), returned, precision=lax.Precision.HIGHEST
    )
    return (state, atmos_surface)


def solution(mesh):
    return jax.shard_map(
        per_device,
        mesh=mesh,
        in_specs=(
            P(None, "oy", "ox"),
            P("ox", "oy", None, None),
            P("ox", "oy"),
            P("ox", "oy"),
            P("ox", "oy"),
            P(None, None, "ox", "oy"),
            P("ox", "oy"),
            P(),
        ),
        out_specs=(P(None, None, "ox", "oy"), P("oy", "ox")),
        check_vma=False,
    )
```

```python
import functools

import jax
import jax.numpy as jnp
from jax import lax
from jax.experimental import pallas as pl
from jax.experimental.layout import Layout, with_layout_constraint
from jax.experimental.pallas import tpu as pltpu
from jax.sharding import PartitionSpec as P

STEPS = 3


advect_coef = 0.25
pressure_coef = 0.1
thermal_coef = 0.2
haline_coef = 0.8
coriolis_coef = 0.5
vertical_coef = 0.1
forcing_coef = 0.5


def stencil_kernel(
    diff_ref, cor_ref, state_ref, aux_ref, high_ref, low_ref, north_ref, south_ref,
    out_ref, source, first, second, surface_only,
):
    fields = 4
    channels, rows, lanes = state_ref.shape
    levels = channels // fields
    tall, wide = source.shape[1], source.shape[2]
    width = high_ref.shape[1]

    north_rows = [north_ref[s] for s in range(width)]
    south_rows = [south_ref[s] for s in range(width)]

    def assemble(ch, inner):
        source[ch, :rows, :lanes] = inner
        source[ch, rows:, :] = jnp.zeros((tall - rows, wide), jnp.float32)
        source[ch, :rows, lanes:] = jnp.zeros((rows, wide - lanes), jnp.float32)
        source[ch, rows : rows + width, :lanes] = high_ref[ch]
        source[ch, tall - width :, :lanes] = low_ref[ch]
        for s in range(width):
            source[ch, :, lanes + s : lanes + s + 1] = north_rows[s][:, ch : ch + 1]
            far = wide - width + s
            source[ch, :, far : far + 1] = south_rows[s][:, ch : ch + 1]

    if surface_only:
        for f in range(fields):
            for l in range(min(levels, STEPS + 1)):
                assemble(f * levels + l, state_ref[f * levels + l])
    else:
        for ch in range(channels):
            assemble(ch, state_ref[ch])
    for index in range(aux_ref.shape[0]):
        assemble(channels + index, aux_ref[index])

    def aux(index):
        return source[channels + index]

    def one_step(read, write, last, count):
        def crop(value):
            return value[:rows, :lanes] if last else value

        def level(l, cum):
            up = jnp.maximum(l - 1, 0)
            down = jnp.minimum(l + 1, levels - 1)
            here = [read(f * levels + l) for f in range(fields)]
            density = haline_coef * here[3] - thermal_coef * here[2]
            cum = cum + density
            pressure = cum - 0.5 * density
            zonal = crop(here[0])
            meridional = crop(here[1])
            top = jnp.where(l == 0, forcing_coef, 0.0)
            diff = diff_ref[l]
            coriolis = crop(jnp.broadcast_to(cor_ref[...], (tall, wide)))
            for f in range(fields):
                whole = here[f]
                center = crop(whole)
                east = crop(pltpu.roll(whole, tall - 1, 0))
                west = crop(pltpu.roll(whole, 1, 0))
                north = crop(pltpu.roll(whole, wide - 1, 1))
                south = crop(pltpu.roll(whole, 1, 1))
                advection = -advect_coef * 0.5 * (zonal * (east - west) + meridional * (north - south))
                laplace = diff * (east + west + north + south - 4.0 * center)
                mixing = vertical_coef * (
                    crop(read(f * levels + up)) + crop(read(f * levels + down)) - 2.0 * center
                )
                total = advection + laplace + mixing
                if f == 0:
                    grad = crop(pltpu.roll(pressure, tall - 1, 0)) - crop(pltpu.roll(pressure, 1, 0))
                    total = total + (coriolis * meridional - pressure_coef * 0.5 * grad)
                if f == 1:
                    grad = crop(pltpu.roll(pressure, wide - 1, 1)) - crop(pltpu.roll(pressure, 1, 1))
                    total = total + (-coriolis * zonal - pressure_coef * 0.5 * grad)
                total = total + top * crop(aux(f))
                write(f, l, center + crop(aux(fields)) * total)
            return cum

        lax.fori_loop(0, count, level, jnp.zeros((tall, wide), jnp.float32), unroll=True)

    def read_src(ch):
        return source[ch]

    def read_first(ch):
        return first[ch]

    def read_second(ch):
        return second[ch]

    def write_first(f, l, value):
        first[f * levels + l] = value

    def write_second(f, l, value):
        second[f * levels + l] = value

    def write_out(f, l, value):
        if not surface_only:
            out_ref[f, l] = value
        elif f == 2:
            out_ref[...] = value.astype(out_ref.dtype)

    writers = [write_first, write_second]
    for repeat in range(STEPS):
        write = write_out if repeat == STEPS - 1 else writers[repeat % 2]
        read = read_src if repeat == 0 else (read_first if repeat % 2 == 1 else read_second)
        count = min(levels, STEPS - repeat) if surface_only else levels
        one_step(read, write, repeat == STEPS - 1, count)


def run_steps(state, aux, high, low, north, south, coriolis, diffusivity, out_shape):
    channels = state.shape[0] + aux.shape[0]
    rows, lanes = state.shape[1], state.shape[2]
    width = high.shape[1]
    tall = -(-(rows + 2 * width) // 8) * 8
    wide = -(-(lanes + 2 * width) // 128) * 128
    vmem = pl.BlockSpec(memory_space=pltpu.VMEM)
    operands = (diffusivity, coriolis, state, aux, high, low, north, south)

    def call(surface_only, shape, dtype):
        return pl.pallas_call(
            functools.partial(stencil_kernel, surface_only=surface_only),
            out_shape=jax.ShapeDtypeStruct(shape, dtype),
            in_specs=[pl.BlockSpec(memory_space=pltpu.SMEM)] + [vmem] * 7,
            out_specs=vmem,
            scratch_shapes=[
                pltpu.VMEM((channels, tall, wide), jnp.float32),
                pltpu.VMEM((state.shape[0], tall, wide), jnp.float32),
                pltpu.VMEM((state.shape[0], tall, wide), jnp.float32),
            ],
        )(*operands)

    return call(True, (rows, lanes), jnp.bfloat16), call(False, out_shape, jnp.float32)


def shifted(block, axis, dim, width):
    count = lax.axis_size(axis)
    forward = [(i, i + 1) for i in range(count - 1)]
    backward = [(target, source) for source, target in forward]
    size = block.shape[dim]
    low = lax.ppermute(lax.slice_in_dim(block, size - width, None, axis=dim), axis, forward)
    high = lax.ppermute(lax.slice_in_dim(block, 0, width, axis=dim), axis, backward)
    return low, high


def lat_factor(first_cell, count, lat_total):
    latitude = (first_cell + jnp.arange(count, dtype=jnp.int32)).astype(jnp.float32)
    return coriolis_coef * (2.0 * (latitude + 0.5) / lat_total - 1.0)


def per_device(
    atm_flux,
    remap_weights,
    tile_slots,
    need_blocks,
    send_blocks,
    ocean_state,
    land_mask,
    diffusivity,
):
    blocks_here = atm_flux.shape[1]
    block_width = atm_flux.shape[2]
    owners = lax.axis_size("ox")
    capacity = send_blocks.shape[1]
    slots = owners * capacity
    block_line = jnp.arange(blocks_here, dtype=jnp.int32)
    to_block = send_blocks[:, :, None] == block_line[None, None, :]
    outgoing = jnp.broadcast_to(atm_flux[None], (owners,) + atm_flux.shape)
    incoming = lax.all_to_all(outgoing, "ox", 0, 0, tiled=True)
    owner_of = tile_slots // capacity
    block_of = need_blocks.reshape(-1)[tile_slots]
    picks = incoming[owner_of, :, block_of, :]
    forcing = jnp.einsum("tkfa,tkra->ftr", picks, remap_weights, preferred_element_type=jnp.float32)
    fields, levels, rows, lat_cells = ocean_state.shape
    lat_total = lat_cells * lax.axis_size("oy")
    lat_start = lax.axis_index("oy") * lat_cells
    wetness = land_mask.astype(jnp.float32)
    inner = ocean_state.reshape(fields * levels, rows, lat_cells)
    aux = jnp.concatenate([forcing, wetness[None]], axis=0)
    packed = jnp.concatenate([inner, aux], axis=0)
    packed = with_layout_constraint(packed, Layout((0, 1, 2)))
    tall = -(-(rows + 2 * STEPS) // 8) * 8
    wide = -(-(lat_cells + 2 * STEPS) // 128) * 128
    low, high = shifted(packed, "ox", 1, STEPS)
    low = with_layout_constraint(low, Layout((0, 1, 2)))
    high = with_layout_constraint(high, Layout((0, 1, 2)))
    gap = jnp.zeros((packed.shape[0], tall - rows - 2 * STEPS, STEPS), jnp.float32)
    south_edge = jnp.concatenate(
        [packed[:, :, -STEPS:], high[:, :, -STEPS:], gap, low[:, :, -STEPS:]], axis=1
    )
    north_edge = jnp.concatenate(
        [packed[:, :, :STEPS], high[:, :, :STEPS], gap, low[:, :, :STEPS]], axis=1
    )
    count = lax.axis_size("oy")
    forward = [(i, i + 1) for i in range(count - 1)]
    backward = [(target, source) for source, target in forward]
    south = jnp.transpose(lax.ppermute(south_edge, "oy", forward), (2, 1, 0))
    north = jnp.transpose(lax.ppermute(north_edge, "oy", backward), (2, 1, 0))
    lane = jnp.arange(wide, dtype=jnp.int32)
    offset = jnp.where(lane < lat_cells + STEPS, lane, lane - wide)
    latitude = (lat_start + offset).astype(jnp.float32)
    coriolis_wide = (coriolis_coef * (2.0 * (latitude + 0.5) / lat_total - 1.0))[None, :]
    top, state = run_steps(inner, aux, high, low, north, south, coriolis_wide, diffusivity, ocean_state.shape)
    surface = top
    slot_line = jnp.arange(slots, dtype=jnp.int32)
    to_slot = tile_slots[None, :, :] == slot_line[:, None, None]
    spread = jnp.where(to_slot[:, :, :, None], surface[None, :, None, :], jnp.zeros((), surface.dtype))
    per_slot = jnp.einsum("stkr,tkra->sa", spread, remap_weights, preferred_element_type=jnp.float32)
    per_slot = per_slot.reshape(owners, capacity, block_width)
    returned = lax.all_to_all(per_slot, "ox", 0, 0, tiled=True)
    atmos_surface = jnp.einsum(
        "isb,isa->ba", to_block.astype(jnp.float32), returned, precision=lax.Precision.HIGHEST
    )
    return (state, atmos_surface)


def solution(mesh):
    return jax.shard_map(
        per_device,
        mesh=mesh,
        in_specs=(
            P(None, "oy", "ox"),
            P("ox", "oy", None, None),
            P("ox", "oy"),
            P("ox", "oy"),
            P("ox", "oy"),
            P(None, None, "ox", "oy"),
            P("ox", "oy"),
            P(),
        ),
        out_specs=(P(None, None, "ox", "oy"), P("oy", "ox")),
        check_vma=False,
    )
```

```python
import functools

import jax
import jax.numpy as jnp
from jax import lax
from jax.experimental import pallas as pl
from jax.experimental.layout import Layout, with_layout_constraint
from jax.experimental.pallas import tpu as pltpu
from jax.sharding import PartitionSpec as P

STEPS = 3


advect_coef = 0.25
pressure_coef = 0.1
thermal_coef = 0.2
haline_coef = 0.8
coriolis_coef = 0.5
vertical_coef = 0.1
forcing_coef = 0.5


def stencil_kernel(
    diff_ref, cor_ref, state_ref, aux_ref, high_ref, low_ref, north_ref, south_ref,
    out_ref, source, first, second, surface_only,
):
    fields = 4
    channels, rows, lanes = state_ref.shape
    levels = channels // fields
    tall, wide = source.shape[1], source.shape[2]
    width = high_ref.shape[1]

    north_rows = [north_ref[s] for s in range(width)]
    south_rows = [south_ref[s] for s in range(width)]

    def assemble(ch, inner):
        source[ch, :rows, :lanes] = inner
        source[ch, rows:, :] = jnp.zeros((tall - rows, wide), jnp.float32)
        source[ch, :rows, lanes:] = jnp.zeros((rows, wide - lanes), jnp.float32)
        source[ch, rows : rows + width, :lanes] = high_ref[ch]
        source[ch, tall - width :, :lanes] = low_ref[ch]
        for s in range(width):
            source[ch, :, lanes + s : lanes + s + 1] = north_rows[s][:, ch : ch + 1]
            far = wide - width + s
            source[ch, :, far : far + 1] = south_rows[s][:, ch : ch + 1]

    if surface_only:
        for f in range(fields):
            for l in range(min(levels, STEPS + 1)):
                assemble(f * levels + l, state_ref[f * levels + l])
    else:
        for ch in range(channels):
            assemble(ch, state_ref[ch])
    for index in range(aux_ref.shape[0]):
        assemble(channels + index, aux_ref[index])

    def aux(index):
        return source[channels + index]

    def one_step(read, write, last, count):
        def crop(value):
            return value[:rows, :lanes] if last else value

        def level(l, cum):
            up = jnp.maximum(l - 1, 0)
            down = jnp.minimum(l + 1, levels - 1)
            here = [read(f * levels + l) for f in range(fields)]
            density = haline_coef * here[3] - thermal_coef * here[2]
            cum = cum + density
            pressure = cum - 0.5 * density
            zonal = crop(here[0])
            meridional = crop(here[1])
            top = jnp.where(l == 0, forcing_coef, 0.0)
            diff = diff_ref[l]
            coriolis = crop(jnp.broadcast_to(cor_ref[...], (tall, wide)))
            for f in range(fields):
                whole = here[f]
                center = crop(whole)
                east = crop(pltpu.roll(whole, tall - 1, 0))
                west = crop(pltpu.roll(whole, 1, 0))
                north = crop(pltpu.roll(whole, wide - 1, 1))
                south = crop(pltpu.roll(whole, 1, 1))
                advection = -advect_coef * 0.5 * (zonal * (east - west) + meridional * (north - south))
                laplace = diff * (east + west + north + south - 4.0 * center)
                mixing = vertical_coef * (
                    crop(read(f * levels + up)) + crop(read(f * levels + down)) - 2.0 * center
                )
                total = advection + laplace + mixing
                if f == 0:
                    grad = crop(pltpu.roll(pressure, tall - 1, 0)) - crop(pltpu.roll(pressure, 1, 0))
                    total = total + (coriolis * meridional - pressure_coef * 0.5 * grad)
                if f == 1:
                    grad = crop(pltpu.roll(pressure, wide - 1, 1)) - crop(pltpu.roll(pressure, 1, 1))
                    total = total + (-coriolis * zonal - pressure_coef * 0.5 * grad)
                total = total + top * crop(aux(f))
                write(f, l, center + crop(aux(fields)) * total)
            return cum

        lax.fori_loop(0, count, level, jnp.zeros((tall, wide), jnp.float32), unroll=True)

    def read_src(ch):
        return source[ch]

    def read_first(ch):
        return first[ch]

    def read_second(ch):
        return second[ch]

    def write_first(f, l, value):
        first[f * levels + l] = value

    def write_second(f, l, value):
        second[f * levels + l] = value

    def write_out(f, l, value):
        if not surface_only:
            out_ref[f, l] = value
        elif f == 2:
            out_ref[...] = value.astype(out_ref.dtype)

    writers = [write_first, write_second]
    for repeat in range(STEPS):
        write = write_out if repeat == STEPS - 1 else writers[repeat % 2]
        read = read_src if repeat == 0 else (read_first if repeat % 2 == 1 else read_second)
        count = min(levels, STEPS - repeat) if surface_only else levels
        one_step(read, write, repeat == STEPS - 1, count)


def run_steps(state, aux, high, low, north, south, coriolis, diffusivity, out_shape):
    channels = state.shape[0] + aux.shape[0]
    rows, lanes = state.shape[1], state.shape[2]
    width = high.shape[1]
    tall = -(-(rows + 2 * width) // 8) * 8
    wide = -(-(lanes + 2 * width) // 128) * 128
    vmem = pl.BlockSpec(memory_space=pltpu.VMEM)
    operands = (diffusivity, coriolis, state, aux, high, low, north, south)

    def call(surface_only, shape, dtype):
        return pl.pallas_call(
            functools.partial(stencil_kernel, surface_only=surface_only),
            out_shape=jax.ShapeDtypeStruct(shape, dtype),
            in_specs=[pl.BlockSpec(memory_space=pltpu.SMEM)] + [vmem] * 7,
            out_specs=vmem,
            scratch_shapes=[
                pltpu.VMEM((channels, tall, wide), jnp.float32),
                pltpu.VMEM((state.shape[0], tall, wide), jnp.float32),
                pltpu.VMEM((state.shape[0], tall, wide), jnp.float32),
            ],
        )(*operands)

    return call(True, (rows, lanes), jnp.bfloat16), call(False, out_shape, jnp.float32)


def shifted(block, axis, dim, width):
    count = lax.axis_size(axis)
    forward = [(i, i + 1) for i in range(count - 1)]
    backward = [(target, source) for source, target in forward]
    size = block.shape[dim]
    low = lax.ppermute(lax.slice_in_dim(block, size - width, None, axis=dim), axis, forward)
    high = lax.ppermute(lax.slice_in_dim(block, 0, width, axis=dim), axis, backward)
    return low, high


def lat_factor(first_cell, count, lat_total):
    latitude = (first_cell + jnp.arange(count, dtype=jnp.int32)).astype(jnp.float32)
    return coriolis_coef * (2.0 * (latitude + 0.5) / lat_total - 1.0)


def per_device(
    atm_flux,
    remap_weights,
    tile_slots,
    need_blocks,
    send_blocks,
    ocean_state,
    land_mask,
    diffusivity,
):
    blocks_here = atm_flux.shape[1]
    block_width = atm_flux.shape[2]
    owners = lax.axis_size("ox")
    capacity = send_blocks.shape[1]
    slots = owners * capacity
    block_line = jnp.arange(blocks_here, dtype=jnp.int32)
    to_block = send_blocks[:, :, None] == block_line[None, None, :]
    outgoing = jnp.broadcast_to(atm_flux[None], (owners,) + atm_flux.shape)
    incoming = lax.all_to_all(outgoing, "ox", 0, 0, tiled=True)
    owner_of = tile_slots // capacity
    block_of = need_blocks.reshape(-1)[tile_slots]
    picks = incoming[owner_of, :, block_of, :]
    forcing = jnp.einsum("tkfa,tkra->ftr", picks, remap_weights, preferred_element_type=jnp.float32)
    fields, levels, rows, lat_cells = ocean_state.shape
    lat_total = lat_cells * lax.axis_size("oy")
    lat_start = lax.axis_index("oy") * lat_cells
    wetness = land_mask.astype(jnp.float32)
    inner = ocean_state.reshape(fields * levels, rows, lat_cells)
    aux = jnp.concatenate([forcing, wetness[None]], axis=0)
    packed = jnp.concatenate([inner, aux], axis=0)
    packed = with_layout_constraint(packed, Layout((0, 1, 2)))
    tall = -(-(rows + 2 * STEPS) // 8) * 8
    wide = -(-(lat_cells + 2 * STEPS) // 128) * 128
    low, high = shifted(packed, "ox", 1, STEPS)
    low = with_layout_constraint(low, Layout((0, 1, 2)))
    high = with_layout_constraint(high, Layout((0, 1, 2)))
    gap = jnp.zeros((packed.shape[0], tall - rows - 2 * STEPS, STEPS), jnp.float32)
    south_edge = jnp.concatenate(
        [packed[:, :, -STEPS:], high[:, :, -STEPS:], gap, low[:, :, -STEPS:]], axis=1
    )
    north_edge = jnp.concatenate(
        [packed[:, :, :STEPS], high[:, :, :STEPS], gap, low[:, :, :STEPS]], axis=1
    )
    count = lax.axis_size("oy")
    forward = [(i, i + 1) for i in range(count - 1)]
    backward = [(target, source) for source, target in forward]
    south = jnp.transpose(lax.ppermute(south_edge, "oy", forward), (2, 1, 0))
    north = jnp.transpose(lax.ppermute(north_edge, "oy", backward), (2, 1, 0))
    lane = jnp.arange(wide, dtype=jnp.int32)
    offset = jnp.where(lane < lat_cells + STEPS, lane, lane - wide)
    latitude = (lat_start + offset).astype(jnp.float32)
    coriolis_wide = (coriolis_coef * (2.0 * (latitude + 0.5) / lat_total - 1.0))[None, :]
    top, state = run_steps(inner, aux, high, low, north, south, coriolis_wide, diffusivity, ocean_state.shape)
    surface = top
    room = -(-capacity // 8) * 8
    slot_of = (tile_slots // capacity) * room + tile_slots % capacity
    slot_line = jnp.arange(owners * room, dtype=jnp.int32)
    to_slot = slot_of[None, :, :] == slot_line[:, None, None]
    spread = jnp.where(to_slot[:, :, :, None], surface[None, :, None, :], jnp.zeros((), surface.dtype))
    per_slot = jnp.einsum("stkr,tkra->sa", spread, remap_weights, preferred_element_type=jnp.float32)
    per_slot = per_slot.reshape(owners, room, block_width)
    returned = lax.all_to_all(per_slot, "ox", 0, 0, tiled=True)
    wide_send = jnp.pad(send_blocks, ((0, 0), (0, room - capacity)), constant_values=-1)
    to_room = wide_send[:, :, None] == block_line[None, None, :]
    atmos_surface = jnp.einsum(
        "isb,isa->ba", to_room.astype(jnp.float32), returned, precision=lax.Precision.HIGHEST
    )
    return (state, atmos_surface)


def solution(mesh):
    return jax.shard_map(
        per_device,
        mesh=mesh,
        in_specs=(
            P(None, "oy", "ox"),
            P("ox", "oy", None, None),
            P("ox", "oy"),
            P("ox", "oy"),
            P("ox", "oy"),
            P(None, None, "ox", "oy"),
            P("ox", "oy"),
            P(),
        ),
        out_specs=(P(None, None, "ox", "oy"), P("oy", "ox")),
        check_vma=False,
    )
```

```python
import functools

import jax
import jax.numpy as jnp
from jax import lax
from jax.experimental import pallas as pl
from jax.experimental.layout import Layout, with_layout_constraint
from jax.experimental.pallas import tpu as pltpu
from jax.sharding import PartitionSpec as P

STEPS = 3


advect_coef = 0.25
pressure_coef = 0.1
thermal_coef = 0.2
haline_coef = 0.8
coriolis_coef = 0.5
vertical_coef = 0.1
forcing_coef = 0.5


def stencil_kernel(
    diff_ref, cor_ref, state_ref, aux_ref, high_ref, low_ref, north_ref, south_ref,
    out_ref, source, first, second, surface_only,
):
    fields = 4
    channels, rows, lanes = state_ref.shape
    levels = channels // fields
    tall, wide = source.shape[1], source.shape[2]
    width = high_ref.shape[1]

    north_rows = [north_ref[s] for s in range(width)]
    south_rows = [south_ref[s] for s in range(width)]

    def assemble(ch, inner):
        source[ch, :rows, :lanes] = inner
        source[ch, rows:, :] = jnp.zeros((tall - rows, wide), jnp.float32)
        source[ch, :rows, lanes:] = jnp.zeros((rows, wide - lanes), jnp.float32)
        source[ch, rows : rows + width, :lanes] = high_ref[ch]
        source[ch, tall - width :, :lanes] = low_ref[ch]
        for s in range(width):
            source[ch, :, lanes + s : lanes + s + 1] = north_rows[s][:, ch : ch + 1]
            far = wide - width + s
            source[ch, :, far : far + 1] = south_rows[s][:, ch : ch + 1]

    if surface_only:
        for f in range(fields):
            for l in range(min(levels, STEPS + 1)):
                assemble(f * levels + l, state_ref[f * levels + l])
    else:
        for ch in range(channels):
            assemble(ch, state_ref[ch])
    for index in range(aux_ref.shape[0]):
        assemble(channels + index, aux_ref[index])

    def aux(index):
        return source[channels + index]

    def one_step(read, write, last, count):
        def crop(value):
            return value[:rows, :lanes] if last else value

        def level(l, cum):
            up = jnp.maximum(l - 1, 0)
            down = jnp.minimum(l + 1, levels - 1)
            here = [read(f * levels + l) for f in range(fields)]
            density = haline_coef * here[3] - thermal_coef * here[2]
            cum = cum + density
            pressure = cum - 0.5 * density
            zonal = crop(here[0])
            meridional = crop(here[1])
            top = jnp.where(l == 0, forcing_coef, 0.0)
            diff = diff_ref[l]
            coriolis = crop(jnp.broadcast_to(cor_ref[...], (tall, wide)))
            for f in range(fields):
                whole = here[f]
                center = crop(whole)
                east = crop(pltpu.roll(whole, tall - 1, 0))
                west = crop(pltpu.roll(whole, 1, 0))
                north = crop(pltpu.roll(whole, wide - 1, 1))
                south = crop(pltpu.roll(whole, 1, 1))
                advection = -advect_coef * 0.5 * (zonal * (east - west) + meridional * (north - south))
                laplace = diff * (east + west + north + south - 4.0 * center)
                mixing = vertical_coef * (
                    crop(read(f * levels + up)) + crop(read(f * levels + down)) - 2.0 * center
                )
                total = advection + laplace + mixing
                if f == 0:
                    grad = crop(pltpu.roll(pressure, tall - 1, 0)) - crop(pltpu.roll(pressure, 1, 0))
                    total = total + (coriolis * meridional - pressure_coef * 0.5 * grad)
                if f == 1:
                    grad = crop(pltpu.roll(pressure, wide - 1, 1)) - crop(pltpu.roll(pressure, 1, 1))
                    total = total + (-coriolis * zonal - pressure_coef * 0.5 * grad)
                total = total + top * crop(aux(f))
                write(f, l, center + crop(aux(fields)) * total)
            return cum

        lax.fori_loop(0, count, level, jnp.zeros((tall, wide), jnp.float32), unroll=True)

    def read_src(ch):
        return source[ch]

    def read_first(ch):
        return first[ch]

    def read_second(ch):
        return second[ch]

    def write_first(f, l, value):
        first[f * levels + l] = value

    def write_second(f, l, value):
        second[f * levels + l] = value

    def write_out(f, l, value):
        if not surface_only:
            out_ref[f, l] = value
        elif f == 2:
            out_ref[...] = value.astype(out_ref.dtype)

    writers = [write_first, write_second]
    for repeat in range(STEPS):
        write = write_out if repeat == STEPS - 1 else writers[repeat % 2]
        read = read_src if repeat == 0 else (read_first if repeat % 2 == 1 else read_second)
        count = min(levels, STEPS - repeat) if surface_only else levels
        one_step(read, write, repeat == STEPS - 1, count)


def run_steps(state, aux, high, low, north, south, coriolis, diffusivity, out_shape):
    channels = state.shape[0] + aux.shape[0]
    rows, lanes = state.shape[1], state.shape[2]
    width = high.shape[1]
    tall = -(-(rows + 2 * width) // 8) * 8
    wide = -(-(lanes + 2 * width) // 128) * 128
    vmem = pl.BlockSpec(memory_space=pltpu.VMEM)
    operands = (diffusivity, coriolis, state, aux, high, low, north, south)

    def call(surface_only, shape, dtype):
        return pl.pallas_call(
            functools.partial(stencil_kernel, surface_only=surface_only),
            out_shape=jax.ShapeDtypeStruct(shape, dtype),
            in_specs=[pl.BlockSpec(memory_space=pltpu.SMEM)] + [vmem] * 7,
            out_specs=vmem,
            scratch_shapes=[
                pltpu.VMEM((channels, tall, wide), jnp.float32),
                pltpu.VMEM((state.shape[0], tall, wide), jnp.float32),
                pltpu.VMEM((state.shape[0], tall, wide), jnp.float32),
            ],
        )(*operands)

    return call(True, (rows, lanes), jnp.bfloat16), call(False, out_shape, jnp.float32)


def shifted(block, axis, dim, width):
    count = lax.axis_size(axis)
    forward = [(i, i + 1) for i in range(count - 1)]
    backward = [(target, source) for source, target in forward]
    size = block.shape[dim]
    low = lax.ppermute(lax.slice_in_dim(block, size - width, None, axis=dim), axis, forward)
    high = lax.ppermute(lax.slice_in_dim(block, 0, width, axis=dim), axis, backward)
    return low, high


def lat_factor(first_cell, count, lat_total):
    latitude = (first_cell + jnp.arange(count, dtype=jnp.int32)).astype(jnp.float32)
    return coriolis_coef * (2.0 * (latitude + 0.5) / lat_total - 1.0)


def per_device(
    atm_flux,
    remap_weights,
    tile_slots,
    need_blocks,
    send_blocks,
    ocean_state,
    land_mask,
    diffusivity,
):
    blocks_here = atm_flux.shape[1]
    block_width = atm_flux.shape[2]
    owners = lax.axis_size("ox")
    capacity = send_blocks.shape[1]
    slots = owners * capacity
    block_line = jnp.arange(blocks_here, dtype=jnp.int32)
    to_block = send_blocks[:, :, None] == block_line[None, None, :]
    outgoing = jnp.broadcast_to(atm_flux[None], (owners,) + atm_flux.shape)
    incoming = lax.all_to_all(outgoing, "ox", 0, 0, tiled=True)
    owner_of = tile_slots // capacity
    block_of = need_blocks.reshape(-1)[tile_slots]
    picks = incoming[owner_of, :, block_of, :]
    forcing = jnp.einsum("tkfa,tkra->ftr", picks, remap_weights, preferred_element_type=jnp.float32)
    fields, levels, rows, lat_cells = ocean_state.shape
    lat_total = lat_cells * lax.axis_size("oy")
    lat_start = lax.axis_index("oy") * lat_cells
    wetness = land_mask.astype(jnp.float32)
    inner = ocean_state.reshape(fields * levels, rows, lat_cells)
    aux = jnp.concatenate([forcing, wetness[None]], axis=0)
    packed = jnp.concatenate([inner, aux], axis=0)
    packed = with_layout_constraint(packed, Layout((0, 1, 2)))
    tall = -(-(rows + 2 * STEPS) // 8) * 8
    wide = -(-(lat_cells + 2 * STEPS) // 128) * 128
    low, high = shifted(packed, "ox", 1, STEPS)
    low = with_layout_constraint(low, Layout((0, 1, 2)))
    high = with_layout_constraint(high, Layout((0, 1, 2)))
    aux, high, low = lax.optimization_barrier((aux, high, low))
    gap = jnp.zeros((packed.shape[0], tall - rows - 2 * STEPS, STEPS), jnp.float32)
    south_edge = jnp.concatenate(
        [packed[:, :, -STEPS:], high[:, :, -STEPS:], gap, low[:, :, -STEPS:]], axis=1
    )
    north_edge = jnp.concatenate(
        [packed[:, :, :STEPS], high[:, :, :STEPS], gap, low[:, :, :STEPS]], axis=1
    )
    count = lax.axis_size("oy")
    forward = [(i, i + 1) for i in range(count - 1)]
    backward = [(target, source) for source, target in forward]
    south = jnp.transpose(lax.ppermute(south_edge, "oy", forward), (2, 1, 0))
    north = jnp.transpose(lax.ppermute(north_edge, "oy", backward), (2, 1, 0))
    lane = jnp.arange(wide, dtype=jnp.int32)
    offset = jnp.where(lane < lat_cells + STEPS, lane, lane - wide)
    latitude = (lat_start + offset).astype(jnp.float32)
    coriolis_wide = (coriolis_coef * (2.0 * (latitude + 0.5) / lat_total - 1.0))[None, :]
    top, state = run_steps(inner, aux, high, low, north, south, coriolis_wide, diffusivity, ocean_state.shape)
    surface = top
    pieces = jnp.einsum("tkra,tr->tka", remap_weights, surface, preferred_element_type=jnp.float32)
    slot_line = jnp.arange(slots, dtype=jnp.int32)
    to_slot = (tile_slots[:, :, None] == slot_line[None, None, :]).astype(jnp.float32)
    per_slot = jnp.einsum("tks,tka->sa", to_slot, pieces, precision=lax.Precision.HIGHEST)
    per_slot = per_slot.reshape(owners, capacity, block_width)
    returned = lax.all_to_all(per_slot, "ox", 0, 0, tiled=True)
    atmos_surface = jnp.einsum(
        "isb,isa->ba", to_block.astype(jnp.float32), returned, precision=lax.Precision.HIGHEST
    )
    return (state, atmos_surface)


def solution(mesh):
    return jax.shard_map(
        per_device,
        mesh=mesh,
        in_specs=(
            P(None, "oy", "ox"),
            P("ox", "oy", None, None),
            P("ox", "oy"),
            P("ox", "oy"),
            P("ox", "oy"),
            P(None, None, "ox", "oy"),
            P("ox", "oy"),
            P(),
        ),
        out_specs=(P(None, None, "ox", "oy"), P("oy", "ox")),
        check_vma=False,
    )
```

```python
import functools

import jax
import jax.numpy as jnp
from jax import lax
from jax.experimental import pallas as pl
from jax.experimental.layout import Layout, with_layout_constraint
from jax.experimental.pallas import tpu as pltpu
from jax.sharding import PartitionSpec as P

STEPS = 3


advect_coef = 0.25
pressure_coef = 0.1
thermal_coef = 0.2
haline_coef = 0.8
coriolis_coef = 0.5
vertical_coef = 0.1
forcing_coef = 0.5


def stencil_kernel(
    diff_ref, cor_ref, state_ref, aux_ref, high_ref, low_ref, north_ref, south_ref,
    out_ref, source, first, second, surface_only,
):
    fields = 4
    channels, rows, lanes = state_ref.shape
    levels = channels // fields
    tall, wide = source.shape[1], source.shape[2]
    width = high_ref.shape[1]

    north_rows = [north_ref[s] for s in range(width)]
    south_rows = [south_ref[s] for s in range(width)]

    def assemble(ch, inner):
        source[ch, :rows, :lanes] = inner
        source[ch, rows:, :] = jnp.zeros((tall - rows, wide), jnp.float32)
        source[ch, :rows, lanes:] = jnp.zeros((rows, wide - lanes), jnp.float32)
        source[ch, rows : rows + width, :lanes] = high_ref[ch]
        source[ch, tall - width :, :lanes] = low_ref[ch]
        for s in range(width):
            source[ch, :, lanes + s : lanes + s + 1] = north_rows[s][:, ch : ch + 1]
            far = wide - width + s
            source[ch, :, far : far + 1] = south_rows[s][:, ch : ch + 1]

    if surface_only:
        for f in range(fields):
            for l in range(min(levels, STEPS + 1)):
                assemble(f * levels + l, state_ref[f * levels + l])
    else:
        for ch in range(channels):
            assemble(ch, state_ref[ch])
    for index in range(aux_ref.shape[0]):
        assemble(channels + index, aux_ref[index])

    def aux(index):
        return source[channels + index]

    def one_step(read, write, last, count):
        def crop(value):
            return value[:rows, :lanes] if last else value

        def level(l, cum):
            up = jnp.maximum(l - 1, 0)
            down = jnp.minimum(l + 1, levels - 1)
            here = [read(f * levels + l) for f in range(fields)]
            density = haline_coef * here[3] - thermal_coef * here[2]
            cum = cum + density
            pressure = cum - 0.5 * density
            zonal = crop(here[0])
            meridional = crop(here[1])
            top = jnp.where(l == 0, forcing_coef, 0.0)
            diff = diff_ref[l]
            coriolis = crop(jnp.broadcast_to(cor_ref[...], (tall, wide)))
            for f in range(fields):
                whole = here[f]
                center = crop(whole)
                east = crop(pltpu.roll(whole, tall - 1, 0))
                west = crop(pltpu.roll(whole, 1, 0))
                north = crop(pltpu.roll(whole, wide - 1, 1))
                south = crop(pltpu.roll(whole, 1, 1))
                advection = -advect_coef * 0.5 * (zonal * (east - west) + meridional * (north - south))
                laplace = diff * (east + west + north + south - 4.0 * center)
                mixing = vertical_coef * (
                    crop(read(f * levels + up)) + crop(read(f * levels + down)) - 2.0 * center
                )
                total = advection + laplace + mixing
                if f == 0:
                    grad = crop(pltpu.roll(pressure, tall - 1, 0)) - crop(pltpu.roll(pressure, 1, 0))
                    total = total + (coriolis * meridional - pressure_coef * 0.5 * grad)
                if f == 1:
                    grad = crop(pltpu.roll(pressure, wide - 1, 1)) - crop(pltpu.roll(pressure, 1, 1))
                    total = total + (-coriolis * zonal - pressure_coef * 0.5 * grad)
                total = total + top * crop(aux(f))
                write(f, l, center + crop(aux(fields)) * total)
            return cum

        lax.fori_loop(0, count, level, jnp.zeros((tall, wide), jnp.float32), unroll=True)

    def read_src(ch):
        return source[ch]

    def read_first(ch):
        return first[ch]

    def read_second(ch):
        return second[ch]

    def write_first(f, l, value):
        first[f * levels + l] = value

    def write_second(f, l, value):
        second[f * levels + l] = value

    def write_out(f, l, value):
        if not surface_only:
            out_ref[f, l] = value
        elif f == 2:
            out_ref[...] = value.astype(out_ref.dtype)

    writers = [write_first, write_second]
    for repeat in range(STEPS):
        write = write_out if repeat == STEPS - 1 else writers[repeat % 2]
        read = read_src if repeat == 0 else (read_first if repeat % 2 == 1 else read_second)
        count = min(levels, STEPS - repeat) if surface_only else levels
        one_step(read, write, repeat == STEPS - 1, count)


def run_steps(state, aux, high, low, north, south, coriolis, diffusivity, out_shape):
    channels = state.shape[0] + aux.shape[0]
    rows, lanes = state.shape[1], state.shape[2]
    width = high.shape[1]
    tall = -(-(rows + 2 * width) // 8) * 8
    wide = -(-(lanes + 2 * width) // 128) * 128
    vmem = pl.BlockSpec(memory_space=pltpu.VMEM)
    operands = (diffusivity, coriolis, state, aux, high, low, north, south)

    def call(surface_only, shape, dtype):
        return pl.pallas_call(
            functools.partial(stencil_kernel, surface_only=surface_only),
            out_shape=jax.ShapeDtypeStruct(shape, dtype),
            in_specs=[pl.BlockSpec(memory_space=pltpu.SMEM)] + [vmem] * 7,
            out_specs=vmem,
            scratch_shapes=[
                pltpu.VMEM((channels, tall, wide), jnp.float32),
                pltpu.VMEM((state.shape[0], tall, wide), jnp.float32),
                pltpu.VMEM((state.shape[0], tall, wide), jnp.float32),
            ],
        )(*operands)

    return call(True, (rows, lanes), jnp.bfloat16), call(False, out_shape, jnp.float32)


def shifted(block, axis, dim, width):
    count = lax.axis_size(axis)
    forward = [(i, i + 1) for i in range(count - 1)]
    backward = [(target, source) for source, target in forward]
    size = block.shape[dim]
    low = lax.ppermute(lax.slice_in_dim(block, size - width, None, axis=dim), axis, forward)
    high = lax.ppermute(lax.slice_in_dim(block, 0, width, axis=dim), axis, backward)
    return low, high


def lat_factor(first_cell, count, lat_total):
    latitude = (first_cell + jnp.arange(count, dtype=jnp.int32)).astype(jnp.float32)
    return coriolis_coef * (2.0 * (latitude + 0.5) / lat_total - 1.0)


def per_device(
    atm_flux,
    remap_weights,
    tile_slots,
    need_blocks,
    send_blocks,
    ocean_state,
    land_mask,
    diffusivity,
):
    blocks_here = atm_flux.shape[1]
    block_width = atm_flux.shape[2]
    owners = lax.axis_size("ox")
    capacity = send_blocks.shape[1]
    slots = owners * capacity
    block_line = jnp.arange(blocks_here, dtype=jnp.int32)
    to_block = send_blocks[:, :, None] == block_line[None, None, :]
    outgoing = jnp.broadcast_to(atm_flux[None], (owners,) + atm_flux.shape)
    incoming = lax.all_to_all(outgoing, "ox", 0, 0, tiled=True)
    owner_of = tile_slots // capacity
    block_of = need_blocks.reshape(-1)[tile_slots]
    owner_line = jnp.arange(owners, dtype=jnp.int32)
    choose = (owner_of[:, :, None, None] == owner_line[None, None, :, None]) & (
        block_of[:, :, None, None] == block_line[None, None, None, :]
    )
    picks = jnp.einsum(
        "tkqb,qfba->tkfa", choose.astype(incoming.dtype), incoming, preferred_element_type=jnp.float32
    ).astype(incoming.dtype)
    forcing = jnp.einsum("tkfa,tkra->ftr", picks, remap_weights, preferred_element_type=jnp.float32)
    fields, levels, rows, lat_cells = ocean_state.shape
    lat_total = lat_cells * lax.axis_size("oy")
    lat_start = lax.axis_index("oy") * lat_cells
    wetness = land_mask.astype(jnp.float32)
    inner = ocean_state.reshape(fields * levels, rows, lat_cells)
    aux = jnp.concatenate([forcing, wetness[None]], axis=0)
    packed = jnp.concatenate([inner, aux], axis=0)
    packed = with_layout_constraint(packed, Layout((0, 1, 2)))
    tall = -(-(rows + 2 * STEPS) // 8) * 8
    wide = -(-(lat_cells + 2 * STEPS) // 128) * 128
    low, high = shifted(packed, "ox", 1, STEPS)
    low = with_layout_constraint(low, Layout((0, 1, 2)))
    high = with_layout_constraint(high, Layout((0, 1, 2)))
    aux, high, low = lax.optimization_barrier((aux, high, low))
    gap = jnp.zeros((packed.shape[0], tall - rows - 2 * STEPS, STEPS), jnp.float32)
    south_edge = jnp.concatenate(
        [packed[:, :, -STEPS:], high[:, :, -STEPS:], gap, low[:, :, -STEPS:]], axis=1
    )
    north_edge = jnp.concatenate(
        [packed[:, :, :STEPS], high[:, :, :STEPS], gap, low[:, :, :STEPS]], axis=1
    )
    count = lax.axis_size("oy")
    forward = [(i, i + 1) for i in range(count - 1)]
    backward = [(target, source) for source, target in forward]
    south = jnp.transpose(lax.ppermute(south_edge, "oy", forward), (2, 1, 0))
    north = jnp.transpose(lax.ppermute(north_edge, "oy", backward), (2, 1, 0))
    lane = jnp.arange(wide, dtype=jnp.int32)
    offset = jnp.where(lane < lat_cells + STEPS, lane, lane - wide)
    latitude = (lat_start + offset).astype(jnp.float32)
    coriolis_wide = (coriolis_coef * (2.0 * (latitude + 0.5) / lat_total - 1.0))[None, :]
    top, state = run_steps(inner, aux, high, low, north, south, coriolis_wide, diffusivity, ocean_state.shape)
    surface = top
    pieces = jnp.einsum("tkra,tr->tka", remap_weights, surface, preferred_element_type=jnp.float32)
    slot_line = jnp.arange(slots, dtype=jnp.int32)
    to_slot = (tile_slots[:, :, None] == slot_line[None, None, :]).astype(jnp.float32)
    per_slot = jnp.einsum("tks,tka->sa", to_slot, pieces, precision=lax.Precision.HIGHEST)
    per_slot = per_slot.reshape(owners, capacity, block_width)
    returned = lax.all_to_all(per_slot, "ox", 0, 0, tiled=True)
    atmos_surface = jnp.einsum(
        "isb,isa->ba", to_block.astype(jnp.float32), returned, precision=lax.Precision.HIGHEST
    )
    return (state, atmos_surface)


def solution(mesh):
    return jax.shard_map(
        per_device,
        mesh=mesh,
        in_specs=(
            P(None, "oy", "ox"),
            P("ox", "oy", None, None),
            P("ox", "oy"),
            P("ox", "oy"),
            P("ox", "oy"),
            P(None, None, "ox", "oy"),
            P("ox", "oy"),
            P(),
        ),
        out_specs=(P(None, None, "ox", "oy"), P("oy", "ox")),
        check_vma=False,
    )
```
